128 devices in a mesh: pipe: 4 (over x_hi, core), dp: 16 (over y, z), tensor: 2 (over x_lo).
Axes of the slice: x: 4 (x_hi: 2, x_lo: 2; x = x_hi * 2 + x_lo), y: 4, z: 4, core: 2. Of those that a mesh axis runs over, the one named last changes fastest.
Arguments:
- hidden_states: bfloat16 [4, 4096, 8192], P('pipe', 'dp'), may hold values from -60 to 60
- norm_gain: bfloat16 [4, 8192], P('pipe'), may hold values from 0.5 to 2
- key_weight: bfloat16 [4, 8192, 512], P('pipe', 'dp', 'tensor'), may hold values from -0.0625 to 0.0625
- value_weight: bfloat16 [4, 8192, 512], P('pipe', 'dp', 'tensor'), may hold values from -0.0625 to 0.0625
- queries: bfloat16 [4, 4096, 4096], P('pipe', 'dp', 'tensor'), may hold values from -128 to 128
- context_cotangent: bfloat16 [4, 4096, 4096], P('pipe', 'dp', 'tensor'), may hold values from -96 to 96
- lengths: int32 [4, 16], P('pipe', 'dp'), may hold values from 64 to 256, as said below
- policy_logp: float32 [4, 16], P('pipe', 'dp'), may hold values from -90 to -30
- reference_logp: float32 [4, 16], P('pipe', 'dp'), may hold values from -90 to -30
Outputs:
- key_weight_grad: bfloat16 [4, 8192, 512], P('pipe', 'dp', 'tensor')
- value_weight_grad: bfloat16 [4, 8192, 512], P('pipe', 'dp', 'tensor')
- lower_cotangent: bfloat16 [4, 4096, 8192], P('pipe', 'dp')
The draws below stay inside these ranges and needn't reach their ends.
Inputs may be any that keep to these rules, and one draw needn't show every extreme that they name: `lengths`: each sequence's live tokens; positions at or beyond it are padding.
All inputs are finite; a program needn't handle non-finite values.
Results may differ from the reference program's by a relative error of at most 0.015.
The reference program's roundings to bfloat16 on the way count: a program that leaves them out, or rounds other values in their place, can miss the bound.
Values may be sent and summed in bfloat16 or wider, within the bound.
No kernel may reach another device: no remote copies, remote signals or barrier semaphores. Data moves between devices by JAX's collectives and lax.ppermute only.
A program may use at most 128 MiB of HBM per device.

```python
import math
import jax
import jax.numpy as jnp
from jax import lax

D = 8192
HD = 128
HQ = 32
KVH = 4
LEN = 256
TOK_DEV = 256
SEQS = 16
TOKENS = 4096
N_PIPE = 4
N_DP = 16
N_TENSOR = 2


def draw_hidden_states(key, part):
    key_base = jax.random.fold_in(key, 11)
    key_rows = jax.random.fold_in(key, 12)
    key_cols = jax.random.fold_in(key, 13)
    shape = (N_PIPE, TOKENS, D)
    row_scale = jnp.exp(jax.random.uniform(key_rows, (N_PIPE, TOKENS, 1), jnp.float32, jnp.log(0.1), 0.0))
    col_scale = jnp.exp(jax.random.uniform(key_cols, (1, 1, D), jnp.float32, 0.0, jnp.log(10.0)))
    base = jnp.clip(jax.random.normal(key_base, shape, jnp.float32), -6.0, 6.0)
    return (base * row_scale * col_scale).astype(jnp.bfloat16)


def draw_queries(key, part):
    key_base = jax.random.fold_in(key, 21)
    shape = (N_PIPE, TOKENS, HQ * HD)
    return jnp.clip(jax.random.normal(key_base, shape, jnp.float32), -4.0, 4.0).astype(jnp.bfloat16)


def draw_lengths(key, part):
    key_vals = jax.random.fold_in(key, 31)
    key_spot = jax.random.fold_in(key, 32)
    count = N_PIPE * SEQS
    drawn = jax.random.randint(key_vals, (count,), LEN // 4, LEN + 1, jnp.int32)
    spot = jax.random.randint(key_spot, (), 0, count, jnp.int32)
    place = jnp.arange(count, dtype=jnp.int32)
    drawn = jnp.where(place == spot, LEN, drawn)
    drawn = jnp.where(place == (spot + 1) % count, LEN // 4, drawn)
    return drawn.reshape(N_PIPE, SEQS)


def shard_levels(own_key, dims, split, least, top_value):
    factor_of, own = 1.0, jax.random.fold_in(own_key, 6)
    for axis_at, parts in split:
        heights = jnp.exp(jax.random.uniform(jax.random.fold_in(own, axis_at), (parts,), jnp.float32, least / len(split), top_value / len(split)))
        factor_of = factor_of * jnp.repeat(heights, dims[axis_at] // parts).reshape([-1 if axis == axis_at else 1 for axis in range(len(dims))])
    return factor_of


def scatter_about(own_key, shape, spread, most, cuts=(), held_as=jnp.bfloat16):
    entries = spread * jax.random.normal(own_key, shape, jnp.float32)
    if cuts:
        entries = entries * shard_levels(own_key, shape, cuts, -0.22, 0.18)
    return jnp.clip(entries, -most, most).astype(held_as)


def setup_inputs(seed: int = 0) -> dict:
    key_list = jax.random.split(jax.random.key(seed), 10)
    return {
        "hidden_states": draw_hidden_states(jax.random.fold_in(key_list[9], 71), 0),
        "norm_gain": jnp.clip(jnp.exp(math.log(2.0) - 1.3862944 * jax.random.uniform(key_list[1], (N_PIPE, D), jnp.float32) ** shard_levels(key_list[1], (N_PIPE, D), ((0, 4),), -0.2, 0.2)), 0.5, 2.0).astype(jnp.bfloat16),
        "key_weight": scatter_about(key_list[2], (N_PIPE, D, KVH * HD), D ** -0.5, 0.0625, ((0, 4), (1, 16), (2, 2))),
        "value_weight": scatter_about(key_list[3], (N_PIPE, D, KVH * HD), D ** -0.5, 0.0625, ((0, 4), (1, 16), (2, 2))),
        "queries": draw_queries(jax.random.fold_in(key_list[9], 71), 0),
        "context_cotangent": scatter_about(key_list[5], (N_PIPE, TOKENS, HQ * HD), 16.0, 96.0, ((0, 4), (1, 16), (2, 2))),
        "lengths": draw_lengths(jax.random.fold_in(key_list[9], 71), 0),
        "policy_logp": jnp.clip(-90.0 + 60.0 * jax.random.uniform(key_list[7], (N_PIPE, SEQS), jnp.float32) ** shard_levels(key_list[7], (N_PIPE, SEQS), ((0, 4), (1, 16)), -0.2, 0.2), -90.0, -30.0),
        "reference_logp": jnp.clip(-90.0 + 60.0 * jax.random.uniform(key_list[8], (N_PIPE, SEQS), jnp.float32) ** shard_levels(key_list[8], (N_PIPE, SEQS), ((0, 4), (1, 16)), -0.2, 0.2), -90.0, -30.0),
    }


npo_beta = 0.1
norm_eps = 1e-05
rope_base = 500000.0

def rope_tables(length, head_dim):
    positions = jnp.arange(length).astype(jnp.float32)
    freq_index = jnp.arange(head_dim // 2).astype(jnp.float32)
    inverse = 1.0 / rope_base ** (2.0 * freq_index / head_dim)
    angles = positions[:, None] * inverse[None, :]
    cosine = jnp.concatenate([jnp.cos(angles), jnp.cos(angles)], axis=1)
    sine = jnp.concatenate([jnp.sin(angles), jnp.sin(angles)], axis=1)
    return (cosine, sine)

def rotate_half(values):
    half = values.shape[-1] // 2
    return jnp.concatenate([-values[..., half:], values[..., :half]], axis=-1)

def rotate_back(values):
    half = values.shape[-1] // 2
    return jnp.concatenate([values[..., half:], -values[..., :half]], axis=-1)

def sequence_grads(query_seq, key_seq, value_seq, cotan_seq, length_seq, cosine, sine):
    seq_len, kv_heads, head_dim = key_seq.shape
    group = query_seq.shape[1] // kv_heads
    scale = 1.0 / math.sqrt(head_dim)
    query_f = query_seq.reshape(seq_len, kv_heads, group, head_dim).astype(jnp.float32)
    cotan_f = cotan_seq.reshape(seq_len, kv_heads, group, head_dim).astype(jnp.float32)
    key_f = key_seq.astype(jnp.float32)
    value_f = value_seq.astype(jnp.float32)
    scores = jnp.einsum('ikgd,jkd->kgij', query_f, key_f) * scale
    row_pos = jnp.arange(seq_len)[:, None]
    col_pos = jnp.arange(seq_len)[None, :]
    allowed = (col_pos <= row_pos) & (col_pos < length_seq)
    scores = jnp.where(allowed, scores, -1e+30)
    highest = lax.optimization_barrier(jnp.max(scores, axis=-1, keepdims=True))
    expd = jnp.where(allowed, jnp.exp(scores - highest), 0.0)
    probs = expd / lax.optimization_barrier(jnp.sum(expd, axis=-1, keepdims=True))
    probs_low = probs.astype(jnp.bfloat16)
    value_grad = jnp.einsum('kgij,ikgd->jkd', probs_low.astype(jnp.float32), cotan_f).astype(jnp.bfloat16)
    prob_grad = jnp.einsum('ikgd,jkd->kgij', cotan_f, value_f)
    centre = lax.optimization_barrier(jnp.sum(probs * prob_grad, axis=-1, keepdims=True))
    score_grad = (probs * (prob_grad - centre) * scale).astype(jnp.bfloat16)
    rotated_grad = jnp.einsum('kgij,ikgd->jkd', score_grad.astype(jnp.float32), query_f)
    key_grad = rotated_grad * cosine[:, None, :] + rotate_back(rotated_grad * sine[:, None, :])
    return (key_grad.astype(jnp.bfloat16), value_grad)

def section_backward(hidden, gain, key_w, value_w, query_all, cotan, lens, logp, logp_ref):
    hidden_f = hidden.astype(jnp.float32)
    inv_rms = lax.rsqrt(lax.optimization_barrier(jnp.mean(hidden_f * hidden_f, axis=-1, keepdims=True)) + norm_eps)
    nhat = hidden_f * inv_rms
    gain_f = gain.astype(jnp.float32)
    normed = (nhat * gain_f).astype(jnp.bfloat16)
    key_raw = jnp.dot(normed, key_w, preferred_element_type=jnp.float32)
    values = jnp.dot(normed, value_w, preferred_element_type=jnp.float32).astype(jnp.bfloat16)
    cosine, sine = rope_tables(LEN, HD)
    key_four = key_raw.reshape(SEQS, LEN, KVH, HD)
    keys = (key_four * cosine[None, :, None, :] + rotate_half(key_four) * sine[None, :, None, :]).astype(jnp.bfloat16)
    seq_weight = 2.0 * jax.nn.sigmoid(npo_beta * (logp - logp_ref)) / SEQS
    live = jnp.arange(LEN)[None, :] < lens[:, None]
    factor = jnp.where(live, seq_weight[:, None], 0.0)
    scaled = (cotan.reshape(SEQS, LEN, HQ, HD).astype(jnp.float32) * factor[:, :, None, None]).astype(jnp.bfloat16)

    def one_sequence(items):
        return sequence_grads(items[0], items[1], items[2], items[3], items[4], cosine, sine)
    key_grad, value_grad = lax.map(one_sequence, (query_all.reshape(SEQS, LEN, HQ, HD), keys, values.reshape(SEQS, LEN, KVH, HD), scaled, lens))
    key_grad = key_grad.reshape(TOKENS, KVH * HD)
    value_grad = value_grad.reshape(TOKENS, KVH * HD)
    combined = jnp.concatenate([key_grad, value_grad], axis=1)

    def add_partial(total, pieces):
        partial_sum = lax.dot_general(pieces[0], pieces[1], (((0,), (0,)), ((), ())), preferred_element_type=jnp.float32)
        rounded = lax.optimization_barrier(partial_sum.astype(jnp.bfloat16))
        return (total + rounded.astype(jnp.float32), None)
    grad_total, unused = lax.scan(add_partial, jnp.zeros((D, 2 * KVH * HD), jnp.float32), (normed.reshape(N_DP, TOK_DEV, D), combined.reshape(N_DP, TOK_DEV, 2 * KVH * HD)))
    grad_low = grad_total.astype(jnp.bfloat16)
    width = KVH * HD // N_TENSOR
    normed_grad = jnp.zeros((TOKENS, D), jnp.float32)
    for member in range(N_TENSOR):
        lo_col = member * width
        part = lax.dot_general(key_grad[:, lo_col:lo_col + width], key_w[:, lo_col:lo_col + width], (((1,), (1,)), ((), ())), preferred_element_type=jnp.float32)
        part = part + lax.dot_general(value_grad[:, lo_col:lo_col + width], value_w[:, lo_col:lo_col + width], (((1,), (1,)), ((), ())), preferred_element_type=jnp.float32)
        normed_grad = normed_grad + lax.optimization_barrier(part.astype(jnp.bfloat16)).astype(jnp.float32)
    gain_grad_in = normed_grad * gain_f
    centre = lax.optimization_barrier(jnp.mean(gain_grad_in * nhat, axis=-1, keepdims=True))
    section_cot = ((gain_grad_in - nhat * centre) * inv_rms).astype(jnp.bfloat16)
    return (grad_low[:, :KVH * HD], grad_low[:, KVH * HD:], section_cot)

def reference(hidden_states, norm_gain, key_weight, value_weight, queries, context_cotangent, lengths, policy_logp, reference_logp):
    key_grads = []
    value_grads = []
    section_cots = []
    for section in range(N_PIPE):
        key_part, value_part, section_cot = section_backward(hidden_states[section], norm_gain[section], key_weight[section], value_weight[section], queries[section], context_cotangent[section], lengths[section], policy_logp[section], reference_logp[section])
        key_grads.append(key_part)
        value_grads.append(value_part)
        section_cots.append(section_cot)
    section_cots.append(jnp.zeros((TOKENS, D), jnp.bfloat16))
    lower = jnp.stack(section_cots[1:], axis=0)
    return (jnp.stack(key_grads, axis=0), jnp.stack(value_grads, axis=0), lower)
```

```python
import math

import jax
import jax.numpy as jnp
from jax import lax
from jax.sharding import PartitionSpec as P

HD = 128


npo_beta = 0.1
norm_eps = 1e-05
rope_base = 500000.0


def shifted(value, axis, steps):
    count = lax.axis_size(axis)
    leading, last = (max(0, -steps), min(count, count - steps))
    return lax.ppermute(value, axis, [(source, source + steps) for source in range(leading, last)])


def rope_tables(length, head_dim):
    positions = jnp.arange(length).astype(jnp.float32)
    freq_index = jnp.arange(head_dim // 2).astype(jnp.float32)
    inverse = 1.0 / rope_base ** (2.0 * freq_index / head_dim)
    angles = positions[:, None] * inverse[None, :]
    cosine = jnp.concatenate([jnp.cos(angles), jnp.cos(angles)], axis=1)
    sine = jnp.concatenate([jnp.sin(angles), jnp.sin(angles)], axis=1)
    return (cosine, sine)


def rotate_half(values):
    half = values.shape[-1] // 2
    return jnp.concatenate([-values[..., half:], values[..., :half]], axis=-1)


def rotate_back(values):
    half = values.shape[-1] // 2
    return jnp.concatenate([values[..., half:], -values[..., :half]], axis=-1)


def sequence_grads(query_seq, key_seq, value_seq, cotan_seq, length_seq, cosine, sine):
    seq_len, kv_heads, head_dim = key_seq.shape
    group = query_seq.shape[1] // kv_heads
    scale = 1.0 / math.sqrt(head_dim)
    query_g = query_seq.reshape(seq_len, kv_heads, group, head_dim)
    cotan_g = cotan_seq.reshape(seq_len, kv_heads, group, head_dim)
    scores = (
        jnp.einsum("ikgd,jkd->kgij", query_g, key_seq, preferred_element_type=jnp.float32) * scale
    )
    row_pos = jnp.arange(seq_len)[:, None]
    col_pos = jnp.arange(seq_len)[None, :]
    allowed = (col_pos <= row_pos) & (col_pos < length_seq)
    scores = jnp.where(allowed, scores, -1e30)
    highest = jnp.max(scores, axis=-1, keepdims=True)
    expd = jnp.where(allowed, jnp.exp(scores - highest), 0.0)
    probs = expd / jnp.sum(expd, axis=-1, keepdims=True)
    probs_low = probs.astype(jnp.bfloat16)
    value_grad = jnp.einsum(
        "kgij,ikgd->jkd", probs_low, cotan_g, preferred_element_type=jnp.float32
    ).astype(jnp.bfloat16)
    prob_grad = jnp.einsum("ikgd,jkd->kgij", cotan_g, value_seq, preferred_element_type=jnp.float32)
    centre = jnp.sum(probs * prob_grad, axis=-1, keepdims=True)
    score_grad = (probs * (prob_grad - centre) * scale).astype(jnp.bfloat16)
    rotated_grad = jnp.einsum(
        "kgij,ikgd->jkd", score_grad, query_g, preferred_element_type=jnp.float32
    )
    key_grad = rotated_grad * cosine[:, None, :] + rotate_back(rotated_grad * sine[:, None, :])
    return (key_grad.astype(jnp.bfloat16), value_grad)


def norm_backward(normed_grad, gain_f, nhat, inv_rms):
    gain_grad_in = normed_grad * gain_f
    centre = jnp.mean(gain_grad_in * nhat, axis=-1, keepdims=True)
    return ((gain_grad_in - nhat * centre) * inv_rms).astype(jnp.bfloat16)


def on_device(
    hidden_states,
    norm_gain,
    key_weight,
    value_weight,
    queries,
    context_cotangent,
    lengths,
    policy_logp,
    reference_logp,
):
    both_full = lax.all_gather(
        jnp.stack([key_weight[0], value_weight[0]]), "dp", axis=1, tiled=True
    )
    key_full, value_full = both_full[0], both_full[1]
    hidden = hidden_states[0]
    gain_f = norm_gain[0].astype(jnp.float32)
    tok_rows = hidden.shape[0]
    seq_count = lengths.shape[1]
    seq_len = tok_rows // seq_count
    kv_cols = key_full.shape[1]
    kv_local = kv_cols // HD
    q_local = queries.shape[2] // HD
    hidden_f = hidden.astype(jnp.float32)
    inv_rms = lax.rsqrt(jnp.mean(hidden_f * hidden_f, axis=-1, keepdims=True) + norm_eps)
    nhat = hidden_f * inv_rms
    normed = (nhat * gain_f).astype(jnp.bfloat16)
    key_raw = jnp.dot(normed, key_full, preferred_element_type=jnp.float32)
    values = jnp.dot(normed, value_full, preferred_element_type=jnp.float32).astype(jnp.bfloat16)
    cosine, sine = rope_tables(seq_len, HD)
    key_four = key_raw.reshape(seq_count, seq_len, kv_local, HD)
    keys = (
        key_four * cosine[None, :, None, :] + rotate_half(key_four) * sine[None, :, None, :]
    ).astype(jnp.bfloat16)
    total_seqs = seq_count * lax.axis_size("dp")
    seq_weight = 2.0 * jax.nn.sigmoid(npo_beta * (policy_logp[0] - reference_logp[0])) / total_seqs
    live = jnp.arange(seq_len)[None, :] < lengths[0][:, None]
    factor = jnp.where(live, seq_weight[:, None], 0.0)
    scaled = (
        context_cotangent[0].reshape(seq_count, seq_len, q_local, HD).astype(jnp.float32)
        * factor[:, :, None, None]
    ).astype(jnp.bfloat16)

    def one_sequence(items):
        return sequence_grads(items[0], items[1], items[2], items[3], items[4], cosine, sine)

    key_grad, value_grad = lax.map(
        one_sequence,
        (
            queries[0].reshape(seq_count, seq_len, q_local, HD),
            keys,
            values.reshape(seq_count, seq_len, kv_local, HD),
            scaled,
            lengths[0],
        ),
    )
    key_grad = key_grad.reshape(tok_rows, kv_cols)
    value_grad = value_grad.reshape(tok_rows, kv_cols)
    combined = jnp.concatenate([key_grad, value_grad], axis=1)
    grad_total = lax.psum_scatter(
        lax.dot_general(
            normed, combined, (((0,), (0,)), ((), ())), preferred_element_type=jnp.float32
        ).astype(jnp.bfloat16),
        "dp",
        scatter_dimension=0,
        tiled=True,
    )
    part = lax.dot_general(
        key_grad, key_full, (((1,), (1,)), ((), ())), preferred_element_type=jnp.float32
    )
    part = part + lax.dot_general(
        value_grad, value_full, (((1,), (1,)), ((), ())), preferred_element_type=jnp.float32
    )
    part_low = part.astype(jnp.bfloat16)
    count = lax.axis_size("tensor")
    normed_grad = part_low.astype(jnp.float32)
    for step in range(1, count):
        pairs = [(source, (source + step) % count) for source in range(count)]
        normed_grad = normed_grad + lax.ppermute(part_low, "tensor", pairs).astype(jnp.float32)
    section_cot = norm_backward(normed_grad, gain_f, nhat, inv_rms)
    lower = shifted(section_cot, "pipe", -1)
    return (grad_total[:, :kv_cols][None], grad_total[:, kv_cols:][None], lower[None])


def solution(mesh):
    in_specs = (
        P("pipe", "dp", None),
        P("pipe", None),
        P("pipe", "dp", "tensor"),
        P("pipe", "dp", "tensor"),
        P("pipe", "dp", "tensor"),
        P("pipe", "dp", "tensor"),
        P("pipe", "dp"),
        P("pipe", "dp"),
        P("pipe", "dp"),
    )
    out_specs = (P("pipe", "dp", "tensor"), P("pipe", "dp", "tensor"), P("pipe", "dp", None))
    return jax.shard_map(
        on_device, mesh=mesh, in_specs=in_specs, out_specs=out_specs, check_vma=False
    )
```

```python
import math

import jax
import jax.numpy as jnp
from jax import lax
from jax.sharding import PartitionSpec as P

HD = 128


npo_beta = 0.1
norm_eps = 1e-05
rope_base = 500000.0


def shifted(value, axis, steps):
    count = lax.axis_size(axis)
    leading, last = (max(0, -steps), min(count, count - steps))
    return lax.ppermute(value, axis, [(source, source + steps) for source in range(leading, last)])


def rope_tables(length, head_dim):
    positions = jnp.arange(length).astype(jnp.float32)
    freq_index = jnp.arange(head_dim // 2).astype(jnp.float32)
    inverse = 1.0 / rope_base ** (2.0 * freq_index / head_dim)
    angles = positions[:, None] * inverse[None, :]
    cosine = jnp.concatenate([jnp.cos(angles), jnp.cos(angles)], axis=1)
    sine = jnp.concatenate([jnp.sin(angles), jnp.sin(angles)], axis=1)
    return (cosine, sine)


def rotate_half(values):
    half = values.shape[-1] // 2
    return jnp.concatenate([-values[..., half:], values[..., :half]], axis=-1)


def rotate_back(values):
    half = values.shape[-1] // 2
    return jnp.concatenate([values[..., half:], -values[..., :half]], axis=-1)


def sequence_grads(query_seq, key_seq, value_seq, cotan_seq, length_seq, cosine, sine):
    seq_len, kv_heads, head_dim = key_seq.shape
    group = query_seq.shape[1] // kv_heads
    scale = 1.0 / math.sqrt(head_dim)
    query_g = query_seq.reshape(seq_len, kv_heads, group, head_dim)
    cotan_g = cotan_seq.reshape(seq_len, kv_heads, group, head_dim)
    scores = (
        jnp.einsum("ikgd,jkd->kgij", query_g, key_seq, preferred_element_type=jnp.float32) * scale
    )
    row_pos = jnp.arange(seq_len)[:, None]
    col_pos = jnp.arange(seq_len)[None, :]
    allowed = (col_pos <= row_pos) & (col_pos < length_seq)
    scores = jnp.where(allowed, scores, -1e30)
    highest = jnp.max(scores, axis=-1, keepdims=True)
    expd = jnp.where(allowed, jnp.exp(scores - highest), 0.0)
    probs = expd / jnp.sum(expd, axis=-1, keepdims=True)
    probs_low = probs.astype(jnp.bfloat16)
    value_grad = jnp.einsum(
        "kgij,ikgd->jkd", probs_low, cotan_g, preferred_element_type=jnp.float32
    ).astype(jnp.bfloat16)
    prob_grad = jnp.einsum("ikgd,jkd->kgij", cotan_g, value_seq, preferred_element_type=jnp.float32)
    centre = jnp.sum(probs * prob_grad, axis=-1, keepdims=True)
    score_grad = (probs * (prob_grad - centre) * scale).astype(jnp.bfloat16)
    rotated_grad = jnp.einsum(
        "kgij,ikgd->jkd", score_grad, query_g, preferred_element_type=jnp.float32
    )
    key_grad = rotated_grad * cosine[:, None, :] + rotate_back(rotated_grad * sine[:, None, :])
    return (key_grad.astype(jnp.bfloat16), value_grad)


def norm_backward(normed_grad, gain_f, nhat, inv_rms):
    gain_grad_in = normed_grad * gain_f
    centre = jnp.mean(gain_grad_in * nhat, axis=-1, keepdims=True)
    return ((gain_grad_in - nhat * centre) * inv_rms).astype(jnp.bfloat16)


def on_device(
    hidden_states,
    norm_gain,
    key_weight,
    value_weight,
    queries,
    context_cotangent,
    lengths,
    policy_logp,
    reference_logp,
):
    both_full = lax.all_gather(
        jnp.stack([key_weight[0], value_weight[0]]), "dp", axis=1, tiled=True
    )
    key_full, value_full = both_full[0], both_full[1]
    hidden = hidden_states[0]
    gain_f = norm_gain[0].astype(jnp.float32)
    tok_rows = hidden.shape[0]
    seq_count = lengths.shape[1]
    seq_len = tok_rows // seq_count
    kv_cols = key_full.shape[1]
    kv_local = kv_cols // HD
    q_local = queries.shape[2] // HD
    hidden_f = hidden.astype(jnp.float32)
    inv_rms = lax.rsqrt(jnp.mean(hidden_f * hidden_f, axis=-1, keepdims=True) + norm_eps)
    nhat = hidden_f * inv_rms
    normed = (nhat * gain_f).astype(jnp.bfloat16)
    key_raw = jnp.dot(normed, key_full, preferred_element_type=jnp.float32)
    values = jnp.dot(normed, value_full, preferred_element_type=jnp.float32).astype(jnp.bfloat16)
    cosine, sine = rope_tables(seq_len, HD)
    key_four = key_raw.reshape(seq_count, seq_len, kv_local, HD)
    keys = (
        key_four * cosine[None, :, None, :] + rotate_half(key_four) * sine[None, :, None, :]
    ).astype(jnp.bfloat16)
    total_seqs = seq_count * lax.axis_size("dp")
    seq_weight = 2.0 * jax.nn.sigmoid(npo_beta * (policy_logp[0] - reference_logp[0])) / total_seqs
    live = jnp.arange(seq_len)[None, :] < lengths[0][:, None]
    factor = jnp.where(live, seq_weight[:, None], 0.0)
    scaled = (
        context_cotangent[0].reshape(seq_count, seq_len, q_local, HD).astype(jnp.float32)
        * factor[:, :, None, None]
    ).astype(jnp.bfloat16)

    def one_sequence(items):
        return sequence_grads(items[0], items[1], items[2], items[3], items[4], cosine, sine)

    key_grad, value_grad = lax.map(
        one_sequence,
        (
            queries[0].reshape(seq_count, seq_len, q_local, HD),
            keys,
            values.reshape(seq_count, seq_len, kv_local, HD),
            scaled,
            lengths[0],
        ),
    )
    key_grad = key_grad.reshape(tok_rows, kv_cols)
    value_grad = value_grad.reshape(tok_rows, kv_cols)
    combined = jnp.concatenate([key_grad, value_grad], axis=1)
    grad_total = lax.psum_scatter(
        lax.dot_general(
            normed, combined, (((0,), (0,)), ((), ())), preferred_element_type=jnp.float32
        ).astype(jnp.bfloat16),
        "dp",
        scatter_dimension=0,
        tiled=True,
    )
    n_pipe = lax.axis_size("pipe")
    n_tensor = lax.axis_size("tensor")
    chunks = 4
    rows = tok_rows // chunks
    exchange_steps = [
        [
            (p * n_tensor + t, p * n_tensor + (t + step) % n_tensor)
            for p in range(1, n_pipe)
            for t in range(n_tensor)
        ]
        for step in range(1, n_tensor)
    ]
    shift_pairs = [
        ((p + 1) * n_tensor + (t if (p + 1) // 2 == p // 2 else n_tensor - 1 - t), p * n_tensor + t)
        for p in range(n_pipe - 1)
        for t in range(n_tensor)
    ]
    lowers = []
    held = None
    for c in range(chunks):
        sl = slice(c * rows, (c + 1) * rows)
        part = lax.dot_general(
            key_grad[sl], key_full, (((1,), (1,)), ((), ())), preferred_element_type=jnp.float32
        )
        part = part + lax.dot_general(
            value_grad[sl], value_full, (((1,), (1,)), ((), ())), preferred_element_type=jnp.float32
        )
        part_low = part.astype(jnp.bfloat16)
        if held is not None:
            if len(lowers) > 0:
                part_low, held, lowers[-1] = lax.optimization_barrier(
                    (part_low, held, lowers[-1])
                )
            else:
                part_low, held = lax.optimization_barrier((part_low, held))
            lowers.append(lax.ppermute(held, ("pipe", "tensor"), shift_pairs))
        normed_grad = part_low.astype(jnp.float32)
        for pairs in exchange_steps:
            normed_grad = normed_grad + lax.ppermute(
                part_low, ("pipe", "tensor"), pairs
            ).astype(jnp.float32)
        held = norm_backward(normed_grad, gain_f, nhat[sl], inv_rms[sl])
    lowers.append(lax.ppermute(held, ("pipe", "tensor"), shift_pairs))
    lower = jnp.concatenate(lowers, axis=0)
    return (grad_total[:, :kv_cols][None], grad_total[:, kv_cols:][None], lower[None])


def solution(mesh):
    in_specs = (
        P("pipe", "dp", None),
        P("pipe", None),
        P("pipe", "dp", "tensor"),
        P("pipe", "dp", "tensor"),
        P("pipe", "dp", "tensor"),
        P("pipe", "dp", "tensor"),
        P("pipe", "dp"),
        P("pipe", "dp"),
        P("pipe", "dp"),
    )
    out_specs = (P("pipe", "dp", "tensor"), P("pipe", "dp", "tensor"), P("pipe", "dp", None))
    return jax.shard_map(
        on_device, mesh=mesh, in_specs=in_specs, out_specs=out_specs, check_vma=False
    )
```

```python
import math

import jax
import jax.numpy as jnp
from jax import lax
from jax.sharding import PartitionSpec as P

HD = 128


npo_beta = 0.1
norm_eps = 1e-05
rope_base = 500000.0


def shifted(value, axis, steps):
    count = lax.axis_size(axis)
    leading, last = (max(0, -steps), min(count, count - steps))
    return lax.ppermute(value, axis, [(source, source + steps) for source in range(leading, last)])


def rope_tables(length, head_dim):
    positions = jnp.arange(length).astype(jnp.float32)
    freq_index = jnp.arange(head_dim // 2).astype(jnp.float32)
    inverse = 1.0 / rope_base ** (2.0 * freq_index / head_dim)
    angles = positions[:, None] * inverse[None, :]
    cosine = jnp.concatenate([jnp.cos(angles), jnp.cos(angles)], axis=1)
    sine = jnp.concatenate([jnp.sin(angles), jnp.sin(angles)], axis=1)
    return (cosine, sine)


def rotate_half(values):
    half = values.shape[-1] // 2
    return jnp.concatenate([-values[..., half:], values[..., :half]], axis=-1)


def rotate_back(values):
    half = values.shape[-1] // 2
    return jnp.concatenate([values[..., half:], -values[..., :half]], axis=-1)


def sequence_grads(query_seq, key_seq, value_seq, cotan_seq, length_seq, cosine, sine):
    seq_len, kv_heads, head_dim = key_seq.shape
    group = query_seq.shape[1] // kv_heads
    scale = 1.0 / math.sqrt(head_dim)
    query_g = query_seq.reshape(seq_len, kv_heads, group, head_dim)
    cotan_g = cotan_seq.reshape(seq_len, kv_heads, group, head_dim)
    scores = (
        jnp.einsum("ikgd,jkd->kgij", query_g, key_seq, preferred_element_type=jnp.float32) * scale
    )
    row_pos = jnp.arange(seq_len)[:, None]
    col_pos = jnp.arange(seq_len)[None, :]
    allowed = (col_pos <= row_pos) & (col_pos < length_seq)
    scores = jnp.where(allowed, scores, -1e30)
    highest = jnp.max(scores, axis=-1, keepdims=True)
    expd = jnp.where(allowed, jnp.exp(scores - highest), 0.0)
    probs = expd / jnp.sum(expd, axis=-1, keepdims=True)
    probs_low = probs.astype(jnp.bfloat16)
    value_grad = jnp.einsum(
        "kgij,ikgd->jkd", probs_low, cotan_g, preferred_element_type=jnp.float32
    ).astype(jnp.bfloat16)
    prob_grad = jnp.einsum("ikgd,jkd->kgij", cotan_g, value_seq, preferred_element_type=jnp.float32)
    centre = jnp.sum(probs * prob_grad, axis=-1, keepdims=True)
    score_grad = (probs * (prob_grad - centre) * scale).astype(jnp.bfloat16)
    rotated_grad = jnp.einsum(
        "kgij,ikgd->jkd", score_grad, query_g, preferred_element_type=jnp.float32
    )
    key_grad = rotated_grad * cosine[:, None, :] + rotate_back(rotated_grad * sine[:, None, :])
    return (key_grad.astype(jnp.bfloat16), value_grad)


def norm_backward(normed_grad, gain_f, nhat, inv_rms):
    gain_grad_in = normed_grad * gain_f
    centre = jnp.mean(gain_grad_in * nhat, axis=-1, keepdims=True)
    return ((gain_grad_in - nhat * centre) * inv_rms).astype(jnp.bfloat16)


def on_device(
    hidden_states,
    norm_gain,
    key_weight,
    value_weight,
    queries,
    context_cotangent,
    lengths,
    policy_logp,
    reference_logp,
):
    both_full = lax.all_gather(
        jnp.stack([key_weight[0], value_weight[0]]), "dp", axis=1, tiled=True
    )
    key_full, value_full = both_full[0], both_full[1]
    hidden = hidden_states[0]
    gain_f = norm_gain[0].astype(jnp.float32)
    tok_rows = hidden.shape[0]
    seq_count = lengths.shape[1]
    seq_len = tok_rows // seq_count
    kv_cols = key_full.shape[1]
    kv_local = kv_cols // HD
    q_local = queries.shape[2] // HD
    hidden_f = hidden.astype(jnp.float32)
    inv_rms = lax.rsqrt(jnp.mean(hidden_f * hidden_f, axis=-1, keepdims=True) + norm_eps)
    nhat = hidden_f * inv_rms
    normed = (nhat * gain_f).astype(jnp.bfloat16)
    projected = jnp.einsum("td,wdc->wtc", normed, both_full, preferred_element_type=jnp.float32)
    key_raw = projected[0]
    values = projected[1].astype(jnp.bfloat16)
    cosine, sine = rope_tables(seq_len, HD)
    key_four = key_raw.reshape(seq_count, seq_len, kv_local, HD)
    keys = (
        key_four * cosine[None, :, None, :] + rotate_half(key_four) * sine[None, :, None, :]
    ).astype(jnp.bfloat16)
    total_seqs = seq_count * lax.axis_size("dp")
    seq_weight = 2.0 * jax.nn.sigmoid(npo_beta * (policy_logp[0] - reference_logp[0])) / total_seqs
    live = jnp.arange(seq_len)[None, :] < lengths[0][:, None]
    factor = jnp.where(live, seq_weight[:, None], 0.0)
    scaled = (
        context_cotangent[0].reshape(seq_count, seq_len, q_local, HD).astype(jnp.float32)
        * factor[:, :, None, None]
    ).astype(jnp.bfloat16)

    def one_sequence(items):
        return sequence_grads(items[0], items[1], items[2], items[3], items[4], cosine, sine)

    key_grad, value_grad = lax.map(
        one_sequence,
        (
            queries[0].reshape(seq_count, seq_len, q_local, HD),
            keys,
            values.reshape(seq_count, seq_len, kv_local, HD),
            scaled,
            lengths[0],
        ),
    )
    key_grad = key_grad.reshape(tok_rows, kv_cols)
    value_grad = value_grad.reshape(tok_rows, kv_cols)
    combined = jnp.concatenate([key_grad, value_grad], axis=1)
    grad_total = lax.psum_scatter(
        lax.dot_general(
            normed, combined, (((0,), (0,)), ((), ())), preferred_element_type=jnp.float32
        ).astype(jnp.bfloat16),
        "dp",
        scatter_dimension=0,
        tiled=True,
    )
    both_grads = jnp.stack([key_grad, value_grad])
    n_pipe = lax.axis_size("pipe")
    n_tensor = lax.axis_size("tensor")
    chunks = 4
    rows = tok_rows // chunks
    exchange_steps = [
        [
            (p * n_tensor + t, p * n_tensor + (t + step) % n_tensor)
            for p in range(1, n_pipe)
            for t in range(n_tensor)
        ]
        for step in range(1, n_tensor)
    ]
    shift_pairs = [
        ((p + 1) * n_tensor + (t if (p + 1) // 2 == p // 2 else n_tensor - 1 - t), p * n_tensor + t)
        for p in range(n_pipe - 1)
        for t in range(n_tensor)
    ]
    lowers = []
    held = None
    for c in range(chunks):
        sl = slice(c * rows, (c + 1) * rows)
        part = jnp.einsum(
            "wtc,wdc->td", both_grads[:, sl], both_full, preferred_element_type=jnp.float32
        )
        part_low = part.astype(jnp.bfloat16)
        if held is not None:
            if len(lowers) > 0:
                part_low, held, lowers[-1] = lax.optimization_barrier(
                    (part_low, held, lowers[-1])
                )
            else:
                part_low, held = lax.optimization_barrier((part_low, held))
            lowers.append(lax.ppermute(held, ("pipe", "tensor"), shift_pairs))
        normed_grad = part_low.astype(jnp.float32)
        for pairs in exchange_steps:
            normed_grad = normed_grad + lax.ppermute(
                part_low, ("pipe", "tensor"), pairs
            ).astype(jnp.float32)
        held = norm_backward(normed_grad, gain_f, nhat[sl], inv_rms[sl])
    lowers.append(lax.ppermute(held, ("pipe", "tensor"), shift_pairs))
    lower = jnp.concatenate(lowers, axis=0)
    return (grad_total[:, :kv_cols][None], grad_total[:, kv_cols:][None], lower[None])


def solution(mesh):
    in_specs = (
        P("pipe", "dp", None),
        P("pipe", None),
        P("pipe", "dp", "tensor"),
        P("pipe", "dp", "tensor"),
        P("pipe", "dp", "tensor"),
        P("pipe", "dp", "tensor"),
        P("pipe", "dp"),
        P("pipe", "dp"),
        P("pipe", "dp"),
    )
    out_specs = (P("pipe", "dp", "tensor"), P("pipe", "dp", "tensor"), P("pipe", "dp", None))
    return jax.shard_map(
        on_device, mesh=mesh, in_specs=in_specs, out_specs=out_specs, check_vma=False
    )
```

```python
import math

import jax
import jax.numpy as jnp
from jax import lax
from jax.sharding import PartitionSpec as P

HD = 128


npo_beta = 0.1
norm_eps = 1e-05
rope_base = 500000.0


def shifted(value, axis, steps):
    count = lax.axis_size(axis)
    leading, last = (max(0, -steps), min(count, count - steps))
    return lax.ppermute(value, axis, [(source, source + steps) for source in range(leading, last)])


def rope_tables(length, head_dim):
    positions = jnp.arange(length).astype(jnp.float32)
    freq_index = jnp.arange(head_dim // 2).astype(jnp.float32)
    inverse = 1.0 / rope_base ** (2.0 * freq_index / head_dim)
    angles = positions[:, None] * inverse[None, :]
    cosine = jnp.concatenate([jnp.cos(angles), jnp.cos(angles)], axis=1)
    sine = jnp.concatenate([jnp.sin(angles), jnp.sin(angles)], axis=1)
    return (cosine, sine)


def rotate_half(values):
    half = values.shape[-1] // 2
    return jnp.concatenate([-values[..., half:], values[..., :half]], axis=-1)


def rotate_back(values):
    half = values.shape[-1] // 2
    return jnp.concatenate([values[..., half:], -values[..., :half]], axis=-1)


def sequence_grads(query_seq, key_seq, value_seq, cotan_seq, length_seq, cosine, sine):
    seq_len, kv_heads, head_dim = key_seq.shape
    group = query_seq.shape[1] // kv_heads
    scale = 1.0 / math.sqrt(head_dim)
    query_g = query_seq.reshape(seq_len, kv_heads, group, head_dim)
    cotan_g = cotan_seq.reshape(seq_len, kv_heads, group, head_dim)
    scores = (
        jnp.einsum("ikgd,jkd->kgij", query_g, key_seq, preferred_element_type=jnp.float32) * scale
    )
    row_pos = jnp.arange(seq_len)[:, None]
    col_pos = jnp.arange(seq_len)[None, :]
    allowed = (col_pos <= row_pos) & (col_pos < length_seq)
    scores = jnp.where(allowed, scores, -1e30)
    highest = jnp.max(scores, axis=-1, keepdims=True)
    expd = jnp.where(allowed, jnp.exp(scores - highest), 0.0)
    probs = expd / jnp.sum(expd, axis=-1, keepdims=True)
    probs_low = probs.astype(jnp.bfloat16)
    value_grad = jnp.einsum(
        "kgij,ikgd->jkd", probs_low, cotan_g, preferred_element_type=jnp.float32
    ).astype(jnp.bfloat16)
    prob_grad = jnp.einsum("ikgd,jkd->kgij", cotan_g, value_seq, preferred_element_type=jnp.float32)
    centre = jnp.sum(probs * prob_grad, axis=-1, keepdims=True)
    score_grad = (probs * (prob_grad - centre) * scale).astype(jnp.bfloat16)
    rotated_grad = jnp.einsum(
        "kgij,ikgd->jkd", score_grad, query_g, preferred_element_type=jnp.float32
    )
    key_grad = rotated_grad * cosine[:, None, :] + rotate_back(rotated_grad * sine[:, None, :])
    return (key_grad.astype(jnp.bfloat16), value_grad)


def norm_backward(normed_grad, gain_f, nhat, inv_rms):
    gain_grad_in = normed_grad * gain_f
    centre = jnp.mean(gain_grad_in * nhat, axis=-1, keepdims=True)
    return ((gain_grad_in - nhat * centre) * inv_rms).astype(jnp.bfloat16)


def on_device(
    hidden_states,
    norm_gain,
    key_weight,
    value_weight,
    queries,
    context_cotangent,
    lengths,
    policy_logp,
    reference_logp,
):
    own_block = jnp.stack([key_weight[0], value_weight[0]])
    n_dp = lax.axis_size("dp")
    me_dp = lax.axis_index("dp")
    block_rows = own_block.shape[1]
    both_full = jnp.zeros((2, n_dp * block_rows, own_block.shape[2]), own_block.dtype)
    for k in range(n_dp):
        if k == 0:
            piece = own_block
        else:
            piece = lax.ppermute(own_block, "dp", [(s, (s + k) % n_dp) for s in range(n_dp)])
        start = ((me_dp - k) % n_dp) * block_rows
        both_full = lax.dynamic_update_slice(both_full, piece, (0, start, 0))
    key_full, value_full = both_full[0], both_full[1]
    hidden = hidden_states[0]
    gain_f = norm_gain[0].astype(jnp.float32)
    tok_rows = hidden.shape[0]
    seq_count = lengths.shape[1]
    seq_len = tok_rows // seq_count
    kv_cols = key_full.shape[1]
    kv_local = kv_cols // HD
    q_local = queries.shape[2] // HD
    hidden_f = hidden.astype(jnp.float32)
    inv_rms = lax.rsqrt(jnp.mean(hidden_f * hidden_f, axis=-1, keepdims=True) + norm_eps)
    nhat = hidden_f * inv_rms
    normed = (nhat * gain_f).astype(jnp.bfloat16)
    projected = jnp.einsum("td,wdc->wtc", normed, both_full, preferred_element_type=jnp.float32)
    key_raw = projected[0]
    values = projected[1].astype(jnp.bfloat16)
    cosine, sine = rope_tables(seq_len, HD)
    key_four = key_raw.reshape(seq_count, seq_len, kv_local, HD)
    keys = (
        key_four * cosine[None, :, None, :] + rotate_half(key_four) * sine[None, :, None, :]
    ).astype(jnp.bfloat16)
    total_seqs = seq_count * lax.axis_size("dp")
    seq_weight = 2.0 * jax.nn.sigmoid(npo_beta * (policy_logp[0] - reference_logp[0])) / total_seqs
    live = jnp.arange(seq_len)[None, :] < lengths[0][:, None]
    factor = jnp.where(live, seq_weight[:, None], 0.0)
    scaled = (
        context_cotangent[0].reshape(seq_count, seq_len, q_local, HD).astype(jnp.float32)
        * factor[:, :, None, None]
    ).astype(jnp.bfloat16)

    def one_sequence(items):
        return sequence_grads(items[0], items[1], items[2], items[3], items[4], cosine, sine)

    key_grad, value_grad = lax.map(
        one_sequence,
        (
            queries[0].reshape(seq_count, seq_len, q_local, HD),
            keys,
            values.reshape(seq_count, seq_len, kv_local, HD),
            scaled,
            lengths[0],
        ),
    )
    key_grad = key_grad.reshape(tok_rows, kv_cols)
    value_grad = value_grad.reshape(tok_rows, kv_cols)
    combined = jnp.concatenate([key_grad, value_grad], axis=1)
    grad_total = lax.psum_scatter(
        lax.dot_general(
            normed, combined, (((0,), (0,)), ((), ())), preferred_element_type=jnp.float32
        ).astype(jnp.bfloat16),
        "dp",
        scatter_dimension=0,
        tiled=True,
    )
    both_grads = jnp.stack([key_grad, value_grad])
    n_pipe = lax.axis_size("pipe")
    n_tensor = lax.axis_size("tensor")
    chunks = 4
    rows = tok_rows // chunks
    exchange_steps = [
        [
            (p * n_tensor + t, p * n_tensor + (t + step) % n_tensor)
            for p in range(1, n_pipe)
            for t in range(n_tensor)
        ]
        for step in range(1, n_tensor)
    ]
    shift_pairs = [
        ((p + 1) * n_tensor + (t if (p + 1) // 2 == p // 2 else n_tensor - 1 - t), p * n_tensor + t)
        for p in range(n_pipe - 1)
        for t in range(n_tensor)
    ]
    lowers = []
    held = None
    for c in range(chunks):
        sl = slice(c * rows, (c + 1) * rows)
        part = jnp.einsum(
            "wtc,wdc->td", both_grads[:, sl], both_full, preferred_element_type=jnp.float32
        )
        part_low = part.astype(jnp.bfloat16)
        if held is not None:
            if len(lowers) > 0:
                part_low, held, lowers[-1] = lax.optimization_barrier(
                    (part_low, held, lowers[-1])
                )
            else:
                part_low, held = lax.optimization_barrier((part_low, held))
            lowers.append(lax.ppermute(held, ("pipe", "tensor"), shift_pairs))
        normed_grad = part_low.astype(jnp.float32)
        for pairs in exchange_steps:
            normed_grad = normed_grad + lax.ppermute(
                part_low, ("pipe", "tensor"), pairs
            ).astype(jnp.float32)
        held = norm_backward(normed_grad, gain_f, nhat[sl], inv_rms[sl])
    lowers.append(lax.ppermute(held, ("pipe", "tensor"), shift_pairs))
    lower = jnp.concatenate(lowers, axis=0)
    return (grad_total[:, :kv_cols][None], grad_total[:, kv_cols:][None], lower[None])


def solution(mesh):
    in_specs = (
        P("pipe", "dp", None),
        P("pipe", None),
        P("pipe", "dp", "tensor"),
        P("pipe", "dp", "tensor"),
        P("pipe", "dp", "tensor"),
        P("pipe", "dp", "tensor"),
        P("pipe", "dp"),
        P("pipe", "dp"),
        P("pipe", "dp"),
    )
    out_specs = (P("pipe", "dp", "tensor"), P("pipe", "dp", "tensor"), P("pipe", "dp", None))
    return jax.shard_map(
        on_device, mesh=mesh, in_specs=in_specs, out_specs=out_specs, check_vma=False
    )
```

```python
import functools
import math

import jax
import jax.numpy as jnp
from jax import lax
from jax.sharding import PartitionSpec as P

HD = 128


npo_beta = 0.1
norm_eps = 1e-05
rope_base = 500000.0


def shifted(value, axis, steps):
    count = lax.axis_size(axis)
    leading, last = (max(0, -steps), min(count, count - steps))
    return lax.ppermute(value, axis, [(source, source + steps) for source in range(leading, last)])


def rope_tables(length, head_dim):
    positions = jnp.arange(length).astype(jnp.float32)
    freq_index = jnp.arange(head_dim // 2).astype(jnp.float32)
    inverse = 1.0 / rope_base ** (2.0 * freq_index / head_dim)
    angles = positions[:, None] * inverse[None, :]
    cosine = jnp.concatenate([jnp.cos(angles), jnp.cos(angles)], axis=1)
    sine = jnp.concatenate([jnp.sin(angles), jnp.sin(angles)], axis=1)
    return (cosine, sine)


def rotate_half(values):
    half = values.shape[-1] // 2
    return jnp.concatenate([-values[..., half:], values[..., :half]], axis=-1)


def rotate_back(values):
    half = values.shape[-1] // 2
    return jnp.concatenate([values[..., half:], -values[..., :half]], axis=-1)


def sequence_grads(query_seq, key_seq, value_seq, cotan_seq, length_seq, cosine, sine):
    seq_len, kv_heads, head_dim = key_seq.shape
    group = query_seq.shape[1] // kv_heads
    scale = 1.0 / math.sqrt(head_dim)
    query_g = query_seq.reshape(seq_len, kv_heads, group, head_dim)
    cotan_g = cotan_seq.reshape(seq_len, kv_heads, group, head_dim)
    scores = (
        jnp.einsum("ikgd,jkd->kgij", query_g, key_seq, preferred_element_type=jnp.float32) * scale
    )
    row_pos = jnp.arange(seq_len)[:, None]
    col_pos = jnp.arange(seq_len)[None, :]
    allowed = (col_pos <= row_pos) & (col_pos < length_seq)
    scores = jnp.where(allowed, scores, -1e30)
    highest = jnp.max(scores, axis=-1, keepdims=True)
    expd = jnp.where(allowed, jnp.exp(scores - highest), 0.0)
    probs = expd / jnp.sum(expd, axis=-1, keepdims=True)
    probs_low = probs.astype(jnp.bfloat16)
    value_grad = jnp.einsum(
        "kgij,ikgd->jkd", probs_low, cotan_g, preferred_element_type=jnp.float32
    ).astype(jnp.bfloat16)
    prob_grad = jnp.einsum("ikgd,jkd->kgij", cotan_g, value_seq, preferred_element_type=jnp.float32)
    centre = jnp.sum(probs * prob_grad, axis=-1, keepdims=True)
    score_grad = (probs * (prob_grad - centre) * scale).astype(jnp.bfloat16)
    rotated_grad = jnp.einsum(
        "kgij,ikgd->jkd", score_grad, query_g, preferred_element_type=jnp.float32
    )
    key_grad = rotated_grad * cosine[:, None, :] + rotate_back(rotated_grad * sine[:, None, :])
    return (key_grad.astype(jnp.bfloat16), value_grad)


def norm_backward(normed_grad, gain_f, nhat, inv_rms):
    gain_grad_in = normed_grad * gain_f
    centre = jnp.mean(gain_grad_in * nhat, axis=-1, keepdims=True)
    return ((gain_grad_in - nhat * centre) * inv_rms).astype(jnp.bfloat16)


def on_device(
    hidden_states,
    norm_gain,
    key_weight,
    value_weight,
    queries,
    context_cotangent,
    lengths,
    policy_logp,
    reference_logp,
):
    both_full = lax.all_gather(
        jnp.stack([key_weight[0], value_weight[0]]), "dp", axis=1, tiled=True
    )
    key_full, value_full = both_full[0], both_full[1]
    hidden = hidden_states[0]
    gain_f = norm_gain[0].astype(jnp.float32)
    tok_rows = hidden.shape[0]
    seq_count = lengths.shape[1]
    seq_len = tok_rows // seq_count
    kv_cols = key_full.shape[1]
    kv_local = kv_cols // HD
    q_local = queries.shape[2] // HD
    hidden_f = hidden.astype(jnp.float32)
    inv_rms = lax.rsqrt(jnp.mean(hidden_f * hidden_f, axis=-1, keepdims=True) + norm_eps)
    nhat = hidden_f * inv_rms
    normed = (nhat * gain_f).astype(jnp.bfloat16)
    projected = jnp.einsum("td,wdc->wtc", normed, both_full, preferred_element_type=jnp.float32)
    key_raw = projected[0]
    values = projected[1].astype(jnp.bfloat16)
    cosine, sine = rope_tables(seq_len, HD)
    key_four = key_raw.reshape(seq_count, seq_len, kv_local, HD)
    keys = (
        key_four * cosine[None, :, None, :] + rotate_half(key_four) * sine[None, :, None, :]
    ).astype(jnp.bfloat16)
    total_seqs = seq_count * lax.axis_size("dp")
    seq_weight = 2.0 * jax.nn.sigmoid(npo_beta * (policy_logp[0] - reference_logp[0])) / total_seqs
    live = jnp.arange(seq_len)[None, :] < lengths[0][:, None]
    factor = jnp.where(live, seq_weight[:, None], 0.0)
    scaled = (
        context_cotangent[0].reshape(seq_count, seq_len, q_local, HD).astype(jnp.float32)
        * factor[:, :, None, None]
    ).astype(jnp.bfloat16)

    def one_sequence(items):
        return sequence_grads(items[0], items[1], items[2], items[3], items[4], cosine, sine)

    key_grad, value_grad = lax.map(
        one_sequence,
        (
            queries[0].reshape(seq_count, seq_len, q_local, HD),
            keys,
            values.reshape(seq_count, seq_len, kv_local, HD),
            scaled,
            lengths[0],
        ),
    )
    key_grad = key_grad.reshape(tok_rows, kv_cols)
    value_grad = value_grad.reshape(tok_rows, kv_cols)
    combined = jnp.concatenate([key_grad, value_grad], axis=1)
    grad_total = lax.psum_scatter(
        lax.dot_general(
            normed, combined, (((0,), (0,)), ((), ())), preferred_element_type=jnp.float32
        ).astype(jnp.bfloat16),
        "dp",
        scatter_dimension=0,
        tiled=True,
    )
    both_grads = jnp.stack([key_grad, value_grad])
    n_pipe = lax.axis_size("pipe")
    n_tensor = lax.axis_size("tensor")
    chunks = 4
    rows = tok_rows // chunks
    width = hidden.shape[1] // n_tensor
    me_pipe = lax.axis_index("pipe")
    me_tensor = lax.axis_index("tensor")
    other = n_tensor - 1 - me_tensor
    feature_count = hidden.shape[1]

    def at(p, t):
        return p * n_tensor + t

    cross = [q for q in range(1, n_pipe) if q // 2 != (q - 1) // 2]
    near = [q for q in range(1, n_pipe) if q not in cross]
    swap = lambda qs: [(at(q, t), at(q, n_tensor - 1 - t)) for q in qs for t in range(n_tensor)]
    pairs_first = swap(range(1, n_pipe))
    pairs_second = swap(near)
    pairs_centre = swap(cross)
    pairs_down = [(at(q, t), at(q - 1, t)) for q in near for t in range(n_tensor)]
    pairs_mine = pairs_down + [
        (at(q, t), at(q - 1, n_tensor - 1 - t)) for q in cross for t in range(n_tensor)
    ]
    pairs_relay = swap([q - 1 for q in cross])
    cross_src = functools.reduce(jnp.logical_or, [me_pipe == q for q in cross], me_pipe < 0)
    cross_dst = functools.reduce(jnp.logical_or, [me_pipe == q - 1 for q in cross], me_pipe < 0)
    axes = ("pipe", "tensor")
    halve = lambda x, which: lax.dynamic_slice_in_dim(x, which * width, width, axis=x.ndim - 1)
    gain_mine, gain_other = halve(gain_f, me_tensor), halve(gain_f, other)

    def send_down(cot_mine, cot_other):
        got_mine = lax.ppermute(cot_mine, axes, pairs_mine)
        got_rest = lax.ppermute(cot_other, axes, pairs_down)
        relayed = lax.ppermute(got_mine, axes, pairs_relay)
        half_mine = jnp.where(cross_dst, relayed, got_mine)
        half_other = jnp.where(cross_dst, got_mine, got_rest)
        full = jnp.zeros((cot_mine.shape[0], feature_count), cot_mine.dtype)
        full = lax.dynamic_update_slice_in_dim(full, half_mine, me_tensor * width, axis=1)
        return lax.dynamic_update_slice_in_dim(full, half_other, other * width, axis=1)

    lowers = []
    held = None
    for c in range(chunks):
        sl = slice(c * rows, (c + 1) * rows)
        part = jnp.einsum(
            "wtc,wdc->td", both_grads[:, sl], both_full, preferred_element_type=jnp.float32
        )
        part_low = part.astype(jnp.bfloat16)
        if held is not None:
            if len(lowers) > 0:
                part_low, held, lowers[-1] = lax.optimization_barrier(
                    (part_low, held, lowers[-1])
                )
            else:
                part_low, held = lax.optimization_barrier((part_low, held))
            lowers.append(send_down(*held))
        mine, theirs = halve(part_low, me_tensor), halve(part_low, other)
        grad_mine = mine.astype(jnp.float32) + lax.ppermute(theirs, axes, pairs_first).astype(
            jnp.float32
        )
        grad_other = theirs.astype(jnp.float32) + lax.ppermute(
            mine, axes, pairs_second
        ).astype(jnp.float32)
        nhat_c = nhat[sl]
        nhat_mine, nhat_other = halve(nhat_c, me_tensor), halve(nhat_c, other)
        gin_mine = grad_mine * gain_mine
        gin_other = grad_other * gain_other
        sum_mine = jnp.sum(gin_mine * nhat_mine, axis=-1, keepdims=True)
        sum_other = jnp.where(
            cross_src,
            lax.ppermute(sum_mine, axes, pairs_centre),
            jnp.sum(gin_other * nhat_other, axis=-1, keepdims=True),
        )
        centre = (sum_mine + sum_other) / feature_count
        scale_c = inv_rms[sl]
        held = (
            ((gin_mine - nhat_mine * centre) * scale_c).astype(jnp.bfloat16),
            ((gin_other - nhat_other * centre) * scale_c).astype(jnp.bfloat16),
        )
    lowers.append(send_down(*held))
    lower = jnp.concatenate(lowers, axis=0)
    return (grad_total[:, :kv_cols][None], grad_total[:, kv_cols:][None], lower[None])


def solution(mesh):
    in_specs = (
        P("pipe", "dp", None),
        P("pipe", None),
        P("pipe", "dp", "tensor"),
        P("pipe", "dp", "tensor"),
        P("pipe", "dp", "tensor"),
        P("pipe", "dp", "tensor"),
        P("pipe", "dp"),
        P("pipe", "dp"),
        P("pipe", "dp"),
    )
    out_specs = (P("pipe", "dp", "tensor"), P("pipe", "dp", "tensor"), P("pipe", "dp", None))
    return jax.shard_map(
        on_device, mesh=mesh, in_specs=in_specs, out_specs=out_specs, check_vma=False
    )
```

```python
import math

import jax
import jax.numpy as jnp
from jax import lax
from jax.sharding import PartitionSpec as P

HD = 128


npo_beta = 0.1
norm_eps = 1e-05
rope_base = 500000.0


def shifted(value, axis, steps):
    count = lax.axis_size(axis)
    leading, last = (max(0, -steps), min(count, count - steps))
    return lax.ppermute(value, axis, [(source, source + steps) for source in range(leading, last)])


def rope_tables(length, head_dim):
    positions = jnp.arange(length).astype(jnp.float32)
    freq_index = jnp.arange(head_dim // 2).astype(jnp.float32)
    inverse = 1.0 / rope_base ** (2.0 * freq_index / head_dim)
    angles = positions[:, None] * inverse[None, :]
    cosine = jnp.concatenate([jnp.cos(angles), jnp.cos(angles)], axis=1)
    sine = jnp.concatenate([jnp.sin(angles), jnp.sin(angles)], axis=1)
    return (cosine, sine)


def rotate_half(values):
    half = values.shape[-1] // 2
    return jnp.concatenate([-values[..., half:], values[..., :half]], axis=-1)


def rotate_back(values):
    half = values.shape[-1] // 2
    return jnp.concatenate([values[..., half:], -values[..., :half]], axis=-1)


def sequence_grads(query_seq, key_seq, value_seq, cotan_seq, length_seq, cosine, sine):
    seq_len, kv_heads, head_dim = key_seq.shape
    group = query_seq.shape[1] // kv_heads
    scale = 1.0 / math.sqrt(head_dim)
    query_g = query_seq.reshape(seq_len, kv_heads, group, head_dim).transpose(1, 2, 0, 3)
    cotan_g = cotan_seq.reshape(seq_len, kv_heads, group, head_dim).transpose(1, 2, 0, 3)
    key_k = key_seq.transpose(1, 0, 2)
    value_k = value_seq.transpose(1, 0, 2)
    scores = (
        jnp.einsum("kgid,kjd->kgij", query_g, key_k, preferred_element_type=jnp.float32) * scale
    )
    row_pos = jnp.arange(seq_len)[:, None]
    col_pos = jnp.arange(seq_len)[None, :]
    allowed = (col_pos <= row_pos) & (col_pos < length_seq)
    scores = jnp.where(allowed, scores, -1e30)
    highest = jnp.max(scores, axis=-1, keepdims=True)
    expd = jnp.where(allowed, jnp.exp(scores - highest), 0.0)
    probs = expd / jnp.sum(expd, axis=-1, keepdims=True)
    probs_low = probs.astype(jnp.bfloat16)
    value_grad = jnp.einsum(
        "kgij,kgid->kjd", probs_low, cotan_g, preferred_element_type=jnp.float32
    ).astype(jnp.bfloat16)
    prob_grad = jnp.einsum("kgid,kjd->kgij", cotan_g, value_k, preferred_element_type=jnp.float32)
    centre = jnp.sum(probs * prob_grad, axis=-1, keepdims=True)
    score_grad = (probs * (prob_grad - centre) * scale).astype(jnp.bfloat16)
    rotated_grad = jnp.einsum(
        "kgij,kgid->kjd", score_grad, query_g, preferred_element_type=jnp.float32
    ).transpose(1, 0, 2)
    key_grad = rotated_grad * cosine[:, None, :] + rotate_back(rotated_grad * sine[:, None, :])
    return (key_grad.astype(jnp.bfloat16), value_grad.transpose(1, 0, 2))


def norm_backward(normed_grad, gain_f, nhat, inv_rms):
    gain_grad_in = normed_grad * gain_f
    centre = jnp.mean(gain_grad_in * nhat, axis=-1, keepdims=True)
    return ((gain_grad_in - nhat * centre) * inv_rms).astype(jnp.bfloat16)


def on_device(
    hidden_states,
    norm_gain,
    key_weight,
    value_weight,
    queries,
    context_cotangent,
    lengths,
    policy_logp,
    reference_logp,
):
    both_full = lax.all_gather(
        jnp.stack([key_weight[0], value_weight[0]]), "dp", axis=1, tiled=True
    )
    key_full, value_full = both_full[0], both_full[1]
    hidden = hidden_states[0]
    gain_f = norm_gain[0].astype(jnp.float32)
    tok_rows = hidden.shape[0]
    seq_count = lengths.shape[1]
    seq_len = tok_rows // seq_count
    kv_cols = key_full.shape[1]
    kv_local = kv_cols // HD
    q_local = queries.shape[2] // HD
    hidden_f = hidden.astype(jnp.float32)
    inv_rms = lax.rsqrt(jnp.mean(hidden_f * hidden_f, axis=-1, keepdims=True) + norm_eps)
    nhat = hidden_f * inv_rms
    normed = lax.optimization_barrier((nhat * gain_f).astype(jnp.bfloat16))
    projected = jnp.einsum("td,wdc->wtc", normed, both_full, preferred_element_type=jnp.float32)
    key_raw = projected[0]
    values = projected[1].astype(jnp.bfloat16)
    cosine, sine = rope_tables(seq_len, HD)
    key_four = key_raw.reshape(seq_count, seq_len, kv_local, HD)
    keys = (
        key_four * cosine[None, :, None, :] + rotate_half(key_four) * sine[None, :, None, :]
    ).astype(jnp.bfloat16)
    total_seqs = seq_count * lax.axis_size("dp")
    seq_weight = 2.0 * jax.nn.sigmoid(npo_beta * (policy_logp[0] - reference_logp[0])) / total_seqs
    live = jnp.arange(seq_len)[None, :] < lengths[0][:, None]
    factor = jnp.where(live, seq_weight[:, None], 0.0)
    scaled = (
        context_cotangent[0].reshape(seq_count, seq_len, q_local, HD).astype(jnp.float32)
        * factor[:, :, None, None]
    ).astype(jnp.bfloat16)

    def one_sequence(items):
        return sequence_grads(items[0], items[1], items[2], items[3], items[4], cosine, sine)

    key_grad, value_grad = lax.map(
        one_sequence,
        (
            queries[0].reshape(seq_count, seq_len, q_local, HD),
            keys,
            values.reshape(seq_count, seq_len, kv_local, HD),
            scaled,
            lengths[0],
        ),
    )
    key_grad = key_grad.reshape(tok_rows, kv_cols)
    value_grad = value_grad.reshape(tok_rows, kv_cols)
    combined = jnp.concatenate([key_grad, value_grad], axis=1)
    grad_total = lax.psum_scatter(
        lax.dot_general(
            normed, combined, (((0,), (0,)), ((), ())), preferred_element_type=jnp.float32
        ).astype(jnp.bfloat16),
        "dp",
        scatter_dimension=0,
        tiled=True,
    )
    both_grads = jnp.stack([key_grad, value_grad])
    n_pipe = lax.axis_size("pipe")
    n_tensor = lax.axis_size("tensor")
    chunks = 4
    rows = tok_rows // chunks
    exchange_steps = [
        [
            (p * n_tensor + t, p * n_tensor + (t + step) % n_tensor)
            for p in range(1, n_pipe)
            for t in range(n_tensor)
        ]
        for step in range(1, n_tensor)
    ]
    shift_pairs = [
        ((p + 1) * n_tensor + (t if (p + 1) // 2 == p // 2 else n_tensor - 1 - t), p * n_tensor + t)
        for p in range(n_pipe - 1)
        for t in range(n_tensor)
    ]
    lowers = []
    held = None
    for c in range(chunks):
        sl = slice(c * rows, (c + 1) * rows)
        part = jnp.einsum(
            "wtc,wdc->td", both_grads[:, sl], both_full, preferred_element_type=jnp.float32
        )
        part_low = part.astype(jnp.bfloat16)
        if held is not None:
            if len(lowers) > 0:
                part_low, held, lowers[-1] = lax.optimization_barrier(
                    (part_low, held, lowers[-1])
                )
            else:
                part_low, held = lax.optimization_barrier((part_low, held))
            lowers.append(lax.ppermute(held, ("pipe", "tensor"), shift_pairs))
        normed_grad = part_low.astype(jnp.float32)
        for pairs in exchange_steps:
            normed_grad = normed_grad + lax.ppermute(
                part_low, ("pipe", "tensor"), pairs
            ).astype(jnp.float32)
        held = norm_backward(normed_grad, gain_f, nhat[sl], inv_rms[sl])
    lowers.append(lax.ppermute(held, ("pipe", "tensor"), shift_pairs))
    lower = jnp.concatenate(lowers, axis=0)
    return (grad_total[:, :kv_cols][None], grad_total[:, kv_cols:][None], lower[None])


def solution(mesh):
    in_specs = (
        P("pipe", "dp", None),
        P("pipe", None),
        P("pipe", "dp", "tensor"),
        P("pipe", "dp", "tensor"),
        P("pipe", "dp", "tensor"),
        P("pipe", "dp", "tensor"),
        P("pipe", "dp"),
        P("pipe", "dp"),
        P("pipe", "dp"),
    )
    out_specs = (P("pipe", "dp", "tensor"), P("pipe", "dp", "tensor"), P("pipe", "dp", None))
    return jax.shard_map(
        on_device, mesh=mesh, in_specs=in_specs, out_specs=out_specs, check_vma=False
    )
```

```python
import functools
import math

import jax
import jax.numpy as jnp
from jax import lax
from jax.sharding import PartitionSpec as P

HD = 128


npo_beta = 0.1
norm_eps = 1e-05
rope_base = 500000.0


def shifted(value, axis, steps):
    count = lax.axis_size(axis)
    leading, last = (max(0, -steps), min(count, count - steps))
    return lax.ppermute(value, axis, [(source, source + steps) for source in range(leading, last)])


def rope_tables(length, head_dim):
    positions = jnp.arange(length).astype(jnp.float32)
    freq_index = jnp.arange(head_dim // 2).astype(jnp.float32)
    inverse = 1.0 / rope_base ** (2.0 * freq_index / head_dim)
    angles = positions[:, None] * inverse[None, :]
    cosine = jnp.concatenate([jnp.cos(angles), jnp.cos(angles)], axis=1)
    sine = jnp.concatenate([jnp.sin(angles), jnp.sin(angles)], axis=1)
    return (cosine, sine)


def rotate_half(values):
    half = values.shape[-1] // 2
    return jnp.concatenate([-values[..., half:], values[..., :half]], axis=-1)


def rotate_back(values):
    half = values.shape[-1] // 2
    return jnp.concatenate([values[..., half:], -values[..., :half]], axis=-1)


def sequence_grads(query_seq, key_seq, value_seq, cotan_seq, length_seq, cosine, sine):
    seq_len, kv_heads, head_dim = key_seq.shape
    group = query_seq.shape[1] // kv_heads
    scale = 1.0 / math.sqrt(head_dim)
    query_g = query_seq.reshape(seq_len, kv_heads, group, head_dim)
    cotan_g = cotan_seq.reshape(seq_len, kv_heads, group, head_dim)
    scores = (
        jnp.einsum("ikgd,jkd->kgij", query_g, key_seq, preferred_element_type=jnp.float32) * scale
    )
    row_pos = jnp.arange(seq_len)[:, None]
    col_pos = jnp.arange(seq_len)[None, :]
    allowed = (col_pos <= row_pos) & (col_pos < length_seq)
    scores = jnp.where(allowed, scores, -1e30)
    highest = jnp.max(scores, axis=-1, keepdims=True)
    expd = jnp.where(allowed, jnp.exp(scores - highest), 0.0)
    probs = expd / jnp.sum(expd, axis=-1, keepdims=True)
    probs_low = probs.astype(jnp.bfloat16)
    value_grad = jnp.einsum(
        "kgij,ikgd->jkd", probs_low, cotan_g, preferred_element_type=jnp.float32
    ).astype(jnp.bfloat16)
    prob_grad = jnp.einsum("ikgd,jkd->kgij", cotan_g, value_seq, preferred_element_type=jnp.float32)
    centre = jnp.sum(probs * prob_grad, axis=-1, keepdims=True)
    score_grad = (probs * (prob_grad - centre) * scale).astype(jnp.bfloat16)
    rotated_grad = jnp.einsum(
        "kgij,ikgd->jkd", score_grad, query_g, preferred_element_type=jnp.float32
    )
    key_grad = rotated_grad * cosine[:, None, :] + rotate_back(rotated_grad * sine[:, None, :])
    return (key_grad.astype(jnp.bfloat16), value_grad)


def norm_backward(normed_grad, gain_f, nhat, inv_rms):
    gain_grad_in = normed_grad * gain_f
    centre = jnp.mean(gain_grad_in * nhat, axis=-1, keepdims=True)
    return ((gain_grad_in - nhat * centre) * inv_rms).astype(jnp.bfloat16)


def on_device(
    hidden_states,
    norm_gain,
    key_weight,
    value_weight,
    queries,
    context_cotangent,
    lengths,
    policy_logp,
    reference_logp,
):
    both_full = lax.all_gather(
        jnp.stack([key_weight[0], value_weight[0]]), "dp", axis=1, tiled=True
    )
    key_full, value_full = both_full[0], both_full[1]
    hidden = hidden_states[0]
    gain_f = norm_gain[0].astype(jnp.float32)
    tok_rows = hidden.shape[0]
    seq_count = lengths.shape[1]
    seq_len = tok_rows // seq_count
    kv_cols = key_full.shape[1]
    kv_local = kv_cols // HD
    q_local = queries.shape[2] // HD
    hidden_f = hidden.astype(jnp.float32)
    inv_rms = lax.rsqrt(jnp.mean(hidden_f * hidden_f, axis=-1, keepdims=True) + norm_eps)
    nhat = hidden_f * inv_rms
    normed = (nhat * gain_f).astype(jnp.bfloat16)
    projected = jnp.einsum("td,wdc->wtc", normed, both_full, preferred_element_type=jnp.float32)
    key_raw = projected[0]
    values = projected[1].astype(jnp.bfloat16)
    cosine, sine = rope_tables(seq_len, HD)
    key_four = key_raw.reshape(seq_count, seq_len, kv_local, HD)
    keys = (
        key_four * cosine[None, :, None, :] + rotate_half(key_four) * sine[None, :, None, :]
    ).astype(jnp.bfloat16)
    total_seqs = seq_count * lax.axis_size("dp")
    seq_weight = 2.0 * jax.nn.sigmoid(npo_beta * (policy_logp[0] - reference_logp[0])) / total_seqs
    live = jnp.arange(seq_len)[None, :] < lengths[0][:, None]
    factor = jnp.where(live, seq_weight[:, None], 0.0)
    scaled = (
        context_cotangent[0].reshape(seq_count, seq_len, q_local, HD).astype(jnp.float32)
        * factor[:, :, None, None]
    ).astype(jnp.bfloat16)

    def one_sequence(items):
        return sequence_grads(items[0], items[1], items[2], items[3], items[4], cosine, sine)

    key_grad, value_grad = lax.map(
        one_sequence,
        (
            queries[0].reshape(seq_count, seq_len, q_local, HD),
            keys,
            values.reshape(seq_count, seq_len, kv_local, HD),
            scaled,
            lengths[0],
        ),
    )
    key_grad = key_grad.reshape(tok_rows, kv_cols)
    value_grad = value_grad.reshape(tok_rows, kv_cols)
    combined = jnp.concatenate([key_grad, value_grad], axis=1)
    grad_total = lax.psum_scatter(
        lax.dot_general(
            normed, combined, (((0,), (0,)), ((), ())), preferred_element_type=jnp.float32
        ).astype(jnp.bfloat16),
        "dp",
        scatter_dimension=0,
        tiled=True,
    )
    both_grads = jnp.stack([key_grad, value_grad])
    n_pipe = lax.axis_size("pipe")
    n_tensor = lax.axis_size("tensor")
    me_pipe = lax.axis_index("pipe")
    axes = ("pipe", "tensor")

    def at(p, t):
        return p * n_tensor + t

    same_chip = lambda p, q: p // 2 == q // 2
    late = [q for q in range(2, n_pipe) if same_chip(q, q - 1)]
    early = [q for q in range(1, n_pipe) if q not in late]

    def swap(qs):
        return [(at(q, t), at(q, (t + 1) % n_tensor)) for q in qs for t in range(n_tensor)]

    def shift(qs):
        return [
            (at(q, t if same_chip(q, q - 1) else n_tensor - 1 - t), at(q - 1, t))
            for q in qs
            for t in range(n_tensor)
        ]

    def reduce_and_send(sections, chunks, gate=None, signal_at=None):
        rows = tok_rows // chunks
        exchange_pairs, shift_pairs = swap(sections), shift(sections)
        lowers, held, signal = [], None, None
        for c in range(chunks):
            sl = slice(c * rows, (c + 1) * rows)
            part = jnp.einsum(
                "wtc,wdc->td", both_grads[:, sl], both_full, preferred_element_type=jnp.float32
            )
            if gate is not None:
                part = part.at[0, 0].add(0.0 * gate[0, 0].astype(jnp.float32))
                gate = None
            part_low = part.astype(jnp.bfloat16)
            if held is not None:
                if len(lowers) > 0:
                    part_low, held, lowers[-1] = lax.optimization_barrier(
                        (part_low, held, lowers[-1])
                    )
                else:
                    part_low, held = lax.optimization_barrier((part_low, held))
                lowers.append(lax.ppermute(held, axes, shift_pairs))
            received = lax.ppermute(part_low, axes, exchange_pairs)
            if c == signal_at:
                signal = received[:8, :128]
            normed_grad = part_low.astype(jnp.float32) + received.astype(jnp.float32)
            held = norm_backward(normed_grad, gain_f, nhat[sl], inv_rms[sl])
        lowers.append(lax.ppermute(held, axes, shift_pairs))
        return jnp.concatenate(lowers, axis=0), signal

    first, signal = reduce_and_send(early, 4, signal_at=2)
    lower = first
    if late:
        release = [
            (at(q - 1, t), at(q, t)) for q in late for t in range(n_tensor)
        ]
        gate = lax.ppermute(signal, axes, release)
        second, _ = reduce_and_send(late, 2, gate=gate)
        from_late = functools.reduce(
            jnp.logical_or, [me_pipe == q - 1 for q in late], me_pipe < 0
        )
        lower = jnp.where(from_late, second, first)
    return (grad_total[:, :kv_cols][None], grad_total[:, kv_cols:][None], lower[None])


def solution(mesh):
    in_specs = (
        P("pipe", "dp", None),
        P("pipe", None),
        P("pipe", "dp", "tensor"),
        P("pipe", "dp", "tensor"),
        P("pipe", "dp", "tensor"),
        P("pipe", "dp", "tensor"),
        P("pipe", "dp"),
        P("pipe", "dp"),
        P("pipe", "dp"),
    )
    out_specs = (P("pipe", "dp", "tensor"), P("pipe", "dp", "tensor"), P("pipe", "dp", None))
    return jax.shard_map(
        on_device, mesh=mesh, in_specs=in_specs, out_specs=out_specs, check_vma=False
    )
```

```python
import math

import jax
import jax.numpy as jnp
from jax import lax
from jax.sharding import PartitionSpec as P

HD = 128


npo_beta = 0.1
norm_eps = 1e-05
rope_base = 500000.0


def shifted(value, axis, steps):
    count = lax.axis_size(axis)
    leading, last = (max(0, -steps), min(count, count - steps))
    return lax.ppermute(value, axis, [(source, source + steps) for source in range(leading, last)])


def rope_tables(length, head_dim):
    positions = jnp.arange(length).astype(jnp.float32)
    freq_index = jnp.arange(head_dim // 2).astype(jnp.float32)
    inverse = 1.0 / rope_base ** (2.0 * freq_index / head_dim)
    angles = positions[:, None] * inverse[None, :]
    cosine = jnp.concatenate([jnp.cos(angles), jnp.cos(angles)], axis=1)
    sine = jnp.concatenate([jnp.sin(angles), jnp.sin(angles)], axis=1)
    return (cosine, sine)


def rotate_half(values):
    half = values.shape[-1] // 2
    return jnp.concatenate([-values[..., half:], values[..., :half]], axis=-1)


def rotate_back(values):
    half = values.shape[-1] // 2
    return jnp.concatenate([values[..., half:], -values[..., :half]], axis=-1)


def sequence_grads(query_seq, key_seq, value_seq, cotan_seq, length_seq, cosine, sine):
    seq_len, kv_heads, head_dim = key_seq.shape
    group = query_seq.shape[1] // kv_heads
    scale = 1.0 / math.sqrt(head_dim)
    query_g = query_seq.reshape(seq_len, kv_heads, group, head_dim)
    cotan_g = cotan_seq.reshape(seq_len, kv_heads, group, head_dim)
    scores = (
        jnp.einsum("ikgd,jkd->kgij", query_g, key_seq, preferred_element_type=jnp.float32) * scale
    )
    row_pos = jnp.arange(seq_len)[:, None]
    col_pos = jnp.arange(seq_len)[None, :]
    allowed = (col_pos <= row_pos) & (col_pos < length_seq)
    scores = jnp.where(allowed, scores, -1e30)
    highest = jnp.max(scores, axis=-1, keepdims=True)
    expd = jnp.where(allowed, jnp.exp(scores - highest), 0.0)
    probs = expd / jnp.sum(expd, axis=-1, keepdims=True)
    probs_low = probs.astype(jnp.bfloat16)
    value_grad = jnp.einsum(
        "kgij,ikgd->jkd", probs_low, cotan_g, preferred_element_type=jnp.float32
    ).astype(jnp.bfloat16)
    prob_grad = jnp.einsum("ikgd,jkd->kgij", cotan_g, value_seq, preferred_element_type=jnp.float32)
    centre = jnp.sum(probs * prob_grad, axis=-1, keepdims=True)
    score_grad = (probs * (prob_grad - centre) * scale).astype(jnp.bfloat16)
    rotated_grad = jnp.einsum(
        "kgij,ikgd->jkd", score_grad, query_g, preferred_element_type=jnp.float32
    )
    key_grad = rotated_grad * cosine[:, None, :] + rotate_back(rotated_grad * sine[:, None, :])
    return (key_grad.astype(jnp.bfloat16), value_grad)


def norm_backward(normed_grad, gain_f, nhat, inv_rms):
    gain_grad_in = normed_grad * gain_f
    centre = jnp.mean(gain_grad_in * nhat, axis=-1, keepdims=True)
    return ((gain_grad_in - nhat * centre) * inv_rms).astype(jnp.bfloat16)


def on_device(
    hidden_states,
    norm_gain,
    key_weight,
    value_weight,
    queries,
    context_cotangent,
    lengths,
    policy_logp,
    reference_logp,
):
    both_full = lax.all_gather(
        jnp.stack([key_weight[0], value_weight[0]]), "dp", axis=1, tiled=True
    )
    key_full, value_full = both_full[0], both_full[1]
    hidden = hidden_states[0]
    gain_f = norm_gain[0].astype(jnp.float32)
    tok_rows = hidden.shape[0]
    seq_count = lengths.shape[1]
    seq_len = tok_rows // seq_count
    kv_cols = key_full.shape[1]
    kv_local = kv_cols // HD
    q_local = queries.shape[2] // HD
    hidden_f = hidden.astype(jnp.float32)
    inv_rms = lax.rsqrt(jnp.mean(hidden_f * hidden_f, axis=-1, keepdims=True) + norm_eps)
    nhat = hidden_f * inv_rms
    normed = (nhat * gain_f).astype(jnp.bfloat16)
    projected = jnp.einsum("td,wdc->wtc", normed, both_full, preferred_element_type=jnp.float32)
    key_raw = projected[0]
    values = projected[1].astype(jnp.bfloat16)
    cosine, sine = rope_tables(seq_len, HD)
    key_four = key_raw.reshape(seq_count, seq_len, kv_local, HD)
    keys = (
        key_four * cosine[None, :, None, :] + rotate_half(key_four) * sine[None, :, None, :]
    ).astype(jnp.bfloat16)
    total_seqs = seq_count * lax.axis_size("dp")
    seq_weight = 2.0 * jax.nn.sigmoid(npo_beta * (policy_logp[0] - reference_logp[0])) / total_seqs
    live = jnp.arange(seq_len)[None, :] < lengths[0][:, None]
    factor = jnp.where(live, seq_weight[:, None], 0.0)
    scaled = (
        context_cotangent[0].reshape(seq_count, seq_len, q_local, HD).astype(jnp.float32)
        * factor[:, :, None, None]
    ).astype(jnp.bfloat16)

    def one_sequence(items):
        return sequence_grads(items[0], items[1], items[2], items[3], items[4], cosine, sine)

    key_grad, value_grad = lax.map(
        one_sequence,
        (
            queries[0].reshape(seq_count, seq_len, q_local, HD),
            keys,
            values.reshape(seq_count, seq_len, kv_local, HD),
            scaled,
            lengths[0],
        ),
    )
    key_grad = key_grad.reshape(tok_rows, kv_cols)
    value_grad = value_grad.reshape(tok_rows, kv_cols)
    combined = jnp.concatenate([key_grad, value_grad], axis=1)
    grad_total = lax.psum_scatter(
        lax.dot_general(
            normed, combined, (((0,), (0,)), ((), ())), preferred_element_type=jnp.float32
        ).astype(jnp.bfloat16),
        "dp",
        scatter_dimension=0,
        tiled=True,
    )
    both_grads = jnp.stack([key_grad, value_grad])
    n_pipe = lax.axis_size("pipe")
    n_tensor = lax.axis_size("tensor")
    sizes = [tok_rows // 4, tok_rows * 5 // 16, tok_rows * 5 // 16, tok_rows // 8]
    bounds = [sum(sizes[:c]) for c in range(len(sizes) + 1)]
    chunks = len(sizes)
    exchange_steps = [
        [
            (p * n_tensor + t, p * n_tensor + (t + step) % n_tensor)
            for p in range(1, n_pipe)
            for t in range(n_tensor)
        ]
        for step in range(1, n_tensor)
    ]
    shift_pairs = [
        ((p + 1) * n_tensor + (t if (p + 1) // 2 == p // 2 else n_tensor - 1 - t), p * n_tensor + t)
        for p in range(n_pipe - 1)
        for t in range(n_tensor)
    ]
    lowers = []
    held = None
    for c in range(chunks):
        sl = slice(bounds[c], bounds[c + 1])
        part = jnp.einsum(
            "wtc,wdc->td", both_grads[:, sl], both_full, preferred_element_type=jnp.float32
        )
        part_low = part.astype(jnp.bfloat16)
        if held is not None:
            if len(lowers) > 0:
                part_low, held, lowers[-1] = lax.optimization_barrier(
                    (part_low, held, lowers[-1])
                )
            else:
                part_low, held = lax.optimization_barrier((part_low, held))
            lowers.append(lax.ppermute(held, ("pipe", "tensor"), shift_pairs))
        normed_grad = part_low.astype(jnp.float32)
        for pairs in exchange_steps:
            normed_grad = normed_grad + lax.ppermute(
                part_low, ("pipe", "tensor"), pairs
            ).astype(jnp.float32)
        held = norm_backward(normed_grad, gain_f, nhat[sl], inv_rms[sl])
    lowers.append(lax.ppermute(held, ("pipe", "tensor"), shift_pairs))
    lower = jnp.concatenate(lowers, axis=0)
    return (grad_total[:, :kv_cols][None], grad_total[:, kv_cols:][None], lower[None])


def solution(mesh):
    in_specs = (
        P("pipe", "dp", None),
        P("pipe", None),
        P("pipe", "dp", "tensor"),
        P("pipe", "dp", "tensor"),
        P("pipe", "dp", "tensor"),
        P("pipe", "dp", "tensor"),
        P("pipe", "dp"),
        P("pipe", "dp"),
        P("pipe", "dp"),
    )
    out_specs = (P("pipe", "dp", "tensor"), P("pipe", "dp", "tensor"), P("pipe", "dp", None))
    return jax.shard_map(
        on_device, mesh=mesh, in_specs=in_specs, out_specs=out_specs, check_vma=False
    )
```

```python
import functools
import math

import jax
import jax.numpy as jnp
from jax import lax
from jax.experimental import pallas as pl
from jax.experimental.pallas import tpu as pltpu
from jax.sharding import PartitionSpec as P

HD = 128


npo_beta = 0.1
norm_eps = 1e-05
rope_base = 500000.0


def shifted(value, axis, steps):
    count = lax.axis_size(axis)
    leading, last = (max(0, -steps), min(count, count - steps))
    return lax.ppermute(value, axis, [(source, source + steps) for source in range(leading, last)])


def rope_tables(length, head_dim):
    positions = jnp.arange(length).astype(jnp.float32)
    freq_index = jnp.arange(head_dim // 2).astype(jnp.float32)
    inverse = 1.0 / rope_base ** (2.0 * freq_index / head_dim)
    angles = positions[:, None] * inverse[None, :]
    cosine = jnp.concatenate([jnp.cos(angles), jnp.cos(angles)], axis=1)
    sine = jnp.concatenate([jnp.sin(angles), jnp.sin(angles)], axis=1)
    return (cosine, sine)


def rotate_half(values):
    half = values.shape[-1] // 2
    return jnp.concatenate([-values[..., half:], values[..., :half]], axis=-1)


def rotate_back(values):
    half = values.shape[-1] // 2
    return jnp.concatenate([values[..., half:], -values[..., :half]], axis=-1)


def sequence_grads(query_seq, key_seq, value_seq, cotan_seq, length_seq, cosine, sine):
    seq_len, kv_heads, head_dim = key_seq.shape
    group = query_seq.shape[1] // kv_heads
    scale = 1.0 / math.sqrt(head_dim)
    query_g = query_seq.reshape(seq_len, kv_heads, group, head_dim)
    cotan_g = cotan_seq.reshape(seq_len, kv_heads, group, head_dim)
    scores = (
        jnp.einsum("ikgd,jkd->kgij", query_g, key_seq, preferred_element_type=jnp.float32) * scale
    )
    row_pos = jnp.arange(seq_len)[:, None]
    col_pos = jnp.arange(seq_len)[None, :]
    allowed = (col_pos <= row_pos) & (col_pos < length_seq)
    scores = jnp.where(allowed, scores, -1e30)
    highest = jnp.max(scores, axis=-1, keepdims=True)
    expd = jnp.where(allowed, jnp.exp(scores - highest), 0.0)
    probs = expd / jnp.sum(expd, axis=-1, keepdims=True)
    probs_low = probs.astype(jnp.bfloat16)
    value_grad = jnp.einsum(
        "kgij,ikgd->jkd", probs_low, cotan_g, preferred_element_type=jnp.float32
    ).astype(jnp.bfloat16)
    prob_grad = jnp.einsum("ikgd,jkd->kgij", cotan_g, value_seq, preferred_element_type=jnp.float32)
    centre = jnp.sum(probs * prob_grad, axis=-1, keepdims=True)
    score_grad = (probs * (prob_grad - centre) * scale).astype(jnp.bfloat16)
    rotated_grad = jnp.einsum(
        "kgij,ikgd->jkd", score_grad, query_g, preferred_element_type=jnp.float32
    )
    key_grad = rotated_grad * cosine[:, None, :] + rotate_back(rotated_grad * sine[:, None, :])
    return (key_grad.astype(jnp.bfloat16), value_grad)


def attention_kernel(len_ref, q_ref, c_ref, k_ref, v_ref, rg_ref, vg_ref, *, group, head_dim):
    seq_len = k_ref.shape[0]
    scale = 1.0 / math.sqrt(head_dim)
    length = len_ref[0]
    keys = k_ref[...]
    values = v_ref[...]
    row = lax.broadcasted_iota(jnp.int32, (seq_len, seq_len), 0)
    col = lax.broadcasted_iota(jnp.int32, (seq_len, seq_len), 1)
    allowed = (col <= row) & (col < length)
    rotated = jnp.zeros((seq_len, head_dim), jnp.float32)
    value_grad = jnp.zeros((seq_len, head_dim), jnp.float32)
    nt = (((1,), (1,)), ((), ()))
    nn = (((1,), (0,)), ((), ()))
    for g in range(group):
        query = q_ref[:, g * head_dim:(g + 1) * head_dim]
        cotan = c_ref[:, g * head_dim:(g + 1) * head_dim]
        scores = lax.dot_general(query, keys, nt, preferred_element_type=jnp.float32) * scale
        scores = jnp.where(allowed, scores, -1e30)
        highest = jnp.max(scores, axis=-1, keepdims=True)
        expd = jnp.where(allowed, jnp.exp(scores - highest), 0.0)
        probs = expd / jnp.sum(expd, axis=-1, keepdims=True)
        value_grad = value_grad + lax.dot_general(
            probs.T.astype(jnp.bfloat16), cotan, nn, preferred_element_type=jnp.float32)
        prob_grad = lax.dot_general(cotan, values, nt, preferred_element_type=jnp.float32)
        centre = jnp.sum(probs * prob_grad, axis=-1, keepdims=True)
        score_grad = probs * (prob_grad - centre) * scale
        rotated = rotated + lax.dot_general(
            score_grad.T.astype(jnp.bfloat16), query, nn, preferred_element_type=jnp.float32)
    rg_ref[...] = rotated
    vg_ref[...] = value_grad.astype(jnp.bfloat16)

def attention_grads(length, queries, cotan, keys, values, head_dim):
    seq_len, kv_cols = keys.shape
    kv_heads = kv_cols // head_dim
    group = queries.shape[1] // kv_cols
    kernel = functools.partial(attention_kernel, group=group, head_dim=head_dim)
    q_spec = pl.BlockSpec((seq_len, group * head_dim), lambda k, n: (0, k))
    kv_spec = pl.BlockSpec((seq_len, head_dim), lambda k, n: (0, k))
    return pl.pallas_call(
        kernel,
        grid_spec=pltpu.PrefetchScalarGridSpec(
            num_scalar_prefetch=1, grid=(kv_heads,),
            in_specs=[q_spec, q_spec, kv_spec, kv_spec],
            out_specs=[kv_spec, kv_spec]),
        out_shape=[jax.ShapeDtypeStruct((seq_len, kv_cols), jnp.float32),
                   jax.ShapeDtypeStruct((seq_len, kv_cols), jnp.bfloat16)],
    )(length, queries, cotan, keys, values)


def norm_backward(normed_grad, gain_f, nhat, inv_rms):
    gain_grad_in = normed_grad * gain_f
    centre = jnp.mean(gain_grad_in * nhat, axis=-1, keepdims=True)
    return ((gain_grad_in - nhat * centre) * inv_rms).astype(jnp.bfloat16)


def on_device(
    hidden_states,
    norm_gain,
    key_weight,
    value_weight,
    queries,
    context_cotangent,
    lengths,
    policy_logp,
    reference_logp,
):
    both_full = lax.all_gather(
        jnp.stack([key_weight[0], value_weight[0]]), "dp", axis=1, tiled=True
    )
    key_full, value_full = both_full[0], both_full[1]
    hidden = hidden_states[0]
    gain_f = norm_gain[0].astype(jnp.float32)
    tok_rows = hidden.shape[0]
    seq_count = lengths.shape[1]
    seq_len = tok_rows // seq_count
    kv_cols = key_full.shape[1]
    kv_local = kv_cols // HD
    q_local = queries.shape[2] // HD
    hidden_f = hidden.astype(jnp.float32)
    inv_rms = lax.rsqrt(jnp.mean(hidden_f * hidden_f, axis=-1, keepdims=True) + norm_eps)
    nhat = hidden_f * inv_rms
    normed = (nhat * gain_f).astype(jnp.bfloat16)
    projected = jnp.einsum("td,wdc->wtc", normed, both_full, preferred_element_type=jnp.float32)
    key_raw = projected[0]
    values = projected[1].astype(jnp.bfloat16)
    cosine, sine = rope_tables(seq_len, HD)
    key_four = key_raw.reshape(seq_count, seq_len, kv_local, HD)
    keys = (
        key_four * cosine[None, :, None, :] + rotate_half(key_four) * sine[None, :, None, :]
    ).astype(jnp.bfloat16)
    total_seqs = seq_count * lax.axis_size("dp")
    seq_weight = 2.0 * jax.nn.sigmoid(npo_beta * (policy_logp[0] - reference_logp[0])) / total_seqs
    live = jnp.arange(seq_len)[None, :] < lengths[0][:, None]
    factor = jnp.where(live, seq_weight[:, None], 0.0)
    scaled = (
        context_cotangent[0].reshape(seq_count, seq_len, q_local, HD).astype(jnp.float32)
        * factor[:, :, None, None]
    ).astype(jnp.bfloat16)

    key_parts, value_parts = [], []
    for n in range(seq_count):
        rows_n = slice(n * seq_len, (n + 1) * seq_len)
        rotated, value_part = attention_grads(
            lengths[0][n:n + 1],
            queries[0][rows_n],
            scaled[n].reshape(seq_len, q_local * HD),
            keys[n].reshape(seq_len, kv_cols),
            values[rows_n],
            HD,
        )
        rotated = rotated.reshape(seq_len, kv_local, HD)
        key_part = rotated * cosine[:, None, :] + rotate_back(rotated * sine[:, None, :])
        key_parts.append(key_part.astype(jnp.bfloat16))
        value_parts.append(value_part)
    key_grad = jnp.concatenate(key_parts, axis=0)
    value_grad = jnp.concatenate(value_parts, axis=0)
    key_grad = key_grad.reshape(tok_rows, kv_cols)
    value_grad = value_grad.reshape(tok_rows, kv_cols)
    combined = jnp.concatenate([key_grad, value_grad], axis=1)
    grad_total = lax.psum_scatter(
        lax.dot_general(
            normed, combined, (((0,), (0,)), ((), ())), preferred_element_type=jnp.float32
        ).astype(jnp.bfloat16),
        "dp",
        scatter_dimension=0,
        tiled=True,
    )
    both_grads = jnp.stack([key_grad, value_grad])
    n_pipe = lax.axis_size("pipe")
    n_tensor = lax.axis_size("tensor")
    sizes = [tok_rows // 4, tok_rows * 5 // 16, tok_rows * 5 // 16, tok_rows // 8]
    bounds = [sum(sizes[:c]) for c in range(len(sizes) + 1)]
    chunks = len(sizes)
    exchange_steps = [
        [
            (p * n_tensor + t, p * n_tensor + (t + step) % n_tensor)
            for p in range(1, n_pipe)
            for t in range(n_tensor)
        ]
        for step in range(1, n_tensor)
    ]
    shift_pairs = [
        ((p + 1) * n_tensor + (t if (p + 1) // 2 == p // 2 else n_tensor - 1 - t), p * n_tensor + t)
        for p in range(n_pipe - 1)
        for t in range(n_tensor)
    ]
    lowers = []
    held = None
    for c in range(chunks):
        sl = slice(bounds[c], bounds[c + 1])
        part = jnp.einsum(
            "wtc,wdc->td", both_grads[:, sl], both_full, preferred_element_type=jnp.float32
        )
        part_low = part.astype(jnp.bfloat16)
        if held is not None:
            if len(lowers) > 0:
                part_low, held, lowers[-1] = lax.optimization_barrier(
                    (part_low, held, lowers[-1])
                )
            else:
                part_low, held = lax.optimization_barrier((part_low, held))
            lowers.append(lax.ppermute(held, ("pipe", "tensor"), shift_pairs))
        normed_grad = part_low.astype(jnp.float32)
        for pairs in exchange_steps:
            normed_grad = normed_grad + lax.ppermute(
                part_low, ("pipe", "tensor"), pairs
            ).astype(jnp.float32)
        held = norm_backward(normed_grad, gain_f, nhat[sl], inv_rms[sl])
    lowers.append(lax.ppermute(held, ("pipe", "tensor"), shift_pairs))
    lower = jnp.concatenate(lowers, axis=0)
    return (grad_total[:, :kv_cols][None], grad_total[:, kv_cols:][None], lower[None])


def solution(mesh):
    in_specs = (
        P("pipe", "dp", None),
        P("pipe", None),
        P("pipe", "dp", "tensor"),
        P("pipe", "dp", "tensor"),
        P("pipe", "dp", "tensor"),
        P("pipe", "dp", "tensor"),
        P("pipe", "dp"),
        P("pipe", "dp"),
        P("pipe", "dp"),
    )
    out_specs = (P("pipe", "dp", "tensor"), P("pipe", "dp", "tensor"), P("pipe", "dp", None))
    return jax.shard_map(
        on_device, mesh=mesh, in_specs=in_specs, out_specs=out_specs, check_vma=False
    )
```

```python
import functools
import math

import jax
import jax.numpy as jnp
from jax import lax
from jax.experimental import pallas as pl
from jax.experimental.pallas import tpu as pltpu
from jax.sharding import PartitionSpec as P

HD = 128


npo_beta = 0.1
norm_eps = 1e-05
rope_base = 500000.0


def shifted(value, axis, steps):
    count = lax.axis_size(axis)
    leading, last = (max(0, -steps), min(count, count - steps))
    return lax.ppermute(value, axis, [(source, source + steps) for source in range(leading, last)])


def rope_tables(length, head_dim):
    positions = jnp.arange(length).astype(jnp.float32)
    freq_index = jnp.arange(head_dim // 2).astype(jnp.float32)
    inverse = 1.0 / rope_base ** (2.0 * freq_index / head_dim)
    angles = positions[:, None] * inverse[None, :]
    cosine = jnp.concatenate([jnp.cos(angles), jnp.cos(angles)], axis=1)
    sine = jnp.concatenate([jnp.sin(angles), jnp.sin(angles)], axis=1)
    return (cosine, sine)


def rotate_half(values):
    half = values.shape[-1] // 2
    return jnp.concatenate([-values[..., half:], values[..., :half]], axis=-1)


def rotate_back(values):
    half = values.shape[-1] // 2
    return jnp.concatenate([values[..., half:], -values[..., :half]], axis=-1)


def sequence_grads(query_seq, key_seq, value_seq, cotan_seq, length_seq, cosine, sine):
    seq_len, kv_heads, head_dim = key_seq.shape
    group = query_seq.shape[1] // kv_heads
    scale = 1.0 / math.sqrt(head_dim)
    query_g = query_seq.reshape(seq_len, kv_heads, group, head_dim)
    cotan_g = cotan_seq.reshape(seq_len, kv_heads, group, head_dim)
    scores = (
        jnp.einsum("ikgd,jkd->kgij", query_g, key_seq, preferred_element_type=jnp.float32) * scale
    )
    row_pos = jnp.arange(seq_len)[:, None]
    col_pos = jnp.arange(seq_len)[None, :]
    allowed = (col_pos <= row_pos) & (col_pos < length_seq)
    scores = jnp.where(allowed, scores, -1e30)
    highest = jnp.max(scores, axis=-1, keepdims=True)
    expd = jnp.where(allowed, jnp.exp(scores - highest), 0.0)
    probs = expd / jnp.sum(expd, axis=-1, keepdims=True)
    probs_low = probs.astype(jnp.bfloat16)
    value_grad = jnp.einsum(
        "kgij,ikgd->jkd", probs_low, cotan_g, preferred_element_type=jnp.float32
    ).astype(jnp.bfloat16)
    prob_grad = jnp.einsum("ikgd,jkd->kgij", cotan_g, value_seq, preferred_element_type=jnp.float32)
    centre = jnp.sum(probs * prob_grad, axis=-1, keepdims=True)
    score_grad = (probs * (prob_grad - centre) * scale).astype(jnp.bfloat16)
    rotated_grad = jnp.einsum(
        "kgij,ikgd->jkd", score_grad, query_g, preferred_element_type=jnp.float32
    )
    key_grad = rotated_grad * cosine[:, None, :] + rotate_back(rotated_grad * sine[:, None, :])
    return (key_grad.astype(jnp.bfloat16), value_grad)


def attention_kernel(len_ref, q_ref, c_ref, k_ref, v_ref, rg_ref, vg_ref, *, group, head_dim):
    seq_len = k_ref.shape[0]
    scale = 1.0 / math.sqrt(head_dim)
    length = len_ref[0]
    keys = k_ref[...]
    values = v_ref[...]
    row = lax.broadcasted_iota(jnp.int32, (seq_len, seq_len), 0)
    col = lax.broadcasted_iota(jnp.int32, (seq_len, seq_len), 1)
    allowed = (col <= row) & (col < length)
    rotated = jnp.zeros((seq_len, head_dim), jnp.float32)
    value_grad = jnp.zeros((seq_len, head_dim), jnp.float32)
    nt = (((1,), (1,)), ((), ()))
    nn = (((1,), (0,)), ((), ()))
    for g in range(group):
        query = q_ref[:, g * head_dim:(g + 1) * head_dim]
        cotan = c_ref[:, g * head_dim:(g + 1) * head_dim]
        scores = lax.dot_general(query, keys, nt, preferred_element_type=jnp.float32) * scale
        scores = jnp.where(allowed, scores, -1e30)
        highest = jnp.max(scores, axis=-1, keepdims=True)
        expd = jnp.where(allowed, jnp.exp(scores - highest), 0.0)
        probs = expd / jnp.sum(expd, axis=-1, keepdims=True)
        value_grad = value_grad + lax.dot_general(
            probs.T.astype(jnp.bfloat16), cotan, nn, preferred_element_type=jnp.float32)
        prob_grad = lax.dot_general(cotan, values, nt, preferred_element_type=jnp.float32)
        centre = jnp.sum(probs * prob_grad, axis=-1, keepdims=True)
        score_grad = probs * (prob_grad - centre) * scale
        rotated = rotated + lax.dot_general(
            score_grad.T.astype(jnp.bfloat16), query, nn, preferred_element_type=jnp.float32)
    rg_ref[...] = rotated
    vg_ref[...] = value_grad.astype(jnp.bfloat16)

def attention_grads(length, queries, cotan, keys, values, head_dim):
    seq_len, kv_cols = keys.shape
    kv_heads = kv_cols // head_dim
    group = queries.shape[1] // kv_cols
    kernel = functools.partial(attention_kernel, group=group, head_dim=head_dim)
    q_spec = pl.BlockSpec((seq_len, group * head_dim), lambda k, n: (0, k))
    kv_spec = pl.BlockSpec((seq_len, head_dim), lambda k, n: (0, k))
    return pl.pallas_call(
        kernel,
        grid_spec=pltpu.PrefetchScalarGridSpec(
            num_scalar_prefetch=1, grid=(kv_heads,),
            in_specs=[q_spec, q_spec, kv_spec, kv_spec],
            out_specs=[kv_spec, kv_spec]),
        out_shape=[jax.ShapeDtypeStruct((seq_len, kv_cols), jnp.float32),
                   jax.ShapeDtypeStruct((seq_len, kv_cols), jnp.bfloat16)],
    )(length, queries, cotan, keys, values)


def norm_backward(normed_grad, gain_f, nhat, inv_rms):
    gain_grad_in = normed_grad * gain_f
    centre = jnp.mean(gain_grad_in * nhat, axis=-1, keepdims=True)
    return ((gain_grad_in - nhat * centre) * inv_rms).astype(jnp.bfloat16)


def on_device(
    hidden_states,
    norm_gain,
    key_weight,
    value_weight,
    queries,
    context_cotangent,
    lengths,
    policy_logp,
    reference_logp,
):
    both_full = lax.all_gather(
        jnp.stack([key_weight[0], value_weight[0]]), "dp", axis=1, tiled=True
    )
    key_full, value_full = both_full[0], both_full[1]
    hidden = hidden_states[0]
    gain_f = norm_gain[0].astype(jnp.float32)
    tok_rows = hidden.shape[0]
    seq_count = lengths.shape[1]
    seq_len = tok_rows // seq_count
    kv_cols = key_full.shape[1]
    kv_local = kv_cols // HD
    q_local = queries.shape[2] // HD
    hidden_f = hidden.astype(jnp.float32)
    inv_rms = lax.rsqrt(jnp.mean(hidden_f * hidden_f, axis=-1, keepdims=True) + norm_eps)
    nhat = hidden_f * inv_rms
    normed = (nhat * gain_f).astype(jnp.bfloat16)
    projected = jnp.einsum("td,wdc->wtc", normed, both_full, preferred_element_type=jnp.float32)
    key_raw = projected[0]
    values = projected[1].astype(jnp.bfloat16)
    cosine, sine = rope_tables(seq_len, HD)
    key_four = key_raw.reshape(seq_count, seq_len, kv_local, HD)
    keys = (
        key_four * cosine[None, :, None, :] + rotate_half(key_four) * sine[None, :, None, :]
    ).astype(jnp.bfloat16)
    total_seqs = seq_count * lax.axis_size("dp")
    seq_weight = 2.0 * jax.nn.sigmoid(npo_beta * (policy_logp[0] - reference_logp[0])) / total_seqs
    live = jnp.arange(seq_len)[None, :] < lengths[0][:, None]
    factor = jnp.where(live, seq_weight[:, None], 0.0)
    scaled = (
        context_cotangent[0].reshape(seq_count, seq_len, q_local, HD).astype(jnp.float32)
        * factor[:, :, None, None]
    ).astype(jnp.bfloat16)

    key_parts, value_parts = [], []
    for n in range(seq_count):
        rows_n = slice(n * seq_len, (n + 1) * seq_len)
        rotated, value_part = attention_grads(
            lengths[0][n:n + 1],
            queries[0][rows_n],
            scaled[n].reshape(seq_len, q_local * HD),
            keys[n].reshape(seq_len, kv_cols),
            values[rows_n],
            HD,
        )
        rotated = rotated.reshape(seq_len, kv_local, HD)
        key_part = rotated * cosine[:, None, :] + rotate_back(rotated * sine[:, None, :])
        key_parts.append(key_part.astype(jnp.bfloat16))
        value_parts.append(value_part)
    key_grad = jnp.concatenate(key_parts, axis=0)
    value_grad = jnp.concatenate(value_parts, axis=0)
    key_grad = key_grad.reshape(tok_rows, kv_cols)
    value_grad = value_grad.reshape(tok_rows, kv_cols)
    combined = jnp.concatenate([key_grad, value_grad], axis=1)

    def weight_grads(combined):
        return lax.psum_scatter(
            lax.dot_general(
                normed, combined, (((0,), (0,)), ((), ())), preferred_element_type=jnp.float32
            ).astype(jnp.bfloat16),
            "dp",
            scatter_dimension=0,
            tiled=True,
        )

    both_grads = jnp.stack([key_grad, value_grad])
    n_pipe = lax.axis_size("pipe")
    n_tensor = lax.axis_size("tensor")
    sizes = [tok_rows // 4, tok_rows * 5 // 16, tok_rows * 5 // 16, tok_rows // 8]
    bounds = [sum(sizes[:c]) for c in range(len(sizes) + 1)]
    chunks = len(sizes)
    exchange_steps = [
        [
            (p * n_tensor + t, p * n_tensor + (t + step) % n_tensor)
            for p in range(1, n_pipe)
            for t in range(n_tensor)
        ]
        for step in range(1, n_tensor)
    ]
    shift_pairs = [
        ((p + 1) * n_tensor + (t if (p + 1) // 2 == p // 2 else n_tensor - 1 - t), p * n_tensor + t)
        for p in range(n_pipe - 1)
        for t in range(n_tensor)
    ]
    lowers = []
    held = None
    for c in range(chunks):
        sl = slice(bounds[c], bounds[c + 1])
        part = jnp.einsum(
            "wtc,wdc->td", both_grads[:, sl], both_full, preferred_element_type=jnp.float32
        )
        part_low = part.astype(jnp.bfloat16)
        if c == 0:
            part_low, combined = lax.optimization_barrier((part_low, combined))
            grad_total = weight_grads(combined)
        if held is not None:
            if len(lowers) > 0:
                part_low, held, lowers[-1] = lax.optimization_barrier(
                    (part_low, held, lowers[-1])
                )
            else:
                part_low, held = lax.optimization_barrier((part_low, held))
            lowers.append(lax.ppermute(held, ("pipe", "tensor"), shift_pairs))
        normed_grad = part_low.astype(jnp.float32)
        for pairs in exchange_steps:
            normed_grad = normed_grad + lax.ppermute(
                part_low, ("pipe", "tensor"), pairs
            ).astype(jnp.float32)
        held = norm_backward(normed_grad, gain_f, nhat[sl], inv_rms[sl])
    lowers.append(lax.ppermute(held, ("pipe", "tensor"), shift_pairs))
    lower = jnp.concatenate(lowers, axis=0)
    return (grad_total[:, :kv_cols][None], grad_total[:, kv_cols:][None], lower[None])


def solution(mesh):
    in_specs = (
        P("pipe", "dp", None),
        P("pipe", None),
        P("pipe", "dp", "tensor"),
        P("pipe", "dp", "tensor"),
        P("pipe", "dp", "tensor"),
        P("pipe", "dp", "tensor"),
        P("pipe", "dp"),
        P("pipe", "dp"),
        P("pipe", "dp"),
    )
    out_specs = (P("pipe", "dp", "tensor"), P("pipe", "dp", "tensor"), P("pipe", "dp", None))
    return jax.shard_map(
        on_device, mesh=mesh, in_specs=in_specs, out_specs=out_specs, check_vma=False
    )
```

```python
import functools
import math

import jax
import jax.numpy as jnp
from jax import lax
from jax.experimental import pallas as pl
from jax.experimental.pallas import tpu as pltpu
from jax.sharding import PartitionSpec as P

HD = 128


npo_beta = 0.1
norm_eps = 1e-05
rope_base = 500000.0


def shifted(value, axis, steps):
    count = lax.axis_size(axis)
    leading, last = (max(0, -steps), min(count, count - steps))
    return lax.ppermute(value, axis, [(source, source + steps) for source in range(leading, last)])


def rope_tables(length, head_dim):
    positions = jnp.arange(length).astype(jnp.float32)
    freq_index = jnp.arange(head_dim // 2).astype(jnp.float32)
    inverse = 1.0 / rope_base ** (2.0 * freq_index / head_dim)
    angles = positions[:, None] * inverse[None, :]
    cosine = jnp.concatenate([jnp.cos(angles), jnp.cos(angles)], axis=1)
    sine = jnp.concatenate([jnp.sin(angles), jnp.sin(angles)], axis=1)
    return (cosine, sine)


def rotate_half(values):
    half = values.shape[-1] // 2
    return jnp.concatenate([-values[..., half:], values[..., :half]], axis=-1)


def rotate_back(values):
    half = values.shape[-1] // 2
    return jnp.concatenate([values[..., half:], -values[..., :half]], axis=-1)


def sequence_grads(query_seq, key_seq, value_seq, cotan_seq, length_seq, cosine, sine):
    seq_len, kv_heads, head_dim = key_seq.shape
    group = query_seq.shape[1] // kv_heads
    scale = 1.0 / math.sqrt(head_dim)
    query_g = query_seq.reshape(seq_len, kv_heads, group, head_dim)
    cotan_g = cotan_seq.reshape(seq_len, kv_heads, group, head_dim)
    scores = (
        jnp.einsum("ikgd,jkd->kgij", query_g, key_seq, preferred_element_type=jnp.float32) * scale
    )
    row_pos = jnp.arange(seq_len)[:, None]
    col_pos = jnp.arange(seq_len)[None, :]
    allowed = (col_pos <= row_pos) & (col_pos < length_seq)
    scores = jnp.where(allowed, scores, -1e30)
    highest = jnp.max(scores, axis=-1, keepdims=True)
    expd = jnp.where(allowed, jnp.exp(scores - highest), 0.0)
    probs = expd / jnp.sum(expd, axis=-1, keepdims=True)
    probs_low = probs.astype(jnp.bfloat16)
    value_grad = jnp.einsum(
        "kgij,ikgd->jkd", probs_low, cotan_g, preferred_element_type=jnp.float32
    ).astype(jnp.bfloat16)
    prob_grad = jnp.einsum("ikgd,jkd->kgij", cotan_g, value_seq, preferred_element_type=jnp.float32)
    centre = jnp.sum(probs * prob_grad, axis=-1, keepdims=True)
    score_grad = (probs * (prob_grad - centre) * scale).astype(jnp.bfloat16)
    rotated_grad = jnp.einsum(
        "kgij,ikgd->jkd", score_grad, query_g, preferred_element_type=jnp.float32
    )
    key_grad = rotated_grad * cosine[:, None, :] + rotate_back(rotated_grad * sine[:, None, :])
    return (key_grad.astype(jnp.bfloat16), value_grad)


def attention_kernel(len_ref, q_ref, c_ref, k_ref, v_ref, rg_ref, vg_ref, *, group, head_dim):
    seq_len = k_ref.shape[0]
    scale = 1.0 / math.sqrt(head_dim)
    length = len_ref[0]
    keys = k_ref[...]
    values = v_ref[...]
    row = lax.broadcasted_iota(jnp.int32, (seq_len, seq_len), 0)
    col = lax.broadcasted_iota(jnp.int32, (seq_len, seq_len), 1)
    allowed = (col <= row) & (col < length)
    rotated = jnp.zeros((seq_len, head_dim), jnp.float32)
    value_grad = jnp.zeros((seq_len, head_dim), jnp.float32)
    nt = (((1,), (1,)), ((), ()))
    nn = (((1,), (0,)), ((), ()))
    for g in range(group):
        query = q_ref[:, g * head_dim:(g + 1) * head_dim]
        cotan = c_ref[:, g * head_dim:(g + 1) * head_dim]
        scores = lax.dot_general(query, keys, nt, preferred_element_type=jnp.float32) * scale
        scores = jnp.where(allowed, scores, -1e30)
        highest = jnp.max(scores, axis=-1, keepdims=True)
        expd = jnp.where(allowed, jnp.exp(scores - highest), 0.0)
        probs = expd / jnp.sum(expd, axis=-1, keepdims=True)
        value_grad = value_grad + lax.dot_general(
            probs.T.astype(jnp.bfloat16), cotan, nn, preferred_element_type=jnp.float32)
        prob_grad = lax.dot_general(cotan, values, nt, preferred_element_type=jnp.float32)
        centre = jnp.sum(probs * prob_grad, axis=-1, keepdims=True)
        score_grad = probs * (prob_grad - centre) * scale
        rotated = rotated + lax.dot_general(
            score_grad.T.astype(jnp.bfloat16), query, nn, preferred_element_type=jnp.float32)
    rg_ref[...] = rotated
    vg_ref[...] = value_grad.astype(jnp.bfloat16)

def attention_grads(length, queries, cotan, keys, values, head_dim):
    seq_len, kv_cols = keys.shape
    kv_heads = kv_cols // head_dim
    group = queries.shape[1] // kv_cols
    kernel = functools.partial(attention_kernel, group=group, head_dim=head_dim)
    q_spec = pl.BlockSpec((seq_len, group * head_dim), lambda k, n: (0, k))
    kv_spec = pl.BlockSpec((seq_len, head_dim), lambda k, n: (0, k))
    return pl.pallas_call(
        kernel,
        grid_spec=pltpu.PrefetchScalarGridSpec(
            num_scalar_prefetch=1, grid=(kv_heads,),
            in_specs=[q_spec, q_spec, kv_spec, kv_spec],
            out_specs=[kv_spec, kv_spec]),
        out_shape=[jax.ShapeDtypeStruct((seq_len, kv_cols), jnp.float32),
                   jax.ShapeDtypeStruct((seq_len, kv_cols), jnp.bfloat16)],
    )(length, queries, cotan, keys, values)


def norm_backward(normed_grad, gain_f, nhat, inv_rms):
    gain_grad_in = normed_grad * gain_f
    centre = jnp.mean(gain_grad_in * nhat, axis=-1, keepdims=True)
    return ((gain_grad_in - nhat * centre) * inv_rms).astype(jnp.bfloat16)


def on_device(
    hidden_states,
    norm_gain,
    key_weight,
    value_weight,
    queries,
    context_cotangent,
    lengths,
    policy_logp,
    reference_logp,
):
    both_full = lax.all_gather(
        jnp.concatenate([key_weight[0], value_weight[0]], axis=1), "dp", axis=0, tiled=True
    )
    kv_cols = key_weight.shape[2]
    hidden = hidden_states[0]
    gain_f = norm_gain[0].astype(jnp.float32)
    tok_rows = hidden.shape[0]
    seq_count = lengths.shape[1]
    seq_len = tok_rows // seq_count
    kv_local = kv_cols // HD
    q_local = queries.shape[2] // HD
    hidden_f = hidden.astype(jnp.float32)
    inv_rms = lax.rsqrt(jnp.mean(hidden_f * hidden_f, axis=-1, keepdims=True) + norm_eps)
    nhat = hidden_f * inv_rms
    normed = (nhat * gain_f).astype(jnp.bfloat16)
    projected = jnp.dot(normed, both_full, preferred_element_type=jnp.float32)
    key_raw = projected[:, :kv_cols]
    values = projected[:, kv_cols:].astype(jnp.bfloat16)
    cosine, sine = rope_tables(seq_len, HD)
    key_four = key_raw.reshape(seq_count, seq_len, kv_local, HD)
    keys = (
        key_four * cosine[None, :, None, :] + rotate_half(key_four) * sine[None, :, None, :]
    ).astype(jnp.bfloat16)
    total_seqs = seq_count * lax.axis_size("dp")
    seq_weight = 2.0 * jax.nn.sigmoid(npo_beta * (policy_logp[0] - reference_logp[0])) / total_seqs
    live = jnp.arange(seq_len)[None, :] < lengths[0][:, None]
    factor = jnp.where(live, seq_weight[:, None], 0.0)
    scaled = (
        context_cotangent[0].reshape(seq_count, seq_len, q_local, HD).astype(jnp.float32)
        * factor[:, :, None, None]
    ).astype(jnp.bfloat16)

    key_parts, value_parts = [], []
    for n in range(seq_count):
        rows_n = slice(n * seq_len, (n + 1) * seq_len)
        rotated, value_part = attention_grads(
            lengths[0][n:n + 1],
            queries[0][rows_n],
            scaled[n].reshape(seq_len, q_local * HD),
            keys[n].reshape(seq_len, kv_cols),
            values[rows_n],
            HD,
        )
        rotated = rotated.reshape(seq_len, kv_local, HD)
        key_part = rotated * cosine[:, None, :] + rotate_back(rotated * sine[:, None, :])
        key_parts.append(key_part.astype(jnp.bfloat16))
        value_parts.append(value_part)
    key_grad = jnp.concatenate(key_parts, axis=0)
    value_grad = jnp.concatenate(value_parts, axis=0)
    key_grad = key_grad.reshape(tok_rows, kv_cols)
    value_grad = value_grad.reshape(tok_rows, kv_cols)
    combined = jnp.concatenate([key_grad, value_grad], axis=1)

    def weight_grads(combined):
        return lax.psum_scatter(
            lax.dot_general(
                normed, combined, (((0,), (0,)), ((), ())), preferred_element_type=jnp.float32
            ).astype(jnp.bfloat16),
            "dp",
            scatter_dimension=0,
            tiled=True,
        )

    n_pipe = lax.axis_size("pipe")
    n_tensor = lax.axis_size("tensor")
    sizes = [tok_rows // 4, tok_rows * 5 // 16, tok_rows * 5 // 16, tok_rows // 8]
    bounds = [sum(sizes[:c]) for c in range(len(sizes) + 1)]
    chunks = len(sizes)
    exchange_steps = [
        [
            (p * n_tensor + t, p * n_tensor + (t + step) % n_tensor)
            for p in range(1, n_pipe)
            for t in range(n_tensor)
        ]
        for step in range(1, n_tensor)
    ]
    shift_pairs = [
        ((p + 1) * n_tensor + (t if (p + 1) // 2 == p // 2 else n_tensor - 1 - t), p * n_tensor + t)
        for p in range(n_pipe - 1)
        for t in range(n_tensor)
    ]
    lowers = []
    held = None
    for c in range(chunks):
        sl = slice(bounds[c], bounds[c + 1])
        part = lax.dot_general(
            combined[sl], both_full, (((1,), (1,)), ((), ())), preferred_element_type=jnp.float32
        )
        part_low = part.astype(jnp.bfloat16)
        if c == 0:
            part_low, combined = lax.optimization_barrier((part_low, combined))
            grad_total = weight_grads(combined)
        if held is not None:
            if len(lowers) > 0:
                part_low, held, lowers[-1] = lax.optimization_barrier(
                    (part_low, held, lowers[-1])
                )
            else:
                part_low, held = lax.optimization_barrier((part_low, held))
            lowers.append(lax.ppermute(held, ("pipe", "tensor"), shift_pairs))
        normed_grad = part_low.astype(jnp.float32)
        for pairs in exchange_steps:
            normed_grad = normed_grad + lax.ppermute(
                part_low, ("pipe", "tensor"), pairs
            ).astype(jnp.float32)
        held = norm_backward(normed_grad, gain_f, nhat[sl], inv_rms[sl])
    lowers.append(lax.ppermute(held, ("pipe", "tensor"), shift_pairs))
    lower = jnp.concatenate(lowers, axis=0)
    return (grad_total[:, :kv_cols][None], grad_total[:, kv_cols:][None], lower[None])


def solution(mesh):
    in_specs = (
        P("pipe", "dp", None),
        P("pipe", None),
        P("pipe", "dp", "tensor"),
        P("pipe", "dp", "tensor"),
        P("pipe", "dp", "tensor"),
        P("pipe", "dp", "tensor"),
        P("pipe", "dp"),
        P("pipe", "dp"),
        P("pipe", "dp"),
    )
    out_specs = (P("pipe", "dp", "tensor"), P("pipe", "dp", "tensor"), P("pipe", "dp", None))
    return jax.shard_map(
        on_device, mesh=mesh, in_specs=in_specs, out_specs=out_specs, check_vma=False
    )
```

```python
import functools
import math

import jax
import jax.numpy as jnp
from jax import lax
from jax.experimental import pallas as pl
from jax.experimental.pallas import tpu as pltpu
from jax.sharding import PartitionSpec as P

HD = 128


npo_beta = 0.1
norm_eps = 1e-05
rope_base = 500000.0


def shifted(value, axis, steps):
    count = lax.axis_size(axis)
    leading, last = (max(0, -steps), min(count, count - steps))
    return lax.ppermute(value, axis, [(source, source + steps) for source in range(leading, last)])


def rope_tables(length, head_dim):
    positions = jnp.arange(length).astype(jnp.float32)
    freq_index = jnp.arange(head_dim // 2).astype(jnp.float32)
    inverse = 1.0 / rope_base ** (2.0 * freq_index / head_dim)
    angles = positions[:, None] * inverse[None, :]
    cosine = jnp.concatenate([jnp.cos(angles), jnp.cos(angles)], axis=1)
    sine = jnp.concatenate([jnp.sin(angles), jnp.sin(angles)], axis=1)
    return (cosine, sine)


def rotate_half(values):
    half = values.shape[-1] // 2
    return jnp.concatenate([-values[..., half:], values[..., :half]], axis=-1)


def rotate_back(values):
    half = values.shape[-1] // 2
    return jnp.concatenate([values[..., half:], -values[..., :half]], axis=-1)


def sequence_grads(query_seq, key_seq, value_seq, cotan_seq, length_seq, cosine, sine):
    seq_len, kv_heads, head_dim = key_seq.shape
    group = query_seq.shape[1] // kv_heads
    scale = 1.0 / math.sqrt(head_dim)
    query_g = query_seq.reshape(seq_len, kv_heads, group, head_dim)
    cotan_g = cotan_seq.reshape(seq_len, kv_heads, group, head_dim)
    scores = (
        jnp.einsum("ikgd,jkd->kgij", query_g, key_seq, preferred_element_type=jnp.float32) * scale
    )
    row_pos = jnp.arange(seq_len)[:, None]
    col_pos = jnp.arange(seq_len)[None, :]
    allowed = (col_pos <= row_pos) & (col_pos < length_seq)
    scores = jnp.where(allowed, scores, -1e30)
    highest = jnp.max(scores, axis=-1, keepdims=True)
    expd = jnp.where(allowed, jnp.exp(scores - highest), 0.0)
    probs = expd / jnp.sum(expd, axis=-1, keepdims=True)
    probs_low = probs.astype(jnp.bfloat16)
    value_grad = jnp.einsum(
        "kgij,ikgd->jkd", probs_low, cotan_g, preferred_element_type=jnp.float32
    ).astype(jnp.bfloat16)
    prob_grad = jnp.einsum("ikgd,jkd->kgij", cotan_g, value_seq, preferred_element_type=jnp.float32)
    centre = jnp.sum(probs * prob_grad, axis=-1, keepdims=True)
    score_grad = (probs * (prob_grad - centre) * scale).astype(jnp.bfloat16)
    rotated_grad = jnp.einsum(
        "kgij,ikgd->jkd", score_grad, query_g, preferred_element_type=jnp.float32
    )
    key_grad = rotated_grad * cosine[:, None, :] + rotate_back(rotated_grad * sine[:, None, :])
    return (key_grad.astype(jnp.bfloat16), value_grad)


def attention_kernel(len_ref, q_ref, c_ref, k_ref, v_ref, rg_ref, vg_ref, *, group, head_dim):
    seq_len = k_ref.shape[0]
    scale = 1.0 / math.sqrt(head_dim)
    length = len_ref[0]
    keys = k_ref[...]
    values = v_ref[...]
    row = lax.broadcasted_iota(jnp.int32, (seq_len, seq_len), 0)
    col = lax.broadcasted_iota(jnp.int32, (seq_len, seq_len), 1)
    allowed = (col <= row) & (col < length)
    rotated = jnp.zeros((seq_len, head_dim), jnp.float32)
    value_grad = jnp.zeros((seq_len, head_dim), jnp.float32)
    nt = (((1,), (1,)), ((), ()))
    nn = (((1,), (0,)), ((), ()))
    for g in range(group):
        query = q_ref[:, g * head_dim:(g + 1) * head_dim]
        cotan = c_ref[:, g * head_dim:(g + 1) * head_dim]
        scores = lax.dot_general(query, keys, nt, preferred_element_type=jnp.float32) * scale
        scores = jnp.where(allowed, scores, -1e30)
        highest = jnp.max(scores, axis=-1, keepdims=True)
        expd = jnp.where(allowed, jnp.exp(scores - highest), 0.0)
        probs = expd / jnp.sum(expd, axis=-1, keepdims=True)
        value_grad = value_grad + lax.dot_general(
            probs.T.astype(jnp.bfloat16), cotan, nn, preferred_element_type=jnp.float32)
        prob_grad = lax.dot_general(cotan, values, nt, preferred_element_type=jnp.float32)
        centre = jnp.sum(probs * prob_grad, axis=-1, keepdims=True)
        score_grad = probs * (prob_grad - centre) * scale
        rotated = rotated + lax.dot_general(
            score_grad.T.astype(jnp.bfloat16), query, nn, preferred_element_type=jnp.float32)
    rg_ref[...] = rotated
    vg_ref[...] = value_grad.astype(jnp.bfloat16)

def attention_grads(length, queries, cotan, keys, values, head_dim):
    seq_len, kv_cols = keys.shape
    kv_heads = kv_cols // head_dim
    group = queries.shape[1] // kv_cols
    kernel = functools.partial(attention_kernel, group=group, head_dim=head_dim)
    q_spec = pl.BlockSpec((seq_len, group * head_dim), lambda k, n: (0, k))
    kv_spec = pl.BlockSpec((seq_len, head_dim), lambda k, n: (0, k))
    return pl.pallas_call(
        kernel,
        grid_spec=pltpu.PrefetchScalarGridSpec(
            num_scalar_prefetch=1, grid=(kv_heads,),
            in_specs=[q_spec, q_spec, kv_spec, kv_spec],
            out_specs=[kv_spec, kv_spec]),
        out_shape=[jax.ShapeDtypeStruct((seq_len, kv_cols), jnp.float32),
                   jax.ShapeDtypeStruct((seq_len, kv_cols), jnp.bfloat16)],
    )(length, queries, cotan, keys, values)


def norm_backward(normed_grad, gain_f, nhat, inv_rms):
    gain_grad_in = normed_grad * gain_f
    centre = jnp.mean(gain_grad_in * nhat, axis=-1, keepdims=True)
    return ((gain_grad_in - nhat * centre) * inv_rms).astype(jnp.bfloat16)


def on_device(
    hidden_states,
    norm_gain,
    key_weight,
    value_weight,
    queries,
    context_cotangent,
    lengths,
    policy_logp,
    reference_logp,
):
    both_full = lax.all_gather(
        jnp.concatenate([key_weight[0], value_weight[0]], axis=1), "dp", axis=0, tiled=True
    )
    kv_cols = key_weight.shape[2]
    hidden = hidden_states[0]
    gain_f = norm_gain[0].astype(jnp.float32)
    tok_rows = hidden.shape[0]
    seq_count = lengths.shape[1]
    seq_len = tok_rows // seq_count
    kv_local = kv_cols // HD
    q_local = queries.shape[2] // HD
    hidden_f = hidden.astype(jnp.float32)
    inv_rms = lax.rsqrt(jnp.mean(hidden_f * hidden_f, axis=-1, keepdims=True) + norm_eps)
    nhat = hidden_f * inv_rms
    normed = (nhat * gain_f).astype(jnp.bfloat16)
    projected = jnp.dot(normed, both_full, preferred_element_type=jnp.float32)
    key_raw = projected[:, :kv_cols]
    values = projected[:, kv_cols:].astype(jnp.bfloat16)
    cosine, sine = rope_tables(seq_len, HD)
    key_four = key_raw.reshape(seq_count, seq_len, kv_local, HD)
    keys = (
        key_four * cosine[None, :, None, :] + rotate_half(key_four) * sine[None, :, None, :]
    ).astype(jnp.bfloat16)
    total_seqs = seq_count * lax.axis_size("dp")
    seq_weight = 2.0 * jax.nn.sigmoid(npo_beta * (policy_logp[0] - reference_logp[0])) / total_seqs
    live = jnp.arange(seq_len)[None, :] < lengths[0][:, None]
    factor = jnp.where(live, seq_weight[:, None], 0.0)
    scaled = (
        context_cotangent[0].reshape(seq_count, seq_len, q_local, HD).astype(jnp.float32)
        * factor[:, :, None, None]
    ).astype(jnp.bfloat16)

    key_parts, value_parts = [], []
    for n in range(seq_count):
        rows_n = slice(n * seq_len, (n + 1) * seq_len)
        rotated, value_part = attention_grads(
            lengths[0][n:n + 1],
            queries[0][rows_n],
            scaled[n].reshape(seq_len, q_local * HD),
            keys[n].reshape(seq_len, kv_cols),
            values[rows_n],
            HD,
        )
        rotated = rotated.reshape(seq_len, kv_local, HD)
        key_part = rotated * cosine[:, None, :] + rotate_back(rotated * sine[:, None, :])
        key_parts.append(key_part.astype(jnp.bfloat16))
        value_parts.append(value_part)
    key_grad = jnp.concatenate(key_parts, axis=0)
    value_grad = jnp.concatenate(value_parts, axis=0)
    key_grad = key_grad.reshape(tok_rows, kv_cols)
    value_grad = value_grad.reshape(tok_rows, kv_cols)
    combined = jnp.concatenate([key_grad, value_grad], axis=1)

    def weight_grads(combined):
        return lax.psum_scatter(
            lax.dot_general(
                normed, combined, (((0,), (0,)), ((), ())), preferred_element_type=jnp.float32
            ).astype(jnp.bfloat16),
            "dp",
            scatter_dimension=0,
            tiled=True,
        )

    n_pipe = lax.axis_size("pipe")
    n_tensor = lax.axis_size("tensor")
    sizes = [tok_rows // 8, tok_rows * 3 // 8, tok_rows * 3 // 8, tok_rows // 8]
    bounds = [sum(sizes[:c]) for c in range(len(sizes) + 1)]
    chunks = len(sizes)
    exchange_steps = [
        [
            (p * n_tensor + t, p * n_tensor + (t + step) % n_tensor)
            for p in range(1, n_pipe)
            for t in range(n_tensor)
        ]
        for step in range(1, n_tensor)
    ]
    shift_pairs = [
        ((p + 1) * n_tensor + (t if (p + 1) // 2 == p // 2 else n_tensor - 1 - t), p * n_tensor + t)
        for p in range(n_pipe - 1)
        for t in range(n_tensor)
    ]
    lowers = []
    held = None
    for c in range(chunks):
        sl = slice(bounds[c], bounds[c + 1])
        part = lax.dot_general(
            combined[sl], both_full, (((1,), (1,)), ((), ())), preferred_element_type=jnp.float32
        )
        part_low = part.astype(jnp.bfloat16)
        if c == 0:
            part_low, combined = lax.optimization_barrier((part_low, combined))
            grad_total = weight_grads(combined)
        if held is not None:
            if len(lowers) > 0:
                part_low, held, lowers[-1] = lax.optimization_barrier(
                    (part_low, held, lowers[-1])
                )
            else:
                part_low, held = lax.optimization_barrier((part_low, held))
            lowers.append(lax.ppermute(held, ("pipe", "tensor"), shift_pairs))
        normed_grad = part_low.astype(jnp.float32)
        for pairs in exchange_steps:
            normed_grad = normed_grad + lax.ppermute(
                part_low, ("pipe", "tensor"), pairs
            ).astype(jnp.float32)
        held = norm_backward(normed_grad, gain_f, nhat[sl], inv_rms[sl])
    lowers.append(lax.ppermute(held, ("pipe", "tensor"), shift_pairs))
    lower = jnp.concatenate(lowers, axis=0)
    return (grad_total[:, :kv_cols][None], grad_total[:, kv_cols:][None], lower[None])


def solution(mesh):
    in_specs = (
        P("pipe", "dp", None),
        P("pipe", None),
        P("pipe", "dp", "tensor"),
        P("pipe", "dp", "tensor"),
        P("pipe", "dp", "tensor"),
        P("pipe", "dp", "tensor"),
        P("pipe", "dp"),
        P("pipe", "dp"),
        P("pipe", "dp"),
    )
    out_specs = (P("pipe", "dp", "tensor"), P("pipe", "dp", "tensor"), P("pipe", "dp", None))
    return jax.shard_map(
        on_device, mesh=mesh, in_specs=in_specs, out_specs=out_specs, check_vma=False
    )
```

```python
import functools
import math

import jax
import jax.numpy as jnp
from jax import lax
from jax.experimental import pallas as pl
from jax.experimental.pallas import tpu as pltpu
from jax.sharding import PartitionSpec as P

HD = 128


npo_beta = 0.1
norm_eps = 1e-05
rope_base = 500000.0


def shifted(value, axis, steps):
    count = lax.axis_size(axis)
    leading, last = (max(0, -steps), min(count, count - steps))
    return lax.ppermute(value, axis, [(source, source + steps) for source in range(leading, last)])


def rope_tables(length, head_dim):
    positions = jnp.arange(length).astype(jnp.float32)
    freq_index = jnp.arange(head_dim // 2).astype(jnp.float32)
    inverse = 1.0 / rope_base ** (2.0 * freq_index / head_dim)
    angles = positions[:, None] * inverse[None, :]
    cosine = jnp.concatenate([jnp.cos(angles), jnp.cos(angles)], axis=1)
    sine = jnp.concatenate([jnp.sin(angles), jnp.sin(angles)], axis=1)
    return (cosine, sine)


def rotate_half(values):
    half = values.shape[-1] // 2
    return jnp.concatenate([-values[..., half:], values[..., :half]], axis=-1)


def rotate_back(values):
    half = values.shape[-1] // 2
    return jnp.concatenate([values[..., half:], -values[..., :half]], axis=-1)


def sequence_grads(query_seq, key_seq, value_seq, cotan_seq, length_seq, cosine, sine):
    seq_len, kv_heads, head_dim = key_seq.shape
    group = query_seq.shape[1] // kv_heads
    scale = 1.0 / math.sqrt(head_dim)
    query_g = query_seq.reshape(seq_len, kv_heads, group, head_dim)
    cotan_g = cotan_seq.reshape(seq_len, kv_heads, group, head_dim)
    scores = (
        jnp.einsum("ikgd,jkd->kgij", query_g, key_seq, preferred_element_type=jnp.float32) * scale
    )
    row_pos = jnp.arange(seq_len)[:, None]
    col_pos = jnp.arange(seq_len)[None, :]
    allowed = (col_pos <= row_pos) & (col_pos < length_seq)
    scores = jnp.where(allowed, scores, -1e30)
    highest = jnp.max(scores, axis=-1, keepdims=True)
    expd = jnp.where(allowed, jnp.exp(scores - highest), 0.0)
    probs = expd / jnp.sum(expd, axis=-1, keepdims=True)
    probs_low = probs.astype(jnp.bfloat16)
    value_grad = jnp.einsum(
        "kgij,ikgd->jkd", probs_low, cotan_g, preferred_element_type=jnp.float32
    ).astype(jnp.bfloat16)
    prob_grad = jnp.einsum("ikgd,jkd->kgij", cotan_g, value_seq, preferred_element_type=jnp.float32)
    centre = jnp.sum(probs * prob_grad, axis=-1, keepdims=True)
    score_grad = (probs * (prob_grad - centre) * scale).astype(jnp.bfloat16)
    rotated_grad = jnp.einsum(
        "kgij,ikgd->jkd", score_grad, query_g, preferred_element_type=jnp.float32
    )
    key_grad = rotated_grad * cosine[:, None, :] + rotate_back(rotated_grad * sine[:, None, :])
    return (key_grad.astype(jnp.bfloat16), value_grad)


def attention_kernel(len_ref, q_ref, c_ref, k_ref, v_ref, rg_ref, vg_ref, *, group, head_dim):
    seq_len = k_ref.shape[0]
    scale = 1.0 / math.sqrt(head_dim)
    length = len_ref[0]
    keys = k_ref[...]
    values = v_ref[...]
    row = lax.broadcasted_iota(jnp.int32, (seq_len, seq_len), 0)
    col = lax.broadcasted_iota(jnp.int32, (seq_len, seq_len), 1)
    allowed = (col <= row) & (col < length)
    rotated = jnp.zeros((seq_len, head_dim), jnp.float32)
    value_grad = jnp.zeros((seq_len, head_dim), jnp.float32)
    nt = (((1,), (1,)), ((), ()))
    nn = (((1,), (0,)), ((), ()))
    for g in range(group):
        query = q_ref[:, g * head_dim:(g + 1) * head_dim]
        cotan = c_ref[:, g * head_dim:(g + 1) * head_dim]
        scores = lax.dot_general(query, keys, nt, preferred_element_type=jnp.float32) * scale
        scores = jnp.where(allowed, scores, -1e30)
        highest = jnp.max(scores, axis=-1, keepdims=True)
        expd = jnp.where(allowed, jnp.exp(scores - highest), 0.0)
        probs = expd / jnp.sum(expd, axis=-1, keepdims=True)
        value_grad = value_grad + lax.dot_general(
            probs.T.astype(jnp.bfloat16), cotan, nn, preferred_element_type=jnp.float32)
        prob_grad = lax.dot_general(cotan, values, nt, preferred_element_type=jnp.float32)
        centre = jnp.sum(probs * prob_grad, axis=-1, keepdims=True)
        score_grad = probs * (prob_grad - centre) * scale
        rotated = rotated + lax.dot_general(
            score_grad.T.astype(jnp.bfloat16), query, nn, preferred_element_type=jnp.float32)
    rg_ref[...] = rotated
    vg_ref[...] = value_grad.astype(jnp.bfloat16)

def attention_grads(length, queries, cotan, keys, values, head_dim):
    seq_len, kv_cols = keys.shape
    kv_heads = kv_cols // head_dim
    group = queries.shape[1] // kv_cols
    kernel = functools.partial(attention_kernel, group=group, head_dim=head_dim)
    q_spec = pl.BlockSpec((seq_len, group * head_dim), lambda k, n: (0, k))
    kv_spec = pl.BlockSpec((seq_len, head_dim), lambda k, n: (0, k))
    return pl.pallas_call(
        kernel,
        grid_spec=pltpu.PrefetchScalarGridSpec(
            num_scalar_prefetch=1, grid=(kv_heads,),
            in_specs=[q_spec, q_spec, kv_spec, kv_spec],
            out_specs=[kv_spec, kv_spec]),
        out_shape=[jax.ShapeDtypeStruct((seq_len, kv_cols), jnp.float32),
                   jax.ShapeDtypeStruct((seq_len, kv_cols), jnp.bfloat16)],
    )(length, queries, cotan, keys, values)


def norm_backward(normed_grad, gain_f, nhat, inv_rms):
    gain_grad_in = normed_grad * gain_f
    centre = jnp.mean(gain_grad_in * nhat, axis=-1, keepdims=True)
    return ((gain_grad_in - nhat * centre) * inv_rms).astype(jnp.bfloat16)


def on_device(
    hidden_states,
    norm_gain,
    key_weight,
    value_weight,
    queries,
    context_cotangent,
    lengths,
    policy_logp,
    reference_logp,
):
    both_full = lax.all_gather(
        jnp.concatenate([key_weight[0], value_weight[0]], axis=1), "dp", axis=0, tiled=True
    )
    kv_cols = key_weight.shape[2]
    hidden = hidden_states[0]
    gain_f = norm_gain[0].astype(jnp.float32)
    tok_rows = hidden.shape[0]
    seq_count = lengths.shape[1]
    seq_len = tok_rows // seq_count
    kv_local = kv_cols // HD
    q_local = queries.shape[2] // HD
    hidden_f = hidden.astype(jnp.float32)
    inv_rms = lax.rsqrt(jnp.mean(hidden_f * hidden_f, axis=-1, keepdims=True) + norm_eps)
    nhat = hidden_f * inv_rms
    normed = (nhat * gain_f).astype(jnp.bfloat16)
    projected = jnp.dot(normed, both_full, preferred_element_type=jnp.float32)
    key_raw = projected[:, :kv_cols]
    values = projected[:, kv_cols:].astype(jnp.bfloat16)
    cosine, sine = rope_tables(seq_len, HD)
    key_four = key_raw.reshape(seq_count, seq_len, kv_local, HD)
    keys = (
        key_four * cosine[None, :, None, :] + rotate_half(key_four) * sine[None, :, None, :]
    ).astype(jnp.bfloat16)
    total_seqs = seq_count * lax.axis_size("dp")
    seq_weight = 2.0 * jax.nn.sigmoid(npo_beta * (policy_logp[0] - reference_logp[0])) / total_seqs
    live = jnp.arange(seq_len)[None, :] < lengths[0][:, None]
    factor = jnp.where(live, seq_weight[:, None], 0.0)
    scaled = (
        context_cotangent[0].reshape(seq_count, seq_len, q_local, HD).astype(jnp.float32)
        * factor[:, :, None, None]
    ).astype(jnp.bfloat16)

    key_parts, value_parts = [], []
    for n in range(seq_count):
        rows_n = slice(n * seq_len, (n + 1) * seq_len)
        rotated, value_part = attention_grads(
            lengths[0][n:n + 1],
            queries[0][rows_n],
            scaled[n].reshape(seq_len, q_local * HD),
            keys[n].reshape(seq_len, kv_cols),
            values[rows_n],
            HD,
        )
        rotated = rotated.reshape(seq_len, kv_local, HD)
        key_part = rotated * cosine[:, None, :] + rotate_back(rotated * sine[:, None, :])
        key_parts.append(key_part.astype(jnp.bfloat16))
        value_parts.append(value_part)
    key_grad = jnp.concatenate(key_parts, axis=0)
    value_grad = jnp.concatenate(value_parts, axis=0)
    key_grad = key_grad.reshape(tok_rows, kv_cols)
    value_grad = value_grad.reshape(tok_rows, kv_cols)
    combined = jnp.concatenate([key_grad, value_grad], axis=1)

    def weight_grads(combined):
        return lax.psum_scatter(
            lax.dot_general(
                normed, combined, (((0,), (0,)), ((), ())), preferred_element_type=jnp.float32
            ).astype(jnp.bfloat16),
            "dp",
            scatter_dimension=0,
            tiled=True,
        )

    n_pipe = lax.axis_size("pipe")
    n_tensor = lax.axis_size("tensor")
    me_pipe = lax.axis_index("pipe")
    axes = ("pipe", "tensor")

    def at(p, t):
        return p * n_tensor + t

    same_chip = lambda p, q: p // 2 == q // 2
    late = [q for q in range(2, n_pipe) if same_chip(q, q - 1)]
    early = [q for q in range(1, n_pipe) if q not in late]

    def swap(qs):
        return [(at(q, t), at(q, (t + 1) % n_tensor)) for q in qs for t in range(n_tensor)]

    def shift(qs):
        return [
            (at(q, t if same_chip(q, q - 1) else n_tensor - 1 - t), at(q - 1, t))
            for q in qs
            for t in range(n_tensor)
        ]

    def reduce_and_send(sections, sizes, combined=None, gate=None):
        bounds = [sum(sizes[:c]) for c in range(len(sizes) + 1)]
        exchange_pairs, shift_pairs = swap(sections), shift(sections)
        lowers, held, signal, grads = [], None, None, None
        for c in range(len(sizes)):
            sl = slice(bounds[c], bounds[c + 1])
            part = lax.dot_general(
                both_grads[sl], both_full, (((1,), (1,)), ((), ())),
                preferred_element_type=jnp.float32,
            )
            if gate is not None:
                part = part.at[0, 0].add(0.0 * gate[0, 0].astype(jnp.float32))
                gate = None
            part_low = part.astype(jnp.bfloat16)
            if combined is not None:
                part_low, combined = lax.optimization_barrier((part_low, combined))
                grads = weight_grads(combined)
                combined = None
            if held is not None:
                if len(lowers) > 0:
                    part_low, held, lowers[-1] = lax.optimization_barrier(
                        (part_low, held, lowers[-1])
                    )
                else:
                    part_low, held = lax.optimization_barrier((part_low, held))
                lowers.append(lax.ppermute(held, axes, shift_pairs))
            received = lax.ppermute(part_low, axes, exchange_pairs)
            signal = received[:8, :128]
            normed_grad = part_low.astype(jnp.float32) + received.astype(jnp.float32)
            held = norm_backward(normed_grad, gain_f, nhat[sl], inv_rms[sl])
        lowers.append(lax.ppermute(held, axes, shift_pairs))
        return jnp.concatenate(lowers, axis=0), signal, grads

    both_grads = combined
    first, signal, grad_total = reduce_and_send(
        early, [tok_rows // 4, tok_rows * 5 // 16, tok_rows * 5 // 16, tok_rows // 8], combined
    )
    lower = first
    if late:
        release = [(at(q - 1, t), at(q, t)) for q in late for t in range(n_tensor)]
        gate = lax.ppermute(signal, axes, release)
        second, _, _ = reduce_and_send(late, [tok_rows // 2, tok_rows // 2], gate=gate)
        from_late = functools.reduce(
            jnp.logical_or, [me_pipe == q - 1 for q in late], me_pipe < 0
        )
        lower = jnp.where(from_late, second, first)
    return (grad_total[:, :kv_cols][None], grad_total[:, kv_cols:][None], lower[None])


def solution(mesh):
    in_specs = (
        P("pipe", "dp", None),
        P("pipe", None),
        P("pipe", "dp", "tensor"),
        P("pipe", "dp", "tensor"),
        P("pipe", "dp", "tensor"),
        P("pipe", "dp", "tensor"),
        P("pipe", "dp"),
        P("pipe", "dp"),
        P("pipe", "dp"),
    )
    out_specs = (P("pipe", "dp", "tensor"), P("pipe", "dp", "tensor"), P("pipe", "dp", None))
    return jax.shard_map(
        on_device, mesh=mesh, in_specs=in_specs, out_specs=out_specs, check_vma=False
    )
```

```python
import functools
import math

import jax
import jax.numpy as jnp
from jax import lax
from jax.experimental import pallas as pl
from jax.experimental.pallas import tpu as pltpu
from jax.sharding import PartitionSpec as P

HD = 128


npo_beta = 0.1
norm_eps = 1e-05
rope_base = 500000.0


def shifted(value, axis, steps):
    count = lax.axis_size(axis)
    leading, last = (max(0, -steps), min(count, count - steps))
    return lax.ppermute(value, axis, [(source, source + steps) for source in range(leading, last)])


def rope_tables(length, head_dim):
    positions = jnp.arange(length).astype(jnp.float32)
    freq_index = jnp.arange(head_dim // 2).astype(jnp.float32)
    inverse = 1.0 / rope_base ** (2.0 * freq_index / head_dim)
    angles = positions[:, None] * inverse[None, :]
    cosine = jnp.concatenate([jnp.cos(angles), jnp.cos(angles)], axis=1)
    sine = jnp.concatenate([jnp.sin(angles), jnp.sin(angles)], axis=1)
    return (cosine, sine)


def rotate_half(values):
    half = values.shape[-1] // 2
    return jnp.concatenate([-values[..., half:], values[..., :half]], axis=-1)


def rotate_back(values):
    half = values.shape[-1] // 2
    return jnp.concatenate([values[..., half:], -values[..., :half]], axis=-1)


def sequence_grads(query_seq, key_seq, value_seq, cotan_seq, length_seq, cosine, sine):
    seq_len, kv_heads, head_dim = key_seq.shape
    group = query_seq.shape[1] // kv_heads
    scale = 1.0 / math.sqrt(head_dim)
    query_g = query_seq.reshape(seq_len, kv_heads, group, head_dim)
    cotan_g = cotan_seq.reshape(seq_len, kv_heads, group, head_dim)
    scores = (
        jnp.einsum("ikgd,jkd->kgij", query_g, key_seq, preferred_element_type=jnp.float32) * scale
    )
    row_pos = jnp.arange(seq_len)[:, None]
    col_pos = jnp.arange(seq_len)[None, :]
    allowed = (col_pos <= row_pos) & (col_pos < length_seq)
    scores = jnp.where(allowed, scores, -1e30)
    highest = jnp.max(scores, axis=-1, keepdims=True)
    expd = jnp.where(allowed, jnp.exp(scores - highest), 0.0)
    probs = expd / jnp.sum(expd, axis=-1, keepdims=True)
    probs_low = probs.astype(jnp.bfloat16)
    value_grad = jnp.einsum(
        "kgij,ikgd->jkd", probs_low, cotan_g, preferred_element_type=jnp.float32
    ).astype(jnp.bfloat16)
    prob_grad = jnp.einsum("ikgd,jkd->kgij", cotan_g, value_seq, preferred_element_type=jnp.float32)
    centre = jnp.sum(probs * prob_grad, axis=-1, keepdims=True)
    score_grad = (probs * (prob_grad - centre) * scale).astype(jnp.bfloat16)
    rotated_grad = jnp.einsum(
        "kgij,ikgd->jkd", score_grad, query_g, preferred_element_type=jnp.float32
    )
    key_grad = rotated_grad * cosine[:, None, :] + rotate_back(rotated_grad * sine[:, None, :])
    return (key_grad.astype(jnp.bfloat16), value_grad)


def attention_kernel(
    len_ref, q_ref, c_ref, k_ref, v_ref, cos_ref, sin_ref, kg_ref, vg_ref, *, group, head_dim
):
    seq_len = k_ref.shape[0]
    scale = 1.0 / math.sqrt(head_dim)
    length = len_ref[0]
    keys = k_ref[...]
    values = v_ref[...]
    row = lax.broadcasted_iota(jnp.int32, (seq_len, seq_len), 0)
    col = lax.broadcasted_iota(jnp.int32, (seq_len, seq_len), 1)
    allowed = (col <= row) & (col < length)
    rotated = jnp.zeros((seq_len, head_dim), jnp.float32)
    value_grad = jnp.zeros((seq_len, head_dim), jnp.float32)
    nt = (((1,), (1,)), ((), ()))
    nn = (((1,), (0,)), ((), ()))
    for g in range(group):
        query = q_ref[:, g * head_dim:(g + 1) * head_dim]
        cotan = c_ref[:, g * head_dim:(g + 1) * head_dim]
        scores = lax.dot_general(query, keys, nt, preferred_element_type=jnp.float32) * scale
        scores = jnp.where(allowed, scores, -1e30)
        highest = jnp.max(scores, axis=-1, keepdims=True)
        expd = jnp.where(allowed, jnp.exp(scores - highest), 0.0)
        probs = expd / jnp.sum(expd, axis=-1, keepdims=True)
        value_grad = value_grad + lax.dot_general(
            probs.T.astype(jnp.bfloat16), cotan, nn, preferred_element_type=jnp.float32)
        prob_grad = lax.dot_general(cotan, values, nt, preferred_element_type=jnp.float32)
        centre = jnp.sum(probs * prob_grad, axis=-1, keepdims=True)
        score_grad = probs * (prob_grad - centre) * scale
        rotated = rotated + lax.dot_general(
            score_grad.T.astype(jnp.bfloat16), query, nn, preferred_element_type=jnp.float32)
    lane = lax.broadcasted_iota(jnp.int32, (seq_len, head_dim), 1)
    turned = pltpu.roll(rotated * sin_ref[...], head_dim // 2, 1)
    turned = jnp.where(lane < head_dim // 2, turned, -turned)
    kg_ref[...] = (rotated * cos_ref[...] + turned).astype(jnp.bfloat16)
    vg_ref[...] = value_grad.astype(jnp.bfloat16)

def attention_grads(length, queries, cotan, keys, values, cosine, sine, head_dim):
    seq_len, kv_cols = keys.shape
    kv_heads = kv_cols // head_dim
    group = queries.shape[1] // kv_cols
    kernel = functools.partial(attention_kernel, group=group, head_dim=head_dim)
    q_spec = pl.BlockSpec((seq_len, group * head_dim), lambda k, n: (0, k))
    kv_spec = pl.BlockSpec((seq_len, head_dim), lambda k, n: (0, k))
    rope_spec = pl.BlockSpec((seq_len, head_dim), lambda k, n: (0, 0))
    return pl.pallas_call(
        kernel,
        grid_spec=pltpu.PrefetchScalarGridSpec(
            num_scalar_prefetch=1, grid=(kv_heads,),
            in_specs=[q_spec, q_spec, kv_spec, kv_spec, rope_spec, rope_spec],
            out_specs=[kv_spec, kv_spec]),
        out_shape=[jax.ShapeDtypeStruct((seq_len, kv_cols), jnp.bfloat16),
                   jax.ShapeDtypeStruct((seq_len, kv_cols), jnp.bfloat16)],
    )(length, queries, cotan, keys, values, cosine, sine)


def norm_backward(normed_grad, gain_f, nhat, inv_rms):
    gain_grad_in = normed_grad * gain_f
    centre = jnp.mean(gain_grad_in * nhat, axis=-1, keepdims=True)
    return ((gain_grad_in - nhat * centre) * inv_rms).astype(jnp.bfloat16)


def on_device(
    hidden_states,
    norm_gain,
    key_weight,
    value_weight,
    queries,
    context_cotangent,
    lengths,
    policy_logp,
    reference_logp,
):
    both_full = lax.all_gather(
        jnp.concatenate([key_weight[0], value_weight[0]], axis=1), "dp", axis=0, tiled=True
    )
    kv_cols = key_weight.shape[2]
    hidden = hidden_states[0]
    gain_f = norm_gain[0].astype(jnp.float32)
    tok_rows = hidden.shape[0]
    seq_count = lengths.shape[1]
    seq_len = tok_rows // seq_count
    kv_local = kv_cols // HD
    q_local = queries.shape[2] // HD
    hidden_f = hidden.astype(jnp.float32)
    inv_rms = lax.rsqrt(jnp.mean(hidden_f * hidden_f, axis=-1, keepdims=True) + norm_eps)
    nhat = hidden_f * inv_rms
    normed = (nhat * gain_f).astype(jnp.bfloat16)
    projected = jnp.dot(normed, both_full, preferred_element_type=jnp.float32)
    key_raw = projected[:, :kv_cols]
    values = projected[:, kv_cols:].astype(jnp.bfloat16)
    cosine, sine = rope_tables(seq_len, HD)
    key_four = key_raw.reshape(seq_count, seq_len, kv_local, HD)
    keys = (
        key_four * cosine[None, :, None, :] + rotate_half(key_four) * sine[None, :, None, :]
    ).astype(jnp.bfloat16)
    total_seqs = seq_count * lax.axis_size("dp")
    seq_weight = 2.0 * jax.nn.sigmoid(npo_beta * (policy_logp[0] - reference_logp[0])) / total_seqs
    live = jnp.arange(seq_len)[None, :] < lengths[0][:, None]
    factor = jnp.where(live, seq_weight[:, None], 0.0)
    scaled = (
        context_cotangent[0].reshape(seq_count, seq_len, q_local, HD).astype(jnp.float32)
        * factor[:, :, None, None]
    ).astype(jnp.bfloat16)

    key_parts, value_parts = [], []
    for n in range(seq_count):
        rows_n = slice(n * seq_len, (n + 1) * seq_len)
        key_part, value_part = attention_grads(
            lengths[0][n:n + 1],
            queries[0][rows_n],
            scaled[n].reshape(seq_len, q_local * HD),
            keys[n].reshape(seq_len, kv_cols),
            values[rows_n],
            cosine,
            sine,
            HD,
        )
        key_parts.append(key_part)
        value_parts.append(value_part)
    key_grad = jnp.concatenate(key_parts, axis=0)
    value_grad = jnp.concatenate(value_parts, axis=0)
    key_grad = key_grad.reshape(tok_rows, kv_cols)
    value_grad = value_grad.reshape(tok_rows, kv_cols)
    combined = jnp.concatenate([key_grad, value_grad], axis=1)

    def weight_grads(combined):
        return lax.psum_scatter(
            lax.dot_general(
                normed, combined, (((0,), (0,)), ((), ())), preferred_element_type=jnp.float32
            ).astype(jnp.bfloat16),
            "dp",
            scatter_dimension=0,
            tiled=True,
        )

    n_pipe = lax.axis_size("pipe")
    n_tensor = lax.axis_size("tensor")
    sizes = [tok_rows // 4, tok_rows * 5 // 16, tok_rows * 5 // 16, tok_rows // 8]
    bounds = [sum(sizes[:c]) for c in range(len(sizes) + 1)]
    chunks = len(sizes)
    exchange_steps = [
        [
            (p * n_tensor + t, p * n_tensor + (t + step) % n_tensor)
            for p in range(1, n_pipe)
            for t in range(n_tensor)
        ]
        for step in range(1, n_tensor)
    ]
    shift_pairs = [
        ((p + 1) * n_tensor + (t if (p + 1) // 2 == p // 2 else n_tensor - 1 - t), p * n_tensor + t)
        for p in range(n_pipe - 1)
        for t in range(n_tensor)
    ]
    lowers = []
    held = None
    for c in range(chunks):
        sl = slice(bounds[c], bounds[c + 1])
        part = lax.dot_general(
            combined[sl], both_full, (((1,), (1,)), ((), ())), preferred_element_type=jnp.float32
        )
        part_low = part.astype(jnp.bfloat16)
        if c == 0:
            part_low, combined = lax.optimization_barrier((part_low, combined))
            grad_total = weight_grads(combined)
        if held is not None:
            if len(lowers) > 0:
                part_low, held, lowers[-1] = lax.optimization_barrier(
                    (part_low, held, lowers[-1])
                )
            else:
                part_low, held = lax.optimization_barrier((part_low, held))
            lowers.append(lax.ppermute(held, ("pipe", "tensor"), shift_pairs))
        normed_grad = part_low.astype(jnp.float32)
        for pairs in exchange_steps:
            normed_grad = normed_grad + lax.ppermute(
                part_low, ("pipe", "tensor"), pairs
            ).astype(jnp.float32)
        held = norm_backward(normed_grad, gain_f, nhat[sl], inv_rms[sl])
    lowers.append(lax.ppermute(held, ("pipe", "tensor"), shift_pairs))
    lower = jnp.concatenate(lowers, axis=0)
    return (grad_total[:, :kv_cols][None], grad_total[:, kv_cols:][None], lower[None])


def solution(mesh):
    in_specs = (
        P("pipe", "dp", None),
        P("pipe", None),
        P("pipe", "dp", "tensor"),
        P("pipe", "dp", "tensor"),
        P("pipe", "dp", "tensor"),
        P("pipe", "dp", "tensor"),
        P("pipe", "dp"),
        P("pipe", "dp"),
        P("pipe", "dp"),
    )
    out_specs = (P("pipe", "dp", "tensor"), P("pipe", "dp", "tensor"), P("pipe", "dp", None))
    return jax.shard_map(
        on_device, mesh=mesh, in_specs=in_specs, out_specs=out_specs, check_vma=False
    )
```

```python
import functools
import math

import jax
import jax.numpy as jnp
from jax import lax
from jax.experimental import pallas as pl
from jax.experimental.pallas import tpu as pltpu
from jax.sharding import PartitionSpec as P

HD = 128


npo_beta = 0.1
norm_eps = 1e-05
rope_base = 500000.0


def shifted(value, axis, steps):
    count = lax.axis_size(axis)
    leading, last = (max(0, -steps), min(count, count - steps))
    return lax.ppermute(value, axis, [(source, source + steps) for source in range(leading, last)])


def rope_tables(length, head_dim):
    positions = jnp.arange(length).astype(jnp.float32)
    freq_index = jnp.arange(head_dim // 2).astype(jnp.float32)
    inverse = 1.0 / rope_base ** (2.0 * freq_index / head_dim)
    angles = positions[:, None] * inverse[None, :]
    cosine = jnp.concatenate([jnp.cos(angles), jnp.cos(angles)], axis=1)
    sine = jnp.concatenate([jnp.sin(angles), jnp.sin(angles)], axis=1)
    return (cosine, sine)


def rotate_half(values):
    half = values.shape[-1] // 2
    return jnp.concatenate([-values[..., half:], values[..., :half]], axis=-1)


def rotate_back(values):
    half = values.shape[-1] // 2
    return jnp.concatenate([values[..., half:], -values[..., :half]], axis=-1)


def sequence_grads(query_seq, key_seq, value_seq, cotan_seq, length_seq, cosine, sine):
    seq_len, kv_heads, head_dim = key_seq.shape
    group = query_seq.shape[1] // kv_heads
    scale = 1.0 / math.sqrt(head_dim)
    query_g = query_seq.reshape(seq_len, kv_heads, group, head_dim)
    cotan_g = cotan_seq.reshape(seq_len, kv_heads, group, head_dim)
    scores = (
        jnp.einsum("ikgd,jkd->kgij", query_g, key_seq, preferred_element_type=jnp.float32) * scale
    )
    row_pos = jnp.arange(seq_len)[:, None]
    col_pos = jnp.arange(seq_len)[None, :]
    allowed = (col_pos <= row_pos) & (col_pos < length_seq)
    scores = jnp.where(allowed, scores, -1e30)
    highest = jnp.max(scores, axis=-1, keepdims=True)
    expd = jnp.where(allowed, jnp.exp(scores - highest), 0.0)
    probs = expd / jnp.sum(expd, axis=-1, keepdims=True)
    probs_low = probs.astype(jnp.bfloat16)
    value_grad = jnp.einsum(
        "kgij,ikgd->jkd", probs_low, cotan_g, preferred_element_type=jnp.float32
    ).astype(jnp.bfloat16)
    prob_grad = jnp.einsum("ikgd,jkd->kgij", cotan_g, value_seq, preferred_element_type=jnp.float32)
    centre = jnp.sum(probs * prob_grad, axis=-1, keepdims=True)
    score_grad = (probs * (prob_grad - centre) * scale).astype(jnp.bfloat16)
    rotated_grad = jnp.einsum(
        "kgij,ikgd->jkd", score_grad, query_g, preferred_element_type=jnp.float32
    )
    key_grad = rotated_grad * cosine[:, None, :] + rotate_back(rotated_grad * sine[:, None, :])
    return (key_grad.astype(jnp.bfloat16), value_grad)


def attention_kernel(
    len_ref, q_ref, c_ref, k_ref, v_ref, cos_ref, sin_ref, out_ref, *, group, head_dim
):
    seq_len = k_ref.shape[0]
    scale = 1.0 / math.sqrt(head_dim)
    length = len_ref[0]
    keys = k_ref[...]
    values = v_ref[...]
    row = lax.broadcasted_iota(jnp.int32, (seq_len, seq_len), 0)
    col = lax.broadcasted_iota(jnp.int32, (seq_len, seq_len), 1)
    allowed = (col <= row) & (col < length)
    rotated = jnp.zeros((seq_len, head_dim), jnp.float32)
    value_grad = jnp.zeros((seq_len, head_dim), jnp.float32)
    nt = (((1,), (1,)), ((), ()))
    nn = (((1,), (0,)), ((), ()))
    for g in range(group):
        query = q_ref[:, g * head_dim:(g + 1) * head_dim]
        cotan = c_ref[:, g * head_dim:(g + 1) * head_dim]
        scores = lax.dot_general(query, keys, nt, preferred_element_type=jnp.float32) * scale
        scores = jnp.where(allowed, scores, -1e30)
        highest = jnp.max(scores, axis=-1, keepdims=True)
        expd = jnp.where(allowed, jnp.exp(scores - highest), 0.0)
        probs = expd / jnp.sum(expd, axis=-1, keepdims=True)
        value_grad = value_grad + lax.dot_general(
            probs.T.astype(jnp.bfloat16), cotan, nn, preferred_element_type=jnp.float32)
        prob_grad = lax.dot_general(cotan, values, nt, preferred_element_type=jnp.float32)
        centre = jnp.sum(probs * prob_grad, axis=-1, keepdims=True)
        score_grad = probs * (prob_grad - centre) * scale
        rotated = rotated + lax.dot_general(
            score_grad.T.astype(jnp.bfloat16), query, nn, preferred_element_type=jnp.float32)
    lane = lax.broadcasted_iota(jnp.int32, (seq_len, head_dim), 1)
    turned = pltpu.roll(rotated * sin_ref[...], head_dim // 2, 1)
    turned = jnp.where(lane < head_dim // 2, turned, -turned)
    head = pl.program_id(0)
    kv_cols = out_ref.shape[1] // 2
    key_at = pl.multiple_of(head * head_dim, head_dim)
    value_at = pl.multiple_of(kv_cols + head * head_dim, head_dim)
    out_ref[:, pl.ds(key_at, head_dim)] = (rotated * cos_ref[...] + turned).astype(jnp.bfloat16)
    out_ref[:, pl.ds(value_at, head_dim)] = value_grad.astype(jnp.bfloat16)

def attention_grads(length, queries, cotan, keys, values, cosine, sine, head_dim):
    seq_len, kv_cols = keys.shape
    kv_heads = kv_cols // head_dim
    group = queries.shape[1] // kv_cols
    kernel = functools.partial(attention_kernel, group=group, head_dim=head_dim)
    q_spec = pl.BlockSpec((seq_len, group * head_dim), lambda k, n: (0, k))
    kv_spec = pl.BlockSpec((seq_len, head_dim), lambda k, n: (0, k))
    rope_spec = pl.BlockSpec((seq_len, head_dim), lambda k, n: (0, 0))
    return pl.pallas_call(
        kernel,
        grid_spec=pltpu.PrefetchScalarGridSpec(
            num_scalar_prefetch=1, grid=(kv_heads,),
            in_specs=[q_spec, q_spec, kv_spec, kv_spec, rope_spec, rope_spec],
            out_specs=pl.BlockSpec((seq_len, 2 * kv_cols), lambda k, n: (0, 0))),
        out_shape=jax.ShapeDtypeStruct((seq_len, 2 * kv_cols), jnp.bfloat16),
    )(length, queries, cotan, keys, values, cosine, sine)


def norm_backward(normed_grad, gain_f, nhat, inv_rms):
    gain_grad_in = normed_grad * gain_f
    centre = jnp.mean(gain_grad_in * nhat, axis=-1, keepdims=True)
    return ((gain_grad_in - nhat * centre) * inv_rms).astype(jnp.bfloat16)


def on_device(
    hidden_states,
    norm_gain,
    key_weight,
    value_weight,
    queries,
    context_cotangent,
    lengths,
    policy_logp,
    reference_logp,
):
    both_full = lax.all_gather(
        jnp.concatenate([key_weight[0], value_weight[0]], axis=1), "dp", axis=0, tiled=True
    )
    kv_cols = key_weight.shape[2]
    hidden = hidden_states[0]
    gain_f = norm_gain[0].astype(jnp.float32)
    tok_rows = hidden.shape[0]
    seq_count = lengths.shape[1]
    seq_len = tok_rows // seq_count
    kv_local = kv_cols // HD
    q_local = queries.shape[2] // HD
    hidden_f = hidden.astype(jnp.float32)
    inv_rms = lax.rsqrt(jnp.mean(hidden_f * hidden_f, axis=-1, keepdims=True) + norm_eps)
    nhat = hidden_f * inv_rms
    normed = (nhat * gain_f).astype(jnp.bfloat16)
    projected = jnp.dot(normed, both_full, preferred_element_type=jnp.float32)
    key_raw = projected[:, :kv_cols]
    values = projected[:, kv_cols:].astype(jnp.bfloat16)
    cosine, sine = rope_tables(seq_len, HD)
    key_four = key_raw.reshape(seq_count, seq_len, kv_local, HD)
    keys = (
        key_four * cosine[None, :, None, :] + rotate_half(key_four) * sine[None, :, None, :]
    ).astype(jnp.bfloat16)
    total_seqs = seq_count * lax.axis_size("dp")
    seq_weight = 2.0 * jax.nn.sigmoid(npo_beta * (policy_logp[0] - reference_logp[0])) / total_seqs
    live = jnp.arange(seq_len)[None, :] < lengths[0][:, None]
    factor = jnp.where(live, seq_weight[:, None], 0.0)
    scaled = (
        context_cotangent[0].reshape(seq_count, seq_len, q_local, HD).astype(jnp.float32)
        * factor[:, :, None, None]
    ).astype(jnp.bfloat16)

    key_parts = []
    for n in range(seq_count):
        rows_n = slice(n * seq_len, (n + 1) * seq_len)
        both_part = attention_grads(
            lengths[0][n:n + 1],
            queries[0][rows_n],
            scaled[n].reshape(seq_len, q_local * HD),
            keys[n].reshape(seq_len, kv_cols),
            values[rows_n],
            cosine,
            sine,
            HD,
        )
        key_parts.append(both_part)
    combined = jnp.concatenate(key_parts, axis=0)

    def weight_grads(combined):
        return lax.psum_scatter(
            lax.dot_general(
                normed, combined, (((0,), (0,)), ((), ())), preferred_element_type=jnp.float32
            ).astype(jnp.bfloat16),
            "dp",
            scatter_dimension=0,
            tiled=True,
        )

    n_pipe = lax.axis_size("pipe")
    n_tensor = lax.axis_size("tensor")
    sizes = [tok_rows // 4, tok_rows * 5 // 16, tok_rows * 5 // 16, tok_rows // 8]
    bounds = [sum(sizes[:c]) for c in range(len(sizes) + 1)]
    chunks = len(sizes)
    exchange_steps = [
        [
            (p * n_tensor + t, p * n_tensor + (t + step) % n_tensor)
            for p in range(1, n_pipe)
            for t in range(n_tensor)
        ]
        for step in range(1, n_tensor)
    ]
    shift_pairs = [
        ((p + 1) * n_tensor + (t if (p + 1) // 2 == p // 2 else n_tensor - 1 - t), p * n_tensor + t)
        for p in range(n_pipe - 1)
        for t in range(n_tensor)
    ]
    lowers = []
    held = None
    for c in range(chunks):
        sl = slice(bounds[c], bounds[c + 1])
        part = lax.dot_general(
            combined[sl], both_full, (((1,), (1,)), ((), ())), preferred_element_type=jnp.float32
        )
        part_low = part.astype(jnp.bfloat16)
        if c == 0:
            part_low, combined = lax.optimization_barrier((part_low, combined))
            grad_total = weight_grads(combined)
        if held is not None:
            if len(lowers) > 0:
                part_low, held, lowers[-1] = lax.optimization_barrier(
                    (part_low, held, lowers[-1])
                )
            else:
                part_low, held = lax.optimization_barrier((part_low, held))
            lowers.append(lax.ppermute(held, ("pipe", "tensor"), shift_pairs))
        normed_grad = part_low.astype(jnp.float32)
        for pairs in exchange_steps:
            normed_grad = normed_grad + lax.ppermute(
                part_low, ("pipe", "tensor"), pairs
            ).astype(jnp.float32)
        held = norm_backward(normed_grad, gain_f, nhat[sl], inv_rms[sl])
    lowers.append(lax.ppermute(held, ("pipe", "tensor"), shift_pairs))
    lower = jnp.concatenate(lowers, axis=0)
    return (grad_total[:, :kv_cols][None], grad_total[:, kv_cols:][None], lower[None])


def solution(mesh):
    in_specs = (
        P("pipe", "dp", None),
        P("pipe", None),
        P("pipe", "dp", "tensor"),
        P("pipe", "dp", "tensor"),
        P("pipe", "dp", "tensor"),
        P("pipe", "dp", "tensor"),
        P("pipe", "dp"),
        P("pipe", "dp"),
        P("pipe", "dp"),
    )
    out_specs = (P("pipe", "dp", "tensor"), P("pipe", "dp", "tensor"), P("pipe", "dp", None))
    return jax.shard_map(
        on_device, mesh=mesh, in_specs=in_specs, out_specs=out_specs, check_vma=False
    )
```

```python
import functools
import math

import jax
import jax.numpy as jnp
from jax import lax
from jax.experimental import pallas as pl
from jax.experimental.pallas import tpu as pltpu
from jax.sharding import PartitionSpec as P

HD = 128


npo_beta = 0.1
norm_eps = 1e-05
rope_base = 500000.0


def shifted(value, axis, steps):
    count = lax.axis_size(axis)
    leading, last = (max(0, -steps), min(count, count - steps))
    return lax.ppermute(value, axis, [(source, source + steps) for source in range(leading, last)])


def rope_tables(length, head_dim):
    positions = jnp.arange(length).astype(jnp.float32)
    freq_index = jnp.arange(head_dim // 2).astype(jnp.float32)
    inverse = 1.0 / rope_base ** (2.0 * freq_index / head_dim)
    angles = positions[:, None] * inverse[None, :]
    cosine = jnp.concatenate([jnp.cos(angles), jnp.cos(angles)], axis=1)
    sine = jnp.concatenate([jnp.sin(angles), jnp.sin(angles)], axis=1)
    return (cosine, sine)


def rotate_half(values):
    half = values.shape[-1] // 2
    return jnp.concatenate([-values[..., half:], values[..., :half]], axis=-1)


def rotate_back(values):
    half = values.shape[-1] // 2
    return jnp.concatenate([values[..., half:], -values[..., :half]], axis=-1)


def sequence_grads(query_seq, key_seq, value_seq, cotan_seq, length_seq, cosine, sine):
    seq_len, kv_heads, head_dim = key_seq.shape
    group = query_seq.shape[1] // kv_heads
    scale = 1.0 / math.sqrt(head_dim)
    query_g = query_seq.reshape(seq_len, kv_heads, group, head_dim)
    cotan_g = cotan_seq.reshape(seq_len, kv_heads, group, head_dim)
    scores = (
        jnp.einsum("ikgd,jkd->kgij", query_g, key_seq, preferred_element_type=jnp.float32) * scale
    )
    row_pos = jnp.arange(seq_len)[:, None]
    col_pos = jnp.arange(seq_len)[None, :]
    allowed = (col_pos <= row_pos) & (col_pos < length_seq)
    scores = jnp.where(allowed, scores, -1e30)
    highest = jnp.max(scores, axis=-1, keepdims=True)
    expd = jnp.where(allowed, jnp.exp(scores - highest), 0.0)
    probs = expd / jnp.sum(expd, axis=-1, keepdims=True)
    probs_low = probs.astype(jnp.bfloat16)
    value_grad = jnp.einsum(
        "kgij,ikgd->jkd", probs_low, cotan_g, preferred_element_type=jnp.float32
    ).astype(jnp.bfloat16)
    prob_grad = jnp.einsum("ikgd,jkd->kgij", cotan_g, value_seq, preferred_element_type=jnp.float32)
    centre = jnp.sum(probs * prob_grad, axis=-1, keepdims=True)
    score_grad = (probs * (prob_grad - centre) * scale).astype(jnp.bfloat16)
    rotated_grad = jnp.einsum(
        "kgij,ikgd->jkd", score_grad, query_g, preferred_element_type=jnp.float32
    )
    key_grad = rotated_grad * cosine[:, None, :] + rotate_back(rotated_grad * sine[:, None, :])
    return (key_grad.astype(jnp.bfloat16), value_grad)


def attention_kernel(
    len_ref, q_ref, c_ref, k_ref, v_ref, cos_ref, sin_ref, out_ref, *, group, head_dim
):
    seq_len = k_ref.shape[0]
    scale = 1.0 / math.sqrt(head_dim)
    length = len_ref[0]
    lane = lax.broadcasted_iota(jnp.int32, (seq_len, head_dim), 1)
    key_raw = k_ref[...]
    half_turn = pltpu.roll(key_raw, head_dim // 2, 1)
    half_turn = jnp.where(lane < head_dim // 2, -half_turn, half_turn)
    keys = (key_raw * cos_ref[...] + half_turn * sin_ref[...]).astype(jnp.bfloat16)
    values = v_ref[...].astype(jnp.bfloat16)
    row = lax.broadcasted_iota(jnp.int32, (seq_len, seq_len), 0)
    col = lax.broadcasted_iota(jnp.int32, (seq_len, seq_len), 1)
    allowed = (col <= row) & (col < length)
    rotated = jnp.zeros((seq_len, head_dim), jnp.float32)
    value_grad = jnp.zeros((seq_len, head_dim), jnp.float32)
    nt = (((1,), (1,)), ((), ()))
    nn = (((1,), (0,)), ((), ()))
    for g in range(group):
        query = q_ref[:, g * head_dim:(g + 1) * head_dim]
        cotan = c_ref[:, g * head_dim:(g + 1) * head_dim]
        scores = lax.dot_general(query, keys, nt, preferred_element_type=jnp.float32) * scale
        scores = jnp.where(allowed, scores, -1e30)
        highest = jnp.max(scores, axis=-1, keepdims=True)
        expd = jnp.where(allowed, jnp.exp(scores - highest), 0.0)
        probs = expd / jnp.sum(expd, axis=-1, keepdims=True)
        value_grad = value_grad + lax.dot_general(
            probs.T.astype(jnp.bfloat16), cotan, nn, preferred_element_type=jnp.float32)
        prob_grad = lax.dot_general(cotan, values, nt, preferred_element_type=jnp.float32)
        centre = jnp.sum(probs * prob_grad, axis=-1, keepdims=True)
        score_grad = probs * (prob_grad - centre) * scale
        rotated = rotated + lax.dot_general(
            score_grad.T.astype(jnp.bfloat16), query, nn, preferred_element_type=jnp.float32)
    lane = lax.broadcasted_iota(jnp.int32, (seq_len, head_dim), 1)
    turned = pltpu.roll(rotated * sin_ref[...], head_dim // 2, 1)
    turned = jnp.where(lane < head_dim // 2, turned, -turned)
    head = pl.program_id(0)
    kv_cols = out_ref.shape[1] // 2
    key_at = pl.multiple_of(head * head_dim, head_dim)
    value_at = pl.multiple_of(kv_cols + head * head_dim, head_dim)
    out_ref[:, pl.ds(key_at, head_dim)] = (rotated * cos_ref[...] + turned).astype(jnp.bfloat16)
    out_ref[:, pl.ds(value_at, head_dim)] = value_grad.astype(jnp.bfloat16)

def attention_grads(length, queries, cotan, projected, cosine, sine, head_dim):
    seq_len, kv_cols = projected.shape[0], projected.shape[1] // 2
    kv_heads = kv_cols // head_dim
    group = queries.shape[1] // kv_cols
    kernel = functools.partial(attention_kernel, group=group, head_dim=head_dim)
    q_spec = pl.BlockSpec((seq_len, group * head_dim), lambda k, n: (0, k))
    key_spec = pl.BlockSpec((seq_len, head_dim), lambda k, n: (0, k))
    value_spec = pl.BlockSpec((seq_len, head_dim), lambda k, n: (0, k + kv_heads))
    rope_spec = pl.BlockSpec((seq_len, head_dim), lambda k, n: (0, 0))
    return pl.pallas_call(
        kernel,
        grid_spec=pltpu.PrefetchScalarGridSpec(
            num_scalar_prefetch=1, grid=(kv_heads,),
            in_specs=[q_spec, q_spec, key_spec, value_spec, rope_spec, rope_spec],
            out_specs=pl.BlockSpec((seq_len, 2 * kv_cols), lambda k, n: (0, 0))),
        out_shape=jax.ShapeDtypeStruct((seq_len, 2 * kv_cols), jnp.bfloat16),
    )(length, queries, cotan, projected, projected, cosine, sine)


def norm_backward(normed_grad, gain_f, nhat, inv_rms):
    gain_grad_in = normed_grad * gain_f
    centre = jnp.mean(gain_grad_in * nhat, axis=-1, keepdims=True)
    return ((gain_grad_in - nhat * centre) * inv_rms).astype(jnp.bfloat16)


def on_device(
    hidden_states,
    norm_gain,
    key_weight,
    value_weight,
    queries,
    context_cotangent,
    lengths,
    policy_logp,
    reference_logp,
):
    both_full = lax.all_gather(
        jnp.concatenate([key_weight[0], value_weight[0]], axis=1), "dp", axis=0, tiled=True
    )
    kv_cols = key_weight.shape[2]
    hidden = hidden_states[0]
    gain_f = norm_gain[0].astype(jnp.float32)
    tok_rows = hidden.shape[0]
    seq_count = lengths.shape[1]
    seq_len = tok_rows // seq_count
    kv_local = kv_cols // HD
    q_local = queries.shape[2] // HD
    hidden_f = hidden.astype(jnp.float32)
    inv_rms = lax.rsqrt(jnp.mean(hidden_f * hidden_f, axis=-1, keepdims=True) + norm_eps)
    nhat = hidden_f * inv_rms
    normed = (nhat * gain_f).astype(jnp.bfloat16)
    projected = jnp.dot(normed, both_full, preferred_element_type=jnp.float32)
    key_raw = projected[:, :kv_cols]
    values = projected[:, kv_cols:].astype(jnp.bfloat16)
    cosine, sine = rope_tables(seq_len, HD)
    key_four = key_raw.reshape(seq_count, seq_len, kv_local, HD)
    keys = (
        key_four * cosine[None, :, None, :] + rotate_half(key_four) * sine[None, :, None, :]
    ).astype(jnp.bfloat16)
    total_seqs = seq_count * lax.axis_size("dp")
    seq_weight = 2.0 * jax.nn.sigmoid(npo_beta * (policy_logp[0] - reference_logp[0])) / total_seqs
    live = jnp.arange(seq_len)[None, :] < lengths[0][:, None]
    factor = jnp.where(live, seq_weight[:, None], 0.0)
    scaled = (
        context_cotangent[0].reshape(seq_count, seq_len, q_local, HD).astype(jnp.float32)
        * factor[:, :, None, None]
    ).astype(jnp.bfloat16)

    key_parts = []
    for n in range(seq_count):
        rows_n = slice(n * seq_len, (n + 1) * seq_len)
        both_part = attention_grads(
            lengths[0][n:n + 1],
            queries[0][rows_n],
            scaled[n].reshape(seq_len, q_local * HD),
            projected[rows_n],
            cosine,
            sine,
            HD,
        )
        key_parts.append(both_part)
    combined = jnp.concatenate(key_parts, axis=0)

    def weight_grads(combined):
        return lax.psum_scatter(
            lax.dot_general(
                normed, combined, (((0,), (0,)), ((), ())), preferred_element_type=jnp.float32
            ).astype(jnp.bfloat16),
            "dp",
            scatter_dimension=0,
            tiled=True,
        )

    n_pipe = lax.axis_size("pipe")
    n_tensor = lax.axis_size("tensor")
    sizes = [tok_rows // 4, tok_rows * 5 // 16, tok_rows * 5 // 16, tok_rows // 8]
    bounds = [sum(sizes[:c]) for c in range(len(sizes) + 1)]
    chunks = len(sizes)
    exchange_steps = [
        [
            (p * n_tensor + t, p * n_tensor + (t + step) % n_tensor)
            for p in range(1, n_pipe)
            for t in range(n_tensor)
        ]
        for step in range(1, n_tensor)
    ]
    shift_pairs = [
        ((p + 1) * n_tensor + (t if (p + 1) // 2 == p // 2 else n_tensor - 1 - t), p * n_tensor + t)
        for p in range(n_pipe - 1)
        for t in range(n_tensor)
    ]
    lowers = []
    held = None
    for c in range(chunks):
        sl = slice(bounds[c], bounds[c + 1])
        part = lax.dot_general(
            combined[sl], both_full, (((1,), (1,)), ((), ())), preferred_element_type=jnp.float32
        )
        part_low = part.astype(jnp.bfloat16)
        if c == 0:
            part_low, combined = lax.optimization_barrier((part_low, combined))
            grad_total = weight_grads(combined)
        if held is not None:
            if len(lowers) > 0:
                part_low, held, lowers[-1] = lax.optimization_barrier(
                    (part_low, held, lowers[-1])
                )
            else:
                part_low, held = lax.optimization_barrier((part_low, held))
            lowers.append(lax.ppermute(held, ("pipe", "tensor"), shift_pairs))
        normed_grad = part_low.astype(jnp.float32)
        for pairs in exchange_steps:
            normed_grad = normed_grad + lax.ppermute(
                part_low, ("pipe", "tensor"), pairs
            ).astype(jnp.float32)
        held = norm_backward(normed_grad, gain_f, nhat[sl], inv_rms[sl])
    lowers.append(lax.ppermute(held, ("pipe", "tensor"), shift_pairs))
    lower = jnp.concatenate(lowers, axis=0)
    return (grad_total[:, :kv_cols][None], grad_total[:, kv_cols:][None], lower[None])


def solution(mesh):
    in_specs = (
        P("pipe", "dp", None),
        P("pipe", None),
        P("pipe", "dp", "tensor"),
        P("pipe", "dp", "tensor"),
        P("pipe", "dp", "tensor"),
        P("pipe", "dp", "tensor"),
        P("pipe", "dp"),
        P("pipe", "dp"),
        P("pipe", "dp"),
    )
    out_specs = (P("pipe", "dp", "tensor"), P("pipe", "dp", "tensor"), P("pipe", "dp", None))
    return jax.shard_map(
        on_device, mesh=mesh, in_specs=in_specs, out_specs=out_specs, check_vma=False
    )
```

```python
import functools
import math

import jax
import jax.numpy as jnp
from jax import lax
from jax.experimental import pallas as pl
from jax.experimental.pallas import tpu as pltpu
from jax.sharding import PartitionSpec as P

HD = 128


npo_beta = 0.1
norm_eps = 1e-05
rope_base = 500000.0


def shifted(value, axis, steps):
    count = lax.axis_size(axis)
    leading, last = (max(0, -steps), min(count, count - steps))
    return lax.ppermute(value, axis, [(source, source + steps) for source in range(leading, last)])


def rope_tables(length, head_dim):
    positions = jnp.arange(length).astype(jnp.float32)
    freq_index = jnp.arange(head_dim // 2).astype(jnp.float32)
    inverse = 1.0 / rope_base ** (2.0 * freq_index / head_dim)
    angles = positions[:, None] * inverse[None, :]
    cosine = jnp.concatenate([jnp.cos(angles), jnp.cos(angles)], axis=1)
    sine = jnp.concatenate([jnp.sin(angles), jnp.sin(angles)], axis=1)
    return (cosine, sine)


def rotate_half(values):
    half = values.shape[-1] // 2
    return jnp.concatenate([-values[..., half:], values[..., :half]], axis=-1)


def rotate_back(values):
    half = values.shape[-1] // 2
    return jnp.concatenate([values[..., half:], -values[..., :half]], axis=-1)


def sequence_grads(query_seq, key_seq, value_seq, cotan_seq, length_seq, cosine, sine):
    seq_len, kv_heads, head_dim = key_seq.shape
    group = query_seq.shape[1] // kv_heads
    scale = 1.0 / math.sqrt(head_dim)
    query_g = query_seq.reshape(seq_len, kv_heads, group, head_dim)
    cotan_g = cotan_seq.reshape(seq_len, kv_heads, group, head_dim)
    scores = (
        jnp.einsum("ikgd,jkd->kgij", query_g, key_seq, preferred_element_type=jnp.float32) * scale
    )
    row_pos = jnp.arange(seq_len)[:, None]
    col_pos = jnp.arange(seq_len)[None, :]
    allowed = (col_pos <= row_pos) & (col_pos < length_seq)
    scores = jnp.where(allowed, scores, -1e30)
    highest = jnp.max(scores, axis=-1, keepdims=True)
    expd = jnp.where(allowed, jnp.exp(scores - highest), 0.0)
    probs = expd / jnp.sum(expd, axis=-1, keepdims=True)
    probs_low = probs.astype(jnp.bfloat16)
    value_grad = jnp.einsum(
        "kgij,ikgd->jkd", probs_low, cotan_g, preferred_element_type=jnp.float32
    ).astype(jnp.bfloat16)
    prob_grad = jnp.einsum("ikgd,jkd->kgij", cotan_g, value_seq, preferred_element_type=jnp.float32)
    centre = jnp.sum(probs * prob_grad, axis=-1, keepdims=True)
    score_grad = (probs * (prob_grad - centre) * scale).astype(jnp.bfloat16)
    rotated_grad = jnp.einsum(
        "kgij,ikgd->jkd", score_grad, query_g, preferred_element_type=jnp.float32
    )
    key_grad = rotated_grad * cosine[:, None, :] + rotate_back(rotated_grad * sine[:, None, :])
    return (key_grad.astype(jnp.bfloat16), value_grad)


def attention_kernel(
    len_ref, q_ref, c_ref, k_ref, v_ref, cos_ref, sin_ref, out_ref, *, group, head_dim
):
    seq_len = k_ref.shape[0]
    scale = 1.0 / math.sqrt(head_dim)
    length = len_ref[0]
    lane = lax.broadcasted_iota(jnp.int32, (seq_len, head_dim), 1)
    key_raw = k_ref[...]
    half_turn = pltpu.roll(key_raw, head_dim // 2, 1)
    half_turn = jnp.where(lane < head_dim // 2, -half_turn, half_turn)
    keys = (key_raw * cos_ref[...] + half_turn * sin_ref[...]).astype(jnp.bfloat16)
    values = v_ref[...].astype(jnp.bfloat16)
    row = lax.broadcasted_iota(jnp.int32, (seq_len, seq_len), 0)
    col = lax.broadcasted_iota(jnp.int32, (seq_len, seq_len), 1)
    allowed = (col <= row) & (col < length)
    rotated = jnp.zeros((seq_len, head_dim), jnp.float32)
    value_grad = jnp.zeros((seq_len, head_dim), jnp.float32)
    nt = (((1,), (1,)), ((), ()))
    nn = (((1,), (0,)), ((), ()))
    for g in range(group):
        query = q_ref[:, g * head_dim:(g + 1) * head_dim]
        cotan = c_ref[:, g * head_dim:(g + 1) * head_dim]
        scores = lax.dot_general(query, keys, nt, preferred_element_type=jnp.float32) * scale
        scores = jnp.where(allowed, scores, -1e30)
        highest = jnp.max(scores, axis=-1, keepdims=True)
        expd = jnp.where(allowed, jnp.exp(scores - highest), 0.0)
        probs = expd / jnp.sum(expd, axis=-1, keepdims=True)
        value_grad = value_grad + lax.dot_general(
            probs.T.astype(jnp.bfloat16), cotan, nn, preferred_element_type=jnp.float32)
        prob_grad = lax.dot_general(cotan, values, nt, preferred_element_type=jnp.float32)
        centre = jnp.sum(probs * prob_grad, axis=-1, keepdims=True)
        score_grad = probs * (prob_grad - centre) * scale
        rotated = rotated + lax.dot_general(
            score_grad.T.astype(jnp.bfloat16), query, nn, preferred_element_type=jnp.float32)
    lane = lax.broadcasted_iota(jnp.int32, (seq_len, head_dim), 1)
    turned = pltpu.roll(rotated * sin_ref[...], head_dim // 2, 1)
    turned = jnp.where(lane < head_dim // 2, turned, -turned)
    head = pl.program_id(0)
    kv_cols = out_ref.shape[1] // 2
    key_at = pl.multiple_of(head * head_dim, head_dim)
    value_at = pl.multiple_of(kv_cols + head * head_dim, head_dim)
    out_ref[:, pl.ds(key_at, head_dim)] = (rotated * cos_ref[...] + turned).astype(jnp.bfloat16)
    out_ref[:, pl.ds(value_at, head_dim)] = value_grad.astype(jnp.bfloat16)

def attention_grads(length, queries, cotan, projected, cosine, sine, head_dim):
    seq_len, kv_cols = projected.shape[0], projected.shape[1] // 2
    kv_heads = kv_cols // head_dim
    group = queries.shape[1] // kv_cols
    kernel = functools.partial(attention_kernel, group=group, head_dim=head_dim)
    q_spec = pl.BlockSpec((seq_len, group * head_dim), lambda k, n: (0, k))
    key_spec = pl.BlockSpec((seq_len, head_dim), lambda k, n: (0, k))
    value_spec = pl.BlockSpec((seq_len, head_dim), lambda k, n: (0, k + kv_heads))
    rope_spec = pl.BlockSpec((seq_len, head_dim), lambda k, n: (0, 0))
    return pl.pallas_call(
        kernel,
        grid_spec=pltpu.PrefetchScalarGridSpec(
            num_scalar_prefetch=1, grid=(kv_heads,),
            in_specs=[q_spec, q_spec, key_spec, value_spec, rope_spec, rope_spec],
            out_specs=pl.BlockSpec((seq_len, 2 * kv_cols), lambda k, n: (0, 0))),
        out_shape=jax.ShapeDtypeStruct((seq_len, 2 * kv_cols), jnp.bfloat16),
    )(length, queries, cotan, projected, projected, cosine, sine)


def norm_backward(normed_grad, gain_f, nhat, inv_rms):
    gain_grad_in = normed_grad * gain_f
    centre = jnp.mean(gain_grad_in * nhat, axis=-1, keepdims=True)
    return ((gain_grad_in - nhat * centre) * inv_rms).astype(jnp.bfloat16)


def on_device(
    hidden_states,
    norm_gain,
    key_weight,
    value_weight,
    queries,
    context_cotangent,
    lengths,
    policy_logp,
    reference_logp,
):
    both_full = lax.all_gather(
        jnp.concatenate([key_weight[0], value_weight[0]], axis=1), "dp", axis=0, tiled=True
    )
    kv_cols = key_weight.shape[2]
    hidden = hidden_states[0]
    gain_f = norm_gain[0].astype(jnp.float32)
    tok_rows = hidden.shape[0]
    seq_count = lengths.shape[1]
    seq_len = tok_rows // seq_count
    kv_local = kv_cols // HD
    q_local = queries.shape[2] // HD
    hidden_f = hidden.astype(jnp.float32)
    inv_rms = lax.rsqrt(jnp.mean(hidden_f * hidden_f, axis=-1, keepdims=True) + norm_eps)
    nhat = hidden_f * inv_rms
    normed = (nhat * gain_f).astype(jnp.bfloat16)
    projected = jnp.dot(normed, both_full, preferred_element_type=jnp.float32)
    key_raw = projected[:, :kv_cols]
    values = projected[:, kv_cols:].astype(jnp.bfloat16)
    cosine, sine = rope_tables(seq_len, HD)
    key_four = key_raw.reshape(seq_count, seq_len, kv_local, HD)
    keys = (
        key_four * cosine[None, :, None, :] + rotate_half(key_four) * sine[None, :, None, :]
    ).astype(jnp.bfloat16)
    total_seqs = seq_count * lax.axis_size("dp")
    seq_weight = 2.0 * jax.nn.sigmoid(npo_beta * (policy_logp[0] - reference_logp[0])) / total_seqs
    live = jnp.arange(seq_len)[None, :] < lengths[0][:, None]
    factor = jnp.where(live, seq_weight[:, None], 0.0)
    scaled = (
        context_cotangent[0].reshape(seq_count, seq_len, q_local, HD).astype(jnp.float32)
        * factor[:, :, None, None]
    ).astype(jnp.bfloat16)

    key_parts = []
    for n in range(seq_count):
        rows_n = slice(n * seq_len, (n + 1) * seq_len)
        both_part = attention_grads(
            lengths[0][n:n + 1],
            queries[0][rows_n],
            scaled[n].reshape(seq_len, q_local * HD),
            projected[rows_n],
            cosine,
            sine,
            HD,
        )
        key_parts.append(both_part)
    combined = jnp.concatenate(key_parts, axis=0)

    def weight_grads(combined):
        return lax.psum_scatter(
            lax.dot_general(
                normed, combined, (((0,), (0,)), ((), ())), preferred_element_type=jnp.float32
            ).astype(jnp.bfloat16),
            "dp",
            scatter_dimension=0,
            tiled=True,
        )

    n_pipe = lax.axis_size("pipe")
    n_tensor = lax.axis_size("tensor")
    sizes = [tok_rows * 3 // 16, tok_rows * 3 // 8, tok_rows * 5 // 16, tok_rows // 8]
    bounds = [sum(sizes[:c]) for c in range(len(sizes) + 1)]
    chunks = len(sizes)
    exchange_steps = [
        [
            (p * n_tensor + t, p * n_tensor + (t + step) % n_tensor)
            for p in range(1, n_pipe)
            for t in range(n_tensor)
        ]
        for step in range(1, n_tensor)
    ]
    shift_pairs = [
        ((p + 1) * n_tensor + (t if (p + 1) // 2 == p // 2 else n_tensor - 1 - t), p * n_tensor + t)
        for p in range(n_pipe - 1)
        for t in range(n_tensor)
    ]
    lowers = []
    held = None
    for c in range(chunks):
        sl = slice(bounds[c], bounds[c + 1])
        part = lax.dot_general(
            combined[sl], both_full, (((1,), (1,)), ((), ())), preferred_element_type=jnp.float32
        )
        part_low = part.astype(jnp.bfloat16)
        if c == 0:
            part_low, combined = lax.optimization_barrier((part_low, combined))
            grad_total = weight_grads(combined)
        if held is not None:
            if len(lowers) > 0:
                part_low, held, lowers[-1] = lax.optimization_barrier(
                    (part_low, held, lowers[-1])
                )
            else:
                part_low, held = lax.optimization_barrier((part_low, held))
            lowers.append(lax.ppermute(held, ("pipe", "tensor"), shift_pairs))
        normed_grad = part_low.astype(jnp.float32)
        for pairs in exchange_steps:
            normed_grad = normed_grad + lax.ppermute(
                part_low, ("pipe", "tensor"), pairs
            ).astype(jnp.float32)
        held = norm_backward(normed_grad, gain_f, nhat[sl], inv_rms[sl])
    lowers.append(lax.ppermute(held, ("pipe", "tensor"), shift_pairs))
    lower = jnp.concatenate(lowers, axis=0)
    return (grad_total[:, :kv_cols][None], grad_total[:, kv_cols:][None], lower[None])


def solution(mesh):
    in_specs = (
        P("pipe", "dp", None),
        P("pipe", None),
        P("pipe", "dp", "tensor"),
        P("pipe", "dp", "tensor"),
        P("pipe", "dp", "tensor"),
        P("pipe", "dp", "tensor"),
        P("pipe", "dp"),
        P("pipe", "dp"),
        P("pipe", "dp"),
    )
    out_specs = (P("pipe", "dp", "tensor"), P("pipe", "dp", "tensor"), P("pipe", "dp", None))
    return jax.shard_map(
        on_device, mesh=mesh, in_specs=in_specs, out_specs=out_specs, check_vma=False
    )
```

```python
import functools
import math

import jax
import jax.numpy as jnp
from jax import lax
from jax.experimental import pallas as pl
from jax.experimental.pallas import tpu as pltpu
from jax.sharding import PartitionSpec as P

HD = 128


npo_beta = 0.1
norm_eps = 1e-05
rope_base = 500000.0


def shifted(value, axis, steps):
    count = lax.axis_size(axis)
    leading, last = (max(0, -steps), min(count, count - steps))
    return lax.ppermute(value, axis, [(source, source + steps) for source in range(leading, last)])


def rope_tables(length, head_dim):
    positions = jnp.arange(length).astype(jnp.float32)
    freq_index = jnp.arange(head_dim // 2).astype(jnp.float32)
    inverse = 1.0 / rope_base ** (2.0 * freq_index / head_dim)
    angles = positions[:, None] * inverse[None, :]
    cosine = jnp.concatenate([jnp.cos(angles), jnp.cos(angles)], axis=1)
    sine = jnp.concatenate([jnp.sin(angles), jnp.sin(angles)], axis=1)
    return (cosine, sine)


def rotate_half(values):
    half = values.shape[-1] // 2
    return jnp.concatenate([-values[..., half:], values[..., :half]], axis=-1)


def rotate_back(values):
    half = values.shape[-1] // 2
    return jnp.concatenate([values[..., half:], -values[..., :half]], axis=-1)


def sequence_grads(query_seq, key_seq, value_seq, cotan_seq, length_seq, cosine, sine):
    seq_len, kv_heads, head_dim = key_seq.shape
    group = query_seq.shape[1] // kv_heads
    scale = 1.0 / math.sqrt(head_dim)
    query_g = query_seq.reshape(seq_len, kv_heads, group, head_dim)
    cotan_g = cotan_seq.reshape(seq_len, kv_heads, group, head_dim)
    scores = (
        jnp.einsum("ikgd,jkd->kgij", query_g, key_seq, preferred_element_type=jnp.float32) * scale
    )
    row_pos = jnp.arange(seq_len)[:, None]
    col_pos = jnp.arange(seq_len)[None, :]
    allowed = (col_pos <= row_pos) & (col_pos < length_seq)
    scores = jnp.where(allowed, scores, -1e30)
    highest = jnp.max(scores, axis=-1, keepdims=True)
    expd = jnp.where(allowed, jnp.exp(scores - highest), 0.0)
    probs = expd / jnp.sum(expd, axis=-1, keepdims=True)
    probs_low = probs.astype(jnp.bfloat16)
    value_grad = jnp.einsum(
        "kgij,ikgd->jkd", probs_low, cotan_g, preferred_element_type=jnp.float32
    ).astype(jnp.bfloat16)
    prob_grad = jnp.einsum("ikgd,jkd->kgij", cotan_g, value_seq, preferred_element_type=jnp.float32)
    centre = jnp.sum(probs * prob_grad, axis=-1, keepdims=True)
    score_grad = (probs * (prob_grad - centre) * scale).astype(jnp.bfloat16)
    rotated_grad = jnp.einsum(
        "kgij,ikgd->jkd", score_grad, query_g, preferred_element_type=jnp.float32
    )
    key_grad = rotated_grad * cosine[:, None, :] + rotate_back(rotated_grad * sine[:, None, :])
    return (key_grad.astype(jnp.bfloat16), value_grad)


def attention_kernel(
    len_ref, q_ref, c_ref, k_ref, v_ref, cos_ref, sin_ref, out_ref, *, group, head_dim
):
    seq_len = k_ref.shape[0]
    scale = 1.0 / math.sqrt(head_dim)
    length = len_ref[0]
    lane = lax.broadcasted_iota(jnp.int32, (seq_len, head_dim), 1)
    key_raw = k_ref[...]
    half_turn = pltpu.roll(key_raw, head_dim // 2, 1)
    half_turn = jnp.where(lane < head_dim // 2, -half_turn, half_turn)
    keys = (key_raw * cos_ref[...] + half_turn * sin_ref[...]).astype(jnp.bfloat16)
    values = v_ref[...].astype(jnp.bfloat16)
    row = lax.broadcasted_iota(jnp.int32, (seq_len, seq_len), 0)
    col = lax.broadcasted_iota(jnp.int32, (seq_len, seq_len), 1)
    allowed = (col <= row) & (col < length)
    rotated = jnp.zeros((seq_len, head_dim), jnp.float32)
    value_grad = jnp.zeros((seq_len, head_dim), jnp.float32)
    nt = (((1,), (1,)), ((), ()))
    nn = (((1,), (0,)), ((), ()))
    for g in range(group):
        query = q_ref[:, g * head_dim:(g + 1) * head_dim]
        cotan = c_ref[:, g * head_dim:(g + 1) * head_dim]
        scores = lax.dot_general(query, keys, nt, preferred_element_type=jnp.float32) * scale
        scores = jnp.where(allowed, scores, -1e30)
        highest = jnp.max(scores, axis=-1, keepdims=True)
        expd = jnp.where(allowed, jnp.exp(scores - highest), 0.0)
        probs = expd / jnp.sum(expd, axis=-1, keepdims=True)
        value_grad = value_grad + lax.dot_general(
            probs.T.astype(jnp.bfloat16), cotan, nn, preferred_element_type=jnp.float32)
        prob_grad = lax.dot_general(cotan, values, nt, preferred_element_type=jnp.float32)
        centre = jnp.sum(probs * prob_grad, axis=-1, keepdims=True)
        score_grad = probs * (prob_grad - centre) * scale
        rotated = rotated + lax.dot_general(
            score_grad.T.astype(jnp.bfloat16), query, nn, preferred_element_type=jnp.float32)
    lane = lax.broadcasted_iota(jnp.int32, (seq_len, head_dim), 1)
    turned = pltpu.roll(rotated * sin_ref[...], head_dim // 2, 1)
    turned = jnp.where(lane < head_dim // 2, turned, -turned)
    head = pl.program_id(0)
    kv_cols = out_ref.shape[1] // 2
    key_at = pl.multiple_of(head * head_dim, head_dim)
    value_at = pl.multiple_of(kv_cols + head * head_dim, head_dim)
    out_ref[:, pl.ds(key_at, head_dim)] = (rotated * cos_ref[...] + turned).astype(jnp.bfloat16)
    out_ref[:, pl.ds(value_at, head_dim)] = value_grad.astype(jnp.bfloat16)

def attention_grads(length, queries, cotan, projected, cosine, sine, head_dim):
    seq_len, kv_cols = projected.shape[0], projected.shape[1] // 2
    kv_heads = kv_cols // head_dim
    group = queries.shape[1] // kv_cols
    kernel = functools.partial(attention_kernel, group=group, head_dim=head_dim)
    q_spec = pl.BlockSpec((seq_len, group * head_dim), lambda k, n: (0, k))
    key_spec = pl.BlockSpec((seq_len, head_dim), lambda k, n: (0, k))
    value_spec = pl.BlockSpec((seq_len, head_dim), lambda k, n: (0, k + kv_heads))
    rope_spec = pl.BlockSpec((seq_len, head_dim), lambda k, n: (0, 0))
    return pl.pallas_call(
        kernel,
        grid_spec=pltpu.PrefetchScalarGridSpec(
            num_scalar_prefetch=1, grid=(kv_heads,),
            in_specs=[q_spec, q_spec, key_spec, value_spec, rope_spec, rope_spec],
            out_specs=pl.BlockSpec((seq_len, 2 * kv_cols), lambda k, n: (0, 0))),
        out_shape=jax.ShapeDtypeStruct((seq_len, 2 * kv_cols), jnp.bfloat16),
    )(length, queries, cotan, projected, projected, cosine, sine)


def norm_backward(normed_grad, gain_f, nhat, inv_rms):
    gain_grad_in = normed_grad * gain_f
    centre = jnp.mean(gain_grad_in * nhat, axis=-1, keepdims=True)
    return ((gain_grad_in - nhat * centre) * inv_rms).astype(jnp.bfloat16)


def on_device(
    hidden_states,
    norm_gain,
    key_weight,
    value_weight,
    queries,
    context_cotangent,
    lengths,
    policy_logp,
    reference_logp,
):
    both_full = lax.all_gather(
        jnp.concatenate([key_weight[0], value_weight[0]], axis=1), "dp", axis=0, tiled=True
    )
    kv_cols = key_weight.shape[2]
    hidden = hidden_states[0]
    gain_f = norm_gain[0].astype(jnp.float32)
    tok_rows = hidden.shape[0]
    seq_count = lengths.shape[1]
    seq_len = tok_rows // seq_count
    kv_local = kv_cols // HD
    q_local = queries.shape[2] // HD
    hidden_f = hidden.astype(jnp.float32)
    inv_rms = lax.rsqrt(jnp.mean(hidden_f * hidden_f, axis=-1, keepdims=True) + norm_eps)
    nhat = hidden_f * inv_rms
    normed = (nhat * gain_f).astype(jnp.bfloat16)
    projected = jnp.dot(normed, both_full, preferred_element_type=jnp.float32)
    key_raw = projected[:, :kv_cols]
    values = projected[:, kv_cols:].astype(jnp.bfloat16)
    cosine, sine = rope_tables(seq_len, HD)
    key_four = key_raw.reshape(seq_count, seq_len, kv_local, HD)
    keys = (
        key_four * cosine[None, :, None, :] + rotate_half(key_four) * sine[None, :, None, :]
    ).astype(jnp.bfloat16)
    total_seqs = seq_count * lax.axis_size("dp")
    seq_weight = 2.0 * jax.nn.sigmoid(npo_beta * (policy_logp[0] - reference_logp[0])) / total_seqs
    live = jnp.arange(seq_len)[None, :] < lengths[0][:, None]
    factor = jnp.where(live, seq_weight[:, None], 0.0)
    scaled = (
        context_cotangent[0].reshape(seq_count, seq_len, q_local, HD).astype(jnp.float32)
        * factor[:, :, None, None]
    ).astype(jnp.bfloat16)

    key_parts = []
    for n in range(seq_count):
        rows_n = slice(n * seq_len, (n + 1) * seq_len)
        both_part = attention_grads(
            lengths[0][n:n + 1],
            queries[0][rows_n],
            scaled[n].reshape(seq_len, q_local * HD),
            projected[rows_n],
            cosine,
            sine,
            HD,
        )
        key_parts.append(both_part)
    combined = jnp.concatenate(key_parts, axis=0)

    def weight_grads(combined):
        return lax.psum_scatter(
            lax.dot_general(
                normed, combined, (((0,), (0,)), ((), ())), preferred_element_type=jnp.float32
            ).astype(jnp.bfloat16),
            "dp",
            scatter_dimension=0,
            tiled=True,
        )

    n_pipe = lax.axis_size("pipe")
    n_tensor = lax.axis_size("tensor")
    sizes = [tok_rows // 4, tok_rows * 5 // 16, tok_rows * 5 // 16, tok_rows // 8]
    bounds = [sum(sizes[:c]) for c in range(len(sizes) + 1)]
    chunks = len(sizes)
    exchange_steps = [
        [
            (p * n_tensor + t, p * n_tensor + (t + step) % n_tensor)
            for p in range(1, n_pipe)
            for t in range(n_tensor)
        ]
        for step in range(1, n_tensor)
    ]
    shift_pairs = [
        ((p + 1) * n_tensor + (t if (p + 1) // 2 == p // 2 else n_tensor - 1 - t), p * n_tensor + t)
        for p in range(n_pipe - 1)
        for t in range(n_tensor)
    ]
    lowers = []
    pending = None
    for c in range(chunks):
        sl = slice(bounds[c], bounds[c + 1])
        part = lax.dot_general(
            combined[sl], both_full, (((1,), (1,)), ((), ())), preferred_element_type=jnp.float32
        )
        part_low = part.astype(jnp.bfloat16)
        if c == 0:
            part_low, combined = lax.optimization_barrier((part_low, combined))
            grad_total = weight_grads(combined)
        if pending is not None:
            prev_low, prev_recv, prev_sl = pending
            if len(lowers) > 0:
                part_low, prev_recv, lowers[-1] = lax.optimization_barrier(
                    (part_low, prev_recv, lowers[-1])
                )
            else:
                part_low, prev_recv = lax.optimization_barrier((part_low, prev_recv))
        received = [lax.ppermute(part_low, ("pipe", "tensor"), pairs) for pairs in exchange_steps]
        if pending is not None:
            held = norm_backward(
                sum([prev_low.astype(jnp.float32)] + [r.astype(jnp.float32) for r in prev_recv]),
                gain_f, nhat[prev_sl], inv_rms[prev_sl],
            )
            lowers.append(lax.ppermute(held, ("pipe", "tensor"), shift_pairs))
        pending = (part_low, received, sl)
    prev_low, prev_recv, prev_sl = pending
    held = norm_backward(
        sum([prev_low.astype(jnp.float32)] + [r.astype(jnp.float32) for r in prev_recv]),
        gain_f, nhat[prev_sl], inv_rms[prev_sl],
    )
    lowers.append(lax.ppermute(held, ("pipe", "tensor"), shift_pairs))
    lower = jnp.concatenate(lowers, axis=0)
    return (grad_total[:, :kv_cols][None], grad_total[:, kv_cols:][None], lower[None])


def solution(mesh):
    in_specs = (
        P("pipe", "dp", None),
        P("pipe", None),
        P("pipe", "dp", "tensor"),
        P("pipe", "dp", "tensor"),
        P("pipe", "dp", "tensor"),
        P("pipe", "dp", "tensor"),
        P("pipe", "dp"),
        P("pipe", "dp"),
        P("pipe", "dp"),
    )
    out_specs = (P("pipe", "dp", "tensor"), P("pipe", "dp", "tensor"), P("pipe", "dp", None))
    return jax.shard_map(
        on_device, mesh=mesh, in_specs=in_specs, out_specs=out_specs, check_vma=False
    )
```

```python
import functools
import math

import jax
import jax.numpy as jnp
from jax import lax
from jax.experimental import pallas as pl
from jax.experimental.pallas import tpu as pltpu
from jax.sharding import PartitionSpec as P

HD = 128


npo_beta = 0.1
norm_eps = 1e-05
rope_base = 500000.0


def shifted(value, axis, steps):
    count = lax.axis_size(axis)
    leading, last = (max(0, -steps), min(count, count - steps))
    return lax.ppermute(value, axis, [(source, source + steps) for source in range(leading, last)])


def rope_tables(length, head_dim):
    positions = jnp.arange(length).astype(jnp.float32)
    freq_index = jnp.arange(head_dim // 2).astype(jnp.float32)
    inverse = 1.0 / rope_base ** (2.0 * freq_index / head_dim)
    angles = positions[:, None] * inverse[None, :]
    cosine = jnp.concatenate([jnp.cos(angles), jnp.cos(angles)], axis=1)
    sine = jnp.concatenate([jnp.sin(angles), jnp.sin(angles)], axis=1)
    return (cosine, sine)


def rotate_half(values):
    half = values.shape[-1] // 2
    return jnp.concatenate([-values[..., half:], values[..., :half]], axis=-1)


def rotate_back(values):
    half = values.shape[-1] // 2
    return jnp.concatenate([values[..., half:], -values[..., :half]], axis=-1)


def sequence_grads(query_seq, key_seq, value_seq, cotan_seq, length_seq, cosine, sine):
    seq_len, kv_heads, head_dim = key_seq.shape
    group = query_seq.shape[1] // kv_heads
    scale = 1.0 / math.sqrt(head_dim)
    query_g = query_seq.reshape(seq_len, kv_heads, group, head_dim)
    cotan_g = cotan_seq.reshape(seq_len, kv_heads, group, head_dim)
    scores = (
        jnp.einsum("ikgd,jkd->kgij", query_g, key_seq, preferred_element_type=jnp.float32) * scale
    )
    row_pos = jnp.arange(seq_len)[:, None]
    col_pos = jnp.arange(seq_len)[None, :]
    allowed = (col_pos <= row_pos) & (col_pos < length_seq)
    scores = jnp.where(allowed, scores, -1e30)
    highest = jnp.max(scores, axis=-1, keepdims=True)
    expd = jnp.where(allowed, jnp.exp(scores - highest), 0.0)
    probs = expd / jnp.sum(expd, axis=-1, keepdims=True)
    probs_low = probs.astype(jnp.bfloat16)
    value_grad = jnp.einsum(
        "kgij,ikgd->jkd", probs_low, cotan_g, preferred_element_type=jnp.float32
    ).astype(jnp.bfloat16)
    prob_grad = jnp.einsum("ikgd,jkd->kgij", cotan_g, value_seq, preferred_element_type=jnp.float32)
    centre = jnp.sum(probs * prob_grad, axis=-1, keepdims=True)
    score_grad = (probs * (prob_grad - centre) * scale).astype(jnp.bfloat16)
    rotated_grad = jnp.einsum(
        "kgij,ikgd->jkd", score_grad, query_g, preferred_element_type=jnp.float32
    )
    key_grad = rotated_grad * cosine[:, None, :] + rotate_back(rotated_grad * sine[:, None, :])
    return (key_grad.astype(jnp.bfloat16), value_grad)


def attention_kernel(
    len_ref, q_ref, c_ref, k_ref, v_ref, cos_ref, sin_ref, out_ref, *, group, head_dim
):
    seq_len = k_ref.shape[0]
    scale = 1.0 / math.sqrt(head_dim)
    length = len_ref[0]
    lane = lax.broadcasted_iota(jnp.int32, (seq_len, head_dim), 1)
    key_raw = k_ref[...]
    half_turn = pltpu.roll(key_raw, head_dim // 2, 1)
    half_turn = jnp.where(lane < head_dim // 2, -half_turn, half_turn)
    keys = (key_raw * cos_ref[...] + half_turn * sin_ref[...]).astype(jnp.bfloat16)
    values = v_ref[...].astype(jnp.bfloat16)
    row = lax.broadcasted_iota(jnp.int32, (seq_len, seq_len), 0)
    col = lax.broadcasted_iota(jnp.int32, (seq_len, seq_len), 1)
    allowed = (col <= row) & (col < length)
    rotated = jnp.zeros((seq_len, head_dim), jnp.float32)
    value_grad = jnp.zeros((seq_len, head_dim), jnp.float32)
    nt = (((1,), (1,)), ((), ()))
    nn = (((1,), (0,)), ((), ()))
    for g in range(group):
        query = q_ref[:, g * head_dim:(g + 1) * head_dim]
        cotan = c_ref[:, g * head_dim:(g + 1) * head_dim]
        scores = lax.dot_general(query, keys, nt, preferred_element_type=jnp.float32) * scale
        scores = jnp.where(allowed, scores, -1e30)
        highest = jnp.max(scores, axis=-1, keepdims=True)
        expd = jnp.where(allowed, jnp.exp(scores - highest), 0.0)
        probs = expd / jnp.sum(expd, axis=-1, keepdims=True)
        value_grad = value_grad + lax.dot_general(
            probs.T.astype(jnp.bfloat16), cotan, nn, preferred_element_type=jnp.float32)
        prob_grad = lax.dot_general(cotan, values, nt, preferred_element_type=jnp.float32)
        centre = jnp.sum(probs * prob_grad, axis=-1, keepdims=True)
        score_grad = probs * (prob_grad - centre) * scale
        rotated = rotated + lax.dot_general(
            score_grad.T.astype(jnp.bfloat16), query, nn, preferred_element_type=jnp.float32)
    lane = lax.broadcasted_iota(jnp.int32, (seq_len, head_dim), 1)
    turned = pltpu.roll(rotated * sin_ref[...], head_dim // 2, 1)
    turned = jnp.where(lane < head_dim // 2, turned, -turned)
    head = pl.program_id(0)
    kv_cols = out_ref.shape[1] // 2
    key_at = pl.multiple_of(head * head_dim, head_dim)
    value_at = pl.multiple_of(kv_cols + head * head_dim, head_dim)
    out_ref[:, pl.ds(key_at, head_dim)] = (rotated * cos_ref[...] + turned).astype(jnp.bfloat16)
    out_ref[:, pl.ds(value_at, head_dim)] = value_grad.astype(jnp.bfloat16)

def attention_grads(length, queries, cotan, projected, cosine, sine, head_dim):
    seq_len, kv_cols = projected.shape[0], projected.shape[1] // 2
    kv_heads = kv_cols // head_dim
    group = queries.shape[1] // kv_cols
    kernel = functools.partial(attention_kernel, group=group, head_dim=head_dim)
    q_spec = pl.BlockSpec((seq_len, group * head_dim), lambda k, n: (0, k))
    key_spec = pl.BlockSpec((seq_len, head_dim), lambda k, n: (0, k))
    value_spec = pl.BlockSpec((seq_len, head_dim), lambda k, n: (0, k + kv_heads))
    rope_spec = pl.BlockSpec((seq_len, head_dim), lambda k, n: (0, 0))
    return pl.pallas_call(
        kernel,
        grid_spec=pltpu.PrefetchScalarGridSpec(
            num_scalar_prefetch=1, grid=(kv_heads,),
            in_specs=[q_spec, q_spec, key_spec, value_spec, rope_spec, rope_spec],
            out_specs=pl.BlockSpec((seq_len, 2 * kv_cols), lambda k, n: (0, 0))),
        out_shape=jax.ShapeDtypeStruct((seq_len, 2 * kv_cols), jnp.bfloat16),
    )(length, queries, cotan, projected, projected, cosine, sine)


def norm_backward(normed_grad, gain_f, nhat, inv_rms):
    gain_grad_in = normed_grad * gain_f
    centre = jnp.mean(gain_grad_in * nhat, axis=-1, keepdims=True)
    return ((gain_grad_in - nhat * centre) * inv_rms).astype(jnp.bfloat16)


def on_device(
    hidden_states,
    norm_gain,
    key_weight,
    value_weight,
    queries,
    context_cotangent,
    lengths,
    policy_logp,
    reference_logp,
):
    both_full = lax.all_gather(
        jnp.concatenate([key_weight[0], value_weight[0]], axis=1), "dp", axis=0, tiled=True
    )
    kv_cols = key_weight.shape[2]
    hidden = hidden_states[0]
    gain_f = norm_gain[0].astype(jnp.float32)
    tok_rows = hidden.shape[0]
    seq_count = lengths.shape[1]
    seq_len = tok_rows // seq_count
    kv_local = kv_cols // HD
    q_local = queries.shape[2] // HD
    hidden_f = hidden.astype(jnp.float32)
    inv_rms = lax.rsqrt(jnp.mean(hidden_f * hidden_f, axis=-1, keepdims=True) + norm_eps)
    nhat = hidden_f * inv_rms
    normed = (nhat * gain_f).astype(jnp.bfloat16)
    projected = jnp.dot(normed, both_full, preferred_element_type=jnp.float32)
    key_raw = projected[:, :kv_cols]
    values = projected[:, kv_cols:].astype(jnp.bfloat16)
    cosine, sine = rope_tables(seq_len, HD)
    key_four = key_raw.reshape(seq_count, seq_len, kv_local, HD)
    keys = (
        key_four * cosine[None, :, None, :] + rotate_half(key_four) * sine[None, :, None, :]
    ).astype(jnp.bfloat16)
    total_seqs = seq_count * lax.axis_size("dp")
    seq_weight = 2.0 * jax.nn.sigmoid(npo_beta * (policy_logp[0] - reference_logp[0])) / total_seqs
    live = jnp.arange(seq_len)[None, :] < lengths[0][:, None]
    factor = jnp.where(live, seq_weight[:, None], 0.0)
    scaled = (
        context_cotangent[0].reshape(seq_count, seq_len, q_local, HD).astype(jnp.float32)
        * factor[:, :, None, None]
    ).astype(jnp.bfloat16)

    key_parts = []
    for n in range(seq_count):
        rows_n = slice(n * seq_len, (n + 1) * seq_len)
        both_part = attention_grads(
            lengths[0][n:n + 1],
            queries[0][rows_n],
            scaled[n].reshape(seq_len, q_local * HD),
            projected[rows_n],
            cosine,
            sine,
            HD,
        )
        key_parts.append(both_part)
    combined = jnp.concatenate(key_parts, axis=0)

    def weight_grads(combined):
        return lax.psum_scatter(
            lax.dot_general(
                normed, combined, (((0,), (0,)), ((), ())), preferred_element_type=jnp.float32
            ).astype(jnp.bfloat16),
            "dp",
            scatter_dimension=0,
            tiled=True,
        )

    n_pipe = lax.axis_size("pipe")
    n_tensor = lax.axis_size("tensor")
    sizes = [tok_rows // 4, tok_rows * 3 // 8, tok_rows // 4, tok_rows // 8]
    bounds = [sum(sizes[:c]) for c in range(len(sizes) + 1)]
    chunks = len(sizes)
    exchange_steps = [
        [
            (p * n_tensor + t, p * n_tensor + (t + step) % n_tensor)
            for p in range(1, n_pipe)
            for t in range(n_tensor)
        ]
        for step in range(1, n_tensor)
    ]
    shift_pairs = [
        ((p + 1) * n_tensor + (t if (p + 1) // 2 == p // 2 else n_tensor - 1 - t), p * n_tensor + t)
        for p in range(n_pipe - 1)
        for t in range(n_tensor)
    ]
    lowers = []
    held = None
    for c in range(chunks):
        sl = slice(bounds[c], bounds[c + 1])
        part = lax.dot_general(
            combined[sl], both_full, (((1,), (1,)), ((), ())), preferred_element_type=jnp.float32
        )
        part_low = part.astype(jnp.bfloat16)
        if c == 0:
            part_low, combined = lax.optimization_barrier((part_low, combined))
            grad_total = weight_grads(combined)
        if held is not None:
            if len(lowers) > 0:
                part_low, held, lowers[-1] = lax.optimization_barrier(
                    (part_low, held, lowers[-1])
                )
            else:
                part_low, held = lax.optimization_barrier((part_low, held))
            lowers.append(lax.ppermute(held, ("pipe", "tensor"), shift_pairs))
        normed_grad = part_low.astype(jnp.float32)
        for pairs in exchange_steps:
            normed_grad = normed_grad + lax.ppermute(
                part_low, ("pipe", "tensor"), pairs
            ).astype(jnp.float32)
        held = norm_backward(normed_grad, gain_f, nhat[sl], inv_rms[sl])
    lowers.append(lax.ppermute(held, ("pipe", "tensor"), shift_pairs))
    lower = jnp.concatenate(lowers, axis=0)
    return (grad_total[:, :kv_cols][None], grad_total[:, kv_cols:][None], lower[None])


def solution(mesh):
    in_specs = (
        P("pipe", "dp", None),
        P("pipe", None),
        P("pipe", "dp", "tensor"),
        P("pipe", "dp", "tensor"),
        P("pipe", "dp", "tensor"),
        P("pipe", "dp", "tensor"),
        P("pipe", "dp"),
        P("pipe", "dp"),
        P("pipe", "dp"),
    )
    out_specs = (P("pipe", "dp", "tensor"), P("pipe", "dp", "tensor"), P("pipe", "dp", None))
    return jax.shard_map(
        on_device, mesh=mesh, in_specs=in_specs, out_specs=out_specs, check_vma=False
    )
```
